128 devices in a mesh: seq: 32 (over z, x, y_lo), tp: 4 (over y_hi, core).
Axes of the slice: x: 4, y: 4 (y_hi: 2, y_lo: 2; y = y_hi * 2 + y_lo), z: 4, core: 2. Of those that a mesh axis runs over, the one named last changes fastest.
Arguments:
- query_gate: bfloat16 [256, 131072], P('tp', 'seq'), may hold values from -6 to 6
- key_gate: bfloat16 [256, 131072], P('tp', 'seq'), may hold values from -6 to 6
- value_input: bfloat16 [256, 131072], P('tp', 'seq'), may hold values from -6 to 6
- long_filter: float32 [256, 131072], P('tp', 'seq'), may hold values from -2 to 2, as said below
- out_weight: bfloat16 [256, 256], replicated, may hold values from -0.375 to 0.375
Outputs:
- mixed: bfloat16 [256, 131072], P('tp', 'seq')
The draws below stay inside these ranges and needn't reach their ends.
Inputs may be any that keep to these rules, and one draw needn't show every extreme that they name: `long_filter`: each channel's taps follow a decaying envelope.
All inputs are finite; a program needn't handle non-finite values.
Results may differ from the reference program's by a relative error of at most 0.018.
Values may be sent and summed in bfloat16 or wider, within the bound.
No kernel may reach another device: no remote copies, remote signals or barrier semaphores. Data moves between devices by JAX's collectives and lax.ppermute only.
A program may use at most 64 MiB of HBM per device.

```python
import math
import jax
import jax.numpy as jnp
from jax import lax

CH = 256
SEQ = 131072


def geometric_total(rate):
    return jnp.expm1(-SEQ * rate) / jnp.expm1(-rate)


def draw_long_filter(key, part):
    key_noise = jax.random.fold_in(key, 11)
    key_rate = jax.random.fold_in(key, 12)
    key_slow = jax.random.fold_in(key, 13)
    key_share = jax.random.fold_in(key, 14)
    positions = jnp.arange(SEQ, dtype=jnp.float32)[None, :]
    log_fast = jax.random.uniform(key_rate, (CH, 1), jnp.float32, math.log(30.0), math.log(1000.0 * SEQ))
    noise = jnp.clip(jax.random.normal(key_noise, (CH, SEQ), jnp.float32), -6.0, 6.0)
    log_slow = jax.random.uniform(key_slow, (CH, 1), jnp.float32, math.log(SEQ / 2.0), math.log(1000.0 * SEQ))
    share = jax.random.uniform(key_share, (CH, 1), jnp.float32, 0.25, 0.5)
    rate_fast = jnp.exp(-log_fast)
    rate_slow = jnp.exp(-log_slow)
    energy_fast = geometric_total(2.0 * rate_fast)
    energy_slow = geometric_total(2.0 * rate_slow)
    amplitude = jnp.sqrt(share / (1.0 - share) * energy_fast / energy_slow)
    envelope = jnp.exp(-positions * rate_fast) + amplitude * jnp.exp(-positions * rate_slow)
    energy = energy_fast + amplitude * amplitude * energy_slow + 2.0 * amplitude * geometric_total(rate_fast + rate_slow)
    return (noise * envelope / jnp.sqrt(energy)).astype(jnp.float32)


def level_of(key, shape, cuts, smallest, high):
    loudness, own = 1.0, jax.random.fold_in(key, 6)
    for dim, shards_of in cuts:
        steps = jnp.exp(jax.random.uniform(jax.random.fold_in(own, dim), (shards_of,), jnp.float32, smallest / len(cuts), high / len(cuts)))
        loudness = loudness * jnp.repeat(steps, shape[dim] // shards_of).reshape([-1 if axis == dim else 1 for axis in range(len(shape))])
    return loudness


def centred(stream_key, shape, deviation, most, cuts=(), held_as=jnp.bfloat16):
    entries = jax.random.normal(stream_key, shape, jnp.float32) * deviation
    if len(cuts) > 0:
        entries = level_of(stream_key, shape, cuts, -0.22, 0.18) * entries
    return jnp.clip(entries, min=-most, max=most).astype(held_as)


def setup_inputs(seed: int = 0) -> dict:
    seeds = jax.random.split(jax.random.key(seed), 6)
    query_gate = centred(seeds[0], (CH, SEQ), 1.0, 6.0, ((0, 4), (1, 32)))
    key_gate = centred(seeds[1], (CH, SEQ), 1.0, 6.0, ((0, 4), (1, 32)))
    value_input = centred(seeds[2], (CH, SEQ), 1.0, 6.0, ((0, 4), (1, 32)))
    long_filter = draw_long_filter(jax.random.fold_in(seeds[5], 71), 0)
    out_weight = centred(seeds[4], (CH, CH), CH ** -0.5, 0.375)
    return dict(query_gate=query_gate, key_gate=key_gate, value_input=value_input, long_filter=long_filter, out_weight=out_weight)


def conv_block(pair):
    gated, taps = pair
    extent = gated.shape[-1]
    spectrum = jnp.fft.rfft(gated, n=2 * extent, axis=-1) * jnp.fft.rfft(taps, n=2 * extent, axis=-1)
    return jnp.fft.irfft(spectrum, n=2 * extent, axis=-1)[:, :extent].astype(jnp.float32)


def reference(query_gate, key_gate, value_input, long_filter, out_weight):
    gated = key_gate.astype(jnp.float32) * value_input.astype(jnp.float32)
    blocks = 8 if CH % 8 == 0 else 1
    conv = lax.map(conv_block, (gated.reshape(blocks, CH // blocks, SEQ), long_filter.reshape(blocks, CH // blocks, SEQ)))
    conv = conv.reshape(CH, SEQ)
    gated_out = (query_gate.astype(jnp.float32) * conv).astype(jnp.bfloat16)
    return jnp.dot(out_weight, gated_out, preferred_element_type=jnp.float32).astype(jnp.bfloat16)
```

```python
import math

import jax
import jax.numpy as jnp
from jax import lax
from jax.sharding import PartitionSpec as P

HIGHEST = lax.Precision.HIGHEST


def angle_table(row_count, col_count, modulus, row_start, col_start):
    row_ids = lax.broadcasted_iota(jnp.int32, (row_count, col_count), 0) + row_start
    col_ids = lax.broadcasted_iota(jnp.int32, (row_count, col_count), 1) + col_start
    turns = row_ids * col_ids % modulus
    angles = turns.astype(jnp.float32) * (2.0 * math.pi / modulus)
    return (jnp.cos(angles), jnp.sin(angles))


def major(table, data):
    return jnp.einsum("qk,k...->q...", table, data, precision=HIGHEST)


def minor(data, table):
    return jnp.einsum("...b,bm->...m", data, table, precision=HIGHEST)


def body(query_gate, key_gate, value_input, long_filter, out_weight):
    chans, length = key_gate.shape
    seqs = lax.axis_size("seq")
    seq_index = lax.axis_index("seq")
    width = length // seqs
    rows = 2 * seqs
    per = rows // seqs
    full = rows * length
    f32, bf16 = jnp.float32, jnp.bfloat16

    gated = (key_gate.astype(f32) * value_input.astype(f32)).astype(bf16)
    both = jnp.concatenate([gated, long_filter.astype(bf16)], axis=0)
    send = both.reshape(2 * chans, seqs, width).transpose(1, 0, 2)
    got = lax.all_to_all(send, "seq", 0, 0, tiled=True).astype(f32)

    cos_a, sin_a = angle_table(rows, seqs, rows, 0, 0)
    freq_real = major(cos_a, got)
    freq_imag = -major(sin_a, got)
    cos_t, sin_t = angle_table(rows, width, full, 0, seq_index * width)
    cos_t, sin_t = cos_t[:, None, :], sin_t[:, None, :]
    spread_real = freq_real * cos_t + freq_imag * sin_t
    spread_imag = freq_imag * cos_t - freq_real * sin_t
    spread = jnp.stack([spread_real, spread_imag], axis=1).astype(bf16)
    spread = spread.reshape(seqs, per, 2, 2 * chans, width)
    recv = lax.all_to_all(spread, "seq", 0, 0, tiled=True).astype(f32)
    rows_real, rows_imag = recv[:, :, 0], recv[:, :, 1]

    cos_o, sin_o = angle_table(seqs, seqs, seqs, 0, 0)
    cos_w, sin_w = angle_table(seqs, width, length, 0, 0)
    cos_w, sin_w = cos_w[:, None, None, :], sin_w[:, None, None, :]
    cos_i, sin_i = angle_table(width, width, width, 0, 0)
    first_real = major(cos_o, rows_real) + major(sin_o, rows_imag)
    first_imag = major(cos_o, rows_imag) - major(sin_o, rows_real)
    twist_real = first_real * cos_w + first_imag * sin_w
    twist_imag = first_imag * cos_w - first_real * sin_w
    spec_real = minor(twist_real, cos_i) + minor(twist_imag, sin_i)
    spec_imag = minor(twist_imag, cos_i) - minor(twist_real, sin_i)

    signal_real, filter_real = spec_real[:, :, :chans], spec_real[:, :, chans:]
    signal_imag, filter_imag = spec_imag[:, :, :chans], spec_imag[:, :, chans:]
    prod_real = signal_real * filter_real - signal_imag * filter_imag
    prod_imag = signal_real * filter_imag + signal_imag * filter_real

    inv_real = minor(prod_real, cos_i) - minor(prod_imag, sin_i)
    inv_imag = minor(prod_imag, cos_i) + minor(prod_real, sin_i)
    untwist_real = inv_real * cos_w - inv_imag * sin_w
    untwist_imag = inv_imag * cos_w + inv_real * sin_w
    back_real = major(cos_o, untwist_real) - major(sin_o, untwist_imag)
    back_imag = major(cos_o, untwist_imag) + major(sin_o, untwist_real)

    cos_b, sin_b = angle_table(per, length, full, seq_index * per, 0)
    cos_b = cos_b.reshape(per, seqs, width).transpose(1, 0, 2)[:, :, None, :]
    sin_b = sin_b.reshape(per, seqs, width).transpose(1, 0, 2)[:, :, None, :]
    reverted_real = back_real * cos_b - back_imag * sin_b
    reverted_imag = back_imag * cos_b + back_real * sin_b
    reverted = jnp.stack([reverted_real, reverted_imag], axis=2).astype(bf16)
    moved = lax.all_to_all(reverted, "seq", 0, 0, tiled=True).astype(f32)
    moved = moved.reshape(rows, 2, chans, width)

    cos_l, sin_l = angle_table(seqs, rows, rows, 0, 0)
    merged = (major(cos_l, moved[:, 0]) - major(sin_l, moved[:, 1])) * (1.0 / full)
    arrived = lax.all_to_all(merged.astype(bf16), "seq", 0, 0, tiled=True)
    conv = arrived.astype(f32).transpose(1, 0, 2).reshape(chans, length)
    gated_out = (query_gate.astype(f32) * conv).astype(bf16)

    tp_index = lax.axis_index("tp")
    core = tp_index % 2
    half = tp_index // 2
    tps = lax.axis_size("tp")
    columns = lax.dynamic_slice_in_dim(out_weight, tp_index * chans, chans, 1)
    grouped = columns.reshape(2, 2, chans, chans)
    keep_w = lax.dynamic_index_in_dim(grouped, core, 1, keepdims=False)
    send_w = lax.dynamic_index_in_dim(grouped, 1 - core, 1, keepdims=False)
    send_part = jnp.einsum("hoc,cp->hop", send_w, gated_out, preferred_element_type=f32)
    keep_part = jnp.einsum("hoc,cp->hop", keep_w, gated_out, preferred_element_type=f32)
    pair = [(i, i ^ 1) for i in range(tps)]
    chip_sum = keep_part + lax.ppermute(send_part.astype(bf16), "tp", pair).astype(f32)
    keep_chip = lax.dynamic_index_in_dim(chip_sum, half, 0, keepdims=False)
    send_chip = lax.dynamic_index_in_dim(chip_sum, 1 - half, 0, keepdims=False)
    cross = [(i, i ^ 2) for i in range(tps)]
    total = keep_chip + lax.ppermute(send_chip.astype(bf16), "tp", cross).astype(f32)
    return total.astype(bf16)


def solution(mesh):
    return jax.shard_map(
        body,
        mesh=mesh,
        in_specs=(P("tp", "seq"), P("tp", "seq"), P("tp", "seq"), P("tp", "seq"), P()),
        out_specs=P("tp", "seq"),
        check_vma=False,
    )
```

```python
import math

import jax
import jax.numpy as jnp
from jax import lax
from jax.sharding import PartitionSpec as P

HIGHEST = lax.Precision.HIGHEST


def angle_table(row_count, col_count, modulus, row_start, col_start):
    row_ids = lax.broadcasted_iota(jnp.int32, (row_count, col_count), 0) + row_start
    col_ids = lax.broadcasted_iota(jnp.int32, (row_count, col_count), 1) + col_start
    return angles_of(row_ids * col_ids, modulus)


def angles_of(products, modulus):
    angles = (products % modulus).astype(jnp.float32) * (2.0 * math.pi / modulus)
    return (jnp.cos(angles), jnp.sin(angles))


def slot_rows(device, slot, seqs):
    return jnp.where(slot == 0, device, jnp.where(device == 0, seqs, 2 * seqs - device))


def major(table, data):
    return jnp.einsum("qk,k...->q...", table, data, precision=HIGHEST)


def minor(data, table):
    return jnp.einsum("...b,bm->...m", data, table, precision=HIGHEST)


def reversed_grid(data, seqs):
    return jnp.flip(data, axis=(0, data.ndim - 1))


def negated_grid(flipped):
    tail = jnp.roll(flipped[-1:], 1, axis=flipped.ndim - 1)
    return jnp.concatenate([tail, flipped[:-1]], axis=0)


def body(query_gate, key_gate, value_input, long_filter, out_weight):
    chans, length = key_gate.shape
    seqs = lax.axis_size("seq")
    seq_index = lax.axis_index("seq")
    width = length // seqs
    rows = 2 * seqs
    full = rows * length
    pairs = chans // 2
    f32, bf16 = jnp.float32, jnp.bfloat16

    gated = (key_gate.astype(f32) * value_input.astype(f32)).astype(bf16)
    taps = long_filter.astype(bf16)
    both = jnp.concatenate([gated[:pairs], taps[:pairs], gated[pairs:], taps[pairs:]], axis=0)
    send = both.reshape(2 * chans, seqs, width).transpose(1, 0, 2)
    got = lax.all_to_all(send, "seq", 0, 0, tiled=True).astype(f32)
    packed_real, packed_imag = got[:, :chans], got[:, chans:]

    slot_dev = lax.broadcasted_iota(jnp.int32, (seqs, 2), 0).reshape(rows, 1)
    slot_idx = lax.broadcasted_iota(jnp.int32, (seqs, 2), 1).reshape(rows, 1)
    row_of_slot = slot_rows(slot_dev, slot_idx, seqs)
    cos_a, sin_a = angles_of(row_of_slot * lax.broadcasted_iota(jnp.int32, (rows, seqs), 1), rows)
    freq_real = major(cos_a, packed_real) + major(sin_a, packed_imag)
    freq_imag = major(cos_a, packed_imag) - major(sin_a, packed_real)
    cols = lax.broadcasted_iota(jnp.int32, (rows, width), 1) + seq_index * width
    cos_t, sin_t = angles_of(row_of_slot * cols, full)
    cos_t, sin_t = cos_t[:, None, :], sin_t[:, None, :]
    spread_real = freq_real * cos_t + freq_imag * sin_t
    spread_imag = freq_imag * cos_t - freq_real * sin_t
    spread = jnp.stack([spread_real, spread_imag], axis=1).astype(bf16)
    spread = spread.reshape(seqs, 2, 2, chans, width)
    recv = lax.all_to_all(spread, "seq", 0, 0, tiled=True).astype(f32)
    rows_real, rows_imag = recv[:, :, 0], recv[:, :, 1]

    cos_o, sin_o = angle_table(seqs, seqs, seqs, 0, 0)
    cos_w, sin_w = angle_table(seqs, width, length, 0, 0)
    cos_w, sin_w = cos_w[:, None, None, :], sin_w[:, None, None, :]
    cos_i, sin_i = angle_table(width, width, width, 0, 0)
    first_real = major(cos_o, rows_real) + major(sin_o, rows_imag)
    first_imag = major(cos_o, rows_imag) - major(sin_o, rows_real)
    twist_real = first_real * cos_w + first_imag * sin_w
    twist_imag = first_imag * cos_w - first_real * sin_w
    spec_real = minor(twist_real, cos_i) + minor(twist_imag, sin_i)
    spec_imag = minor(twist_imag, cos_i) - minor(twist_real, sin_i)

    flip_real = reversed_grid(spec_real, seqs)
    flip_imag = reversed_grid(spec_imag, seqs)
    own_real = jnp.stack([negated_grid(flip_real[:, 0]), flip_real[:, 1]], axis=1)
    own_imag = jnp.stack([negated_grid(flip_imag[:, 0]), flip_imag[:, 1]], axis=1)
    first_dev = seq_index == 0
    neg_real = jnp.where(first_dev, own_real, flip_real[:, ::-1])
    neg_imag = jnp.where(first_dev, own_imag, flip_imag[:, ::-1])

    a_real = 0.5 * (spec_real + neg_real)
    a_imag = 0.5 * (spec_imag - neg_imag)
    b_real = 0.5 * (spec_imag + neg_imag)
    b_imag = 0.5 * (neg_real - spec_real)
    sig1_r, sig1_i, filt1_r, filt1_i = (
        a_real[:, :, :pairs], a_imag[:, :, :pairs], a_real[:, :, pairs:], a_imag[:, :, pairs:]
    )
    sig2_r, sig2_i, filt2_r, filt2_i = (
        b_real[:, :, :pairs], b_imag[:, :, :pairs], b_real[:, :, pairs:], b_imag[:, :, pairs:]
    )
    prod1_r = sig1_r * filt1_r - sig1_i * filt1_i
    prod1_i = sig1_r * filt1_i + sig1_i * filt1_r
    prod2_r = sig2_r * filt2_r - sig2_i * filt2_i
    prod2_i = sig2_r * filt2_i + sig2_i * filt2_r
    prod_real = prod1_r - prod2_i
    prod_imag = prod1_i + prod2_r

    inv_real = minor(prod_real, cos_i) - minor(prod_imag, sin_i)
    inv_imag = minor(prod_imag, cos_i) + minor(prod_real, sin_i)
    untwist_real = inv_real * cos_w - inv_imag * sin_w
    untwist_imag = inv_imag * cos_w + inv_real * sin_w
    back_real = major(cos_o, untwist_real) - major(sin_o, untwist_imag)
    back_imag = major(cos_o, untwist_imag) + major(sin_o, untwist_real)

    own_rows = slot_rows(seq_index, lax.broadcasted_iota(jnp.int32, (2, length), 0), seqs)
    cos_b, sin_b = angles_of(own_rows * lax.broadcasted_iota(jnp.int32, (2, length), 1), full)
    cos_b = cos_b.reshape(2, seqs, width).transpose(1, 0, 2)[:, :, None, :]
    sin_b = sin_b.reshape(2, seqs, width).transpose(1, 0, 2)[:, :, None, :]
    reverted_real = back_real * cos_b - back_imag * sin_b
    reverted_imag = back_imag * cos_b + back_real * sin_b
    reverted = jnp.stack([reverted_real, reverted_imag], axis=2).astype(bf16)
    moved = lax.all_to_all(reverted, "seq", 0, 0, tiled=True).astype(f32)
    moved = moved.reshape(rows, 2, pairs, width)

    blocks = lax.broadcasted_iota(jnp.int32, (seqs, rows), 0)
    cos_l, sin_l = angles_of(blocks * row_of_slot.reshape(1, rows), rows)
    merged_real = major(cos_l, moved[:, 0]) - major(sin_l, moved[:, 1])
    merged_imag = major(cos_l, moved[:, 1]) + major(sin_l, moved[:, 0])
    merged = jnp.concatenate([merged_real, merged_imag], axis=1) * (1.0 / full)
    arrived = lax.all_to_all(merged.astype(bf16), "seq", 0, 0, tiled=True)
    conv = arrived.astype(f32).transpose(1, 0, 2).reshape(chans, length)
    gated_out = (query_gate.astype(f32) * conv).astype(bf16)

    tp_index = lax.axis_index("tp")
    core = tp_index % 2
    half = tp_index // 2
    tps = lax.axis_size("tp")
    columns = lax.dynamic_slice_in_dim(out_weight, tp_index * chans, chans, 1)
    grouped = columns.reshape(2, 2, chans, chans)
    keep_w = lax.dynamic_index_in_dim(grouped, core, 1, keepdims=False)
    send_w = lax.dynamic_index_in_dim(grouped, 1 - core, 1, keepdims=False)
    send_part = jnp.einsum("hoc,cp->hop", send_w, gated_out, preferred_element_type=f32)
    keep_part = jnp.einsum("hoc,cp->hop", keep_w, gated_out, preferred_element_type=f32)
    pair = [(i, i ^ 1) for i in range(tps)]
    chip_sum = keep_part + lax.ppermute(send_part.astype(bf16), "tp", pair).astype(f32)
    keep_chip = lax.dynamic_index_in_dim(chip_sum, half, 0, keepdims=False)
    send_chip = lax.dynamic_index_in_dim(chip_sum, 1 - half, 0, keepdims=False)
    cross = [(i, i ^ 2) for i in range(tps)]
    total = keep_chip + lax.ppermute(send_chip.astype(bf16), "tp", cross).astype(f32)
    return total.astype(bf16)


def solution(mesh):
    return jax.shard_map(
        body,
        mesh=mesh,
        in_specs=(P("tp", "seq"), P("tp", "seq"), P("tp", "seq"), P("tp", "seq"), P()),
        out_specs=P("tp", "seq"),
        check_vma=False,
    )
```

```python
import math

import jax
import jax.numpy as jnp
from jax import lax
from jax.sharding import PartitionSpec as P

HIGH = lax.Precision.HIGH


def angle_table(row_count, col_count, modulus, row_start, col_start):
    row_ids = lax.broadcasted_iota(jnp.int32, (row_count, col_count), 0) + row_start
    col_ids = lax.broadcasted_iota(jnp.int32, (row_count, col_count), 1) + col_start
    return angles_of(row_ids * col_ids, modulus)


def angles_of(products, modulus):
    angles = (products % modulus).astype(jnp.float32) * (2.0 * math.pi / modulus)
    return (jnp.cos(angles), jnp.sin(angles))


def slot_rows(device, slot, seqs):
    return jnp.where(slot == 0, device, jnp.where(device == 0, seqs, 2 * seqs - device))


def major(table, data):
    return jnp.einsum("qk,k...->q...", table, data, precision=HIGH)


def minor(data, table):
    return jnp.einsum("...b,bm->...m", data, table, precision=HIGH)


def negated_grid(flipped):
    tail = jnp.roll(flipped[-1:], 1, axis=flipped.ndim - 1)
    return jnp.concatenate([tail, flipped[:-1]], axis=0)


def body(query_gate, key_gate, value_input, long_filter, out_weight):
    chans, length = key_gate.shape
    seqs = lax.axis_size("seq")
    seq_index = lax.axis_index("seq")
    width = length // seqs
    rows = 2 * seqs
    full = rows * length
    pairs = chans // 2
    f32, bf16 = jnp.float32, jnp.bfloat16

    gated = (key_gate.astype(f32) * value_input.astype(f32)).astype(bf16)
    taps = long_filter.astype(bf16)
    both = jnp.concatenate([gated[:pairs], taps[:pairs], gated[pairs:], taps[pairs:]], axis=0)
    send = both.reshape(2 * chans, seqs, width).transpose(1, 0, 2)
    got = lax.all_to_all(send, "seq", 0, 0, tiled=True).astype(f32)
    packed_real, packed_imag = got[:, :chans], got[:, chans:]

    slot_dev = lax.broadcasted_iota(jnp.int32, (seqs, 2), 0).reshape(rows, 1)
    slot_idx = lax.broadcasted_iota(jnp.int32, (seqs, 2), 1).reshape(rows, 1)
    row_of_slot = slot_rows(slot_dev, slot_idx, seqs)
    cos_a, sin_a = angles_of(row_of_slot * lax.broadcasted_iota(jnp.int32, (rows, seqs), 1), rows)
    freq_real = major(cos_a, packed_real) + major(sin_a, packed_imag)
    freq_imag = major(cos_a, packed_imag) - major(sin_a, packed_real)
    cols = lax.broadcasted_iota(jnp.int32, (rows, width), 1) + seq_index * width
    cos_t, sin_t = angles_of(row_of_slot * cols, full)
    cos_t, sin_t = cos_t[:, None, :], sin_t[:, None, :]
    spread_real = freq_real * cos_t + freq_imag * sin_t
    spread_imag = freq_imag * cos_t - freq_real * sin_t
    spread = jnp.stack([spread_real, spread_imag], axis=1).astype(bf16)
    spread = spread.reshape(seqs, 2, 2, chans, width)
    recv = lax.all_to_all(spread, "seq", 0, 0, tiled=True).astype(f32)
    rows_real, rows_imag = recv[:, :, 0], recv[:, :, 1]

    cos_o, sin_o = angle_table(seqs, seqs, seqs, 0, 0)
    cos_w, sin_w = angle_table(seqs, width, length, 0, 0)
    cos_w, sin_w = cos_w[:, None, None, :], sin_w[:, None, None, :]
    cos_i, sin_i = angle_table(width, width, width, 0, 0)
    first_real = major(cos_o, rows_real) + major(sin_o, rows_imag)
    first_imag = major(cos_o, rows_imag) - major(sin_o, rows_real)
    twist_real = first_real * cos_w + first_imag * sin_w
    twist_imag = first_imag * cos_w - first_real * sin_w
    spec_real = minor(twist_real, cos_i) + minor(twist_imag, sin_i)
    spec_imag = minor(twist_imag, cos_i) - minor(twist_real, sin_i)

    def self_paired(parts):
        flipped = [jnp.flip(part, axis=(0, 3)) for part in parts]
        return tuple(jnp.stack([negated_grid(f[:, 0]), f[:, 1]], axis=1) for f in flipped)

    def cross_paired(parts):
        return tuple(jnp.flip(part, axis=(0, 1, 3)) for part in parts)

    neg_real, neg_imag = lax.cond(
        seq_index == 0, self_paired, cross_paired, (spec_real, spec_imag)
    )

    a_real = 0.5 * (spec_real + neg_real)
    a_imag = 0.5 * (spec_imag - neg_imag)
    b_real = 0.5 * (spec_imag + neg_imag)
    b_imag = 0.5 * (neg_real - spec_real)
    sig1_r, sig1_i, filt1_r, filt1_i = (
        a_real[:, :, :pairs], a_imag[:, :, :pairs], a_real[:, :, pairs:], a_imag[:, :, pairs:]
    )
    sig2_r, sig2_i, filt2_r, filt2_i = (
        b_real[:, :, :pairs], b_imag[:, :, :pairs], b_real[:, :, pairs:], b_imag[:, :, pairs:]
    )
    prod1_r = sig1_r * filt1_r - sig1_i * filt1_i
    prod1_i = sig1_r * filt1_i + sig1_i * filt1_r
    prod2_r = sig2_r * filt2_r - sig2_i * filt2_i
    prod2_i = sig2_r * filt2_i + sig2_i * filt2_r
    prod_real = prod1_r - prod2_i
    prod_imag = prod1_i + prod2_r

    inv_real = minor(prod_real, cos_i) - minor(prod_imag, sin_i)
    inv_imag = minor(prod_imag, cos_i) + minor(prod_real, sin_i)
    untwist_real = inv_real * cos_w - inv_imag * sin_w
    untwist_imag = inv_imag * cos_w + inv_real * sin_w
    back_real = major(cos_o, untwist_real) - major(sin_o, untwist_imag)
    back_imag = major(cos_o, untwist_imag) + major(sin_o, untwist_real)

    own_rows = slot_rows(seq_index, lax.broadcasted_iota(jnp.int32, (2, length), 0), seqs)
    cos_b, sin_b = angles_of(own_rows * lax.broadcasted_iota(jnp.int32, (2, length), 1), full)
    cos_b = cos_b.reshape(2, seqs, width).transpose(1, 0, 2)[:, :, None, :]
    sin_b = sin_b.reshape(2, seqs, width).transpose(1, 0, 2)[:, :, None, :]
    reverted_real = back_real * cos_b - back_imag * sin_b
    reverted_imag = back_imag * cos_b + back_real * sin_b
    reverted = jnp.stack([reverted_real, reverted_imag], axis=2).astype(bf16)
    moved = lax.all_to_all(reverted, "seq", 0, 0, tiled=True).astype(f32)
    moved = moved.reshape(rows, 2, pairs, width)

    blocks = lax.broadcasted_iota(jnp.int32, (seqs, rows), 0)
    cos_l, sin_l = angles_of(blocks * row_of_slot.reshape(1, rows), rows)
    merged_real = major(cos_l, moved[:, 0]) - major(sin_l, moved[:, 1])
    merged_imag = major(cos_l, moved[:, 1]) + major(sin_l, moved[:, 0])
    merged = jnp.concatenate([merged_real, merged_imag], axis=1) * (1.0 / full)
    arrived = lax.all_to_all(merged.astype(bf16), "seq", 0, 0, tiled=True)
    conv = arrived.astype(f32).transpose(1, 0, 2).reshape(chans, length)
    gated_out = (query_gate.astype(f32) * conv).astype(bf16)

    tp_index = lax.axis_index("tp")
    core = tp_index % 2
    half = tp_index // 2
    tps = lax.axis_size("tp")
    columns = lax.dynamic_slice_in_dim(out_weight, tp_index * chans, chans, 1)
    grouped = columns.reshape(2, 2, chans, chans)
    keep_w = lax.dynamic_index_in_dim(grouped, core, 1, keepdims=False)
    send_w = lax.dynamic_index_in_dim(grouped, 1 - core, 1, keepdims=False)
    send_part = jnp.einsum("hoc,cp->hop", send_w, gated_out, preferred_element_type=f32)
    keep_part = jnp.einsum("hoc,cp->hop", keep_w, gated_out, preferred_element_type=f32)
    pair = [(i, i ^ 1) for i in range(tps)]
    chip_sum = keep_part + lax.ppermute(send_part.astype(bf16), "tp", pair).astype(f32)
    keep_chip = lax.dynamic_index_in_dim(chip_sum, half, 0, keepdims=False)
    send_chip = lax.dynamic_index_in_dim(chip_sum, 1 - half, 0, keepdims=False)
    cross = [(i, i ^ 2) for i in range(tps)]
    total = keep_chip + lax.ppermute(send_chip.astype(bf16), "tp", cross).astype(f32)
    return total.astype(bf16)


def solution(mesh):
    return jax.shard_map(
        body,
        mesh=mesh,
        in_specs=(P("tp", "seq"), P("tp", "seq"), P("tp", "seq"), P("tp", "seq"), P()),
        out_specs=P("tp", "seq"),
        check_vma=False,
    )
```

```python
import math

import jax
import jax.numpy as jnp
from jax import lax
from jax.sharding import PartitionSpec as P

HIGH = lax.Precision.HIGH


def angle_table(row_count, col_count, modulus, row_start, col_start):
    row_ids = lax.broadcasted_iota(jnp.int32, (row_count, col_count), 0) + row_start
    col_ids = lax.broadcasted_iota(jnp.int32, (row_count, col_count), 1) + col_start
    return angles_of(row_ids * col_ids, modulus)


def angles_of(products, modulus):
    angles = (products % modulus).astype(jnp.float32) * (2.0 * math.pi / modulus)
    return (jnp.cos(angles), jnp.sin(angles))


def slot_rows(device, slot, seqs):
    return jnp.where(slot == 0, device, jnp.where(device == 0, seqs, 2 * seqs - device))


def major(table, data):
    return jnp.einsum("qk,k...->q...", table, data, precision=HIGH)


def minor(data, table):
    return jnp.einsum("...b,bm->...m", data, table, precision=HIGH)


def body(query_gate, key_gate, value_input, long_filter, out_weight):
    chans, length = key_gate.shape
    seqs = lax.axis_size("seq")
    seq_index = lax.axis_index("seq")
    width = length // seqs
    rows = 2 * seqs
    full = rows * length
    pairs = chans // 2
    f32, bf16 = jnp.float32, jnp.bfloat16

    gated = (key_gate.astype(f32) * value_input.astype(f32)).astype(bf16)
    taps = long_filter.astype(bf16)
    both = jnp.concatenate([gated[:pairs], taps[:pairs], gated[pairs:], taps[pairs:]], axis=0)
    send = both.reshape(2 * chans, seqs, width).transpose(1, 0, 2)
    got = lax.all_to_all(send, "seq", 0, 0, tiled=True).astype(f32)
    packed_real, packed_imag = got[:, :chans], got[:, chans:]

    slot_dev = lax.broadcasted_iota(jnp.int32, (seqs, 2), 0).reshape(rows, 1)
    slot_idx = lax.broadcasted_iota(jnp.int32, (seqs, 2), 1).reshape(rows, 1)
    row_of_slot = slot_rows(slot_dev, slot_idx, seqs)
    cos_a, sin_a = angles_of(row_of_slot * lax.broadcasted_iota(jnp.int32, (rows, seqs), 1), rows)
    freq_real = major(cos_a, packed_real) + major(sin_a, packed_imag)
    freq_imag = major(cos_a, packed_imag) - major(sin_a, packed_real)
    cols = lax.broadcasted_iota(jnp.int32, (rows, width), 1) + seq_index * width
    cos_t, sin_t = angles_of(row_of_slot * cols, full)
    cos_t, sin_t = cos_t[:, None, :], sin_t[:, None, :]
    spread_real = freq_real * cos_t + freq_imag * sin_t
    spread_imag = freq_imag * cos_t - freq_real * sin_t
    spread = jnp.stack([spread_real, spread_imag], axis=1).astype(bf16)
    spread = spread.reshape(seqs, 2, 2, chans, width)
    recv = lax.all_to_all(spread, "seq", 0, 0, tiled=True).astype(f32)
    rows_real, rows_imag = recv[:, :, 0], recv[:, :, 1]

    cos_o, sin_o = angle_table(seqs, seqs, seqs, 0, 0)
    cos_w, sin_w = angle_table(seqs, width, length, 0, 0)
    cos_w, sin_w = cos_w[:, None, None, :], sin_w[:, None, None, :]
    cos_i, sin_i = angle_table(width, width, width, 0, 0)
    first_real = major(cos_o, rows_real) + major(sin_o, rows_imag)
    first_imag = major(cos_o, rows_imag) - major(sin_o, rows_real)
    twist_real = first_real * cos_w + first_imag * sin_w
    twist_imag = first_imag * cos_w - first_real * sin_w
    spec_real = minor(twist_real, cos_i) + minor(twist_imag, sin_i)
    spec_imag = minor(twist_imag, cos_i) - minor(twist_real, sin_i)

    def self_paired(parts):
        slot = lax.broadcasted_iota(jnp.int32, parts[0].shape, 1)
        out = []
        for part in parts:
            shifted = jnp.where(slot == 0, jnp.roll(part, -1, axis=0), part)
            flipped = jnp.flip(shifted, axis=(0, 3))
            out.append(flipped.at[0, 0].set(jnp.roll(flipped[0, 0], 1, axis=-1)))
        return tuple(out)

    def cross_paired(parts):
        return tuple(jnp.flip(part, axis=(0, 1, 3)) for part in parts)

    neg_real, neg_imag = lax.cond(
        seq_index == 0, self_paired, cross_paired, (spec_real, spec_imag)
    )

    a_real = 0.5 * (spec_real + neg_real)
    a_imag = 0.5 * (spec_imag - neg_imag)
    b_real = 0.5 * (spec_imag + neg_imag)
    b_imag = 0.5 * (neg_real - spec_real)
    sig1_r, sig1_i, filt1_r, filt1_i = (
        a_real[:, :, :pairs], a_imag[:, :, :pairs], a_real[:, :, pairs:], a_imag[:, :, pairs:]
    )
    sig2_r, sig2_i, filt2_r, filt2_i = (
        b_real[:, :, :pairs], b_imag[:, :, :pairs], b_real[:, :, pairs:], b_imag[:, :, pairs:]
    )
    prod1_r = sig1_r * filt1_r - sig1_i * filt1_i
    prod1_i = sig1_r * filt1_i + sig1_i * filt1_r
    prod2_r = sig2_r * filt2_r - sig2_i * filt2_i
    prod2_i = sig2_r * filt2_i + sig2_i * filt2_r
    prod_real = prod1_r - prod2_i
    prod_imag = prod1_i + prod2_r

    inv_real = minor(prod_real, cos_i) - minor(prod_imag, sin_i)
    inv_imag = minor(prod_imag, cos_i) + minor(prod_real, sin_i)
    untwist_real = inv_real * cos_w - inv_imag * sin_w
    untwist_imag = inv_imag * cos_w + inv_real * sin_w
    back_real = major(cos_o, untwist_real) - major(sin_o, untwist_imag)
    back_imag = major(cos_o, untwist_imag) + major(sin_o, untwist_real)

    own_rows = slot_rows(seq_index, lax.broadcasted_iota(jnp.int32, (2, length), 0), seqs)
    cos_b, sin_b = angles_of(own_rows * lax.broadcasted_iota(jnp.int32, (2, length), 1), full)
    cos_b = cos_b.reshape(2, seqs, width).transpose(1, 0, 2)[:, :, None, :]
    sin_b = sin_b.reshape(2, seqs, width).transpose(1, 0, 2)[:, :, None, :]
    reverted_real = back_real * cos_b - back_imag * sin_b
    reverted_imag = back_imag * cos_b + back_real * sin_b
    reverted = jnp.stack([reverted_real, reverted_imag], axis=2).astype(bf16)
    moved = lax.all_to_all(reverted, "seq", 0, 0, tiled=True).astype(f32)
    moved = moved.reshape(rows, 2, pairs, width)

    blocks = lax.broadcasted_iota(jnp.int32, (seqs, rows), 0)
    cos_l, sin_l = angles_of(blocks * row_of_slot.reshape(1, rows), rows)
    merged_real = major(cos_l, moved[:, 0]) - major(sin_l, moved[:, 1])
    merged_imag = major(cos_l, moved[:, 1]) + major(sin_l, moved[:, 0])
    merged = jnp.concatenate([merged_real, merged_imag], axis=1) * (1.0 / full)
    arrived = lax.all_to_all(merged.astype(bf16), "seq", 0, 0, tiled=True)
    conv = arrived.astype(f32).transpose(1, 0, 2).reshape(chans, length)
    gated_out = (query_gate.astype(f32) * conv).astype(bf16)

    tp_index = lax.axis_index("tp")
    core = tp_index % 2
    half = tp_index // 2
    tps = lax.axis_size("tp")
    columns = lax.dynamic_slice_in_dim(out_weight, tp_index * chans, chans, 1)
    grouped = columns.reshape(2, 2, chans, chans)
    keep_w = lax.dynamic_index_in_dim(grouped, core, 1, keepdims=False)
    send_w = lax.dynamic_index_in_dim(grouped, 1 - core, 1, keepdims=False)
    send_part = jnp.einsum("hoc,cp->hop", send_w, gated_out, preferred_element_type=f32)
    keep_part = jnp.einsum("hoc,cp->hop", keep_w, gated_out, preferred_element_type=f32)
    pair = [(i, i ^ 1) for i in range(tps)]
    chip_sum = keep_part + lax.ppermute(send_part.astype(bf16), "tp", pair).astype(f32)
    keep_chip = lax.dynamic_index_in_dim(chip_sum, half, 0, keepdims=False)
    send_chip = lax.dynamic_index_in_dim(chip_sum, 1 - half, 0, keepdims=False)
    cross = [(i, i ^ 2) for i in range(tps)]
    total = keep_chip + lax.ppermute(send_chip.astype(bf16), "tp", cross).astype(f32)
    return total.astype(bf16)


def solution(mesh):
    return jax.shard_map(
        body,
        mesh=mesh,
        in_specs=(P("tp", "seq"), P("tp", "seq"), P("tp", "seq"), P("tp", "seq"), P()),
        out_specs=P("tp", "seq"),
        check_vma=False,
    )
```

```python
import math

import jax
import jax.numpy as jnp
from jax import lax
from jax.sharding import PartitionSpec as P

HIGH = lax.Precision.HIGH
HIGHEST = lax.Precision.HIGHEST


def angle_table(row_count, col_count, modulus, row_start, col_start):
    row_ids = lax.broadcasted_iota(jnp.int32, (row_count, col_count), 0) + row_start
    col_ids = lax.broadcasted_iota(jnp.int32, (row_count, col_count), 1) + col_start
    return angles_of(row_ids * col_ids, modulus)


def angles_of(products, modulus):
    angles = (products % modulus).astype(jnp.float32) * (2.0 * math.pi / modulus)
    return (jnp.cos(angles), jnp.sin(angles))


def slot_rows(device, slot, seqs):
    return jnp.where(slot == 0, device, jnp.where(device == 0, seqs, 2 * seqs - device))


def major(table, data):
    return jnp.einsum("qk,k...->q...", table, data, precision=HIGH)


def minor(data, table):
    return jnp.einsum("...b,bm->...m", data, table, precision=HIGH)


def body(query_gate, key_gate, value_input, long_filter, out_weight):
    chans, length = key_gate.shape
    seqs = lax.axis_size("seq")
    seq_index = lax.axis_index("seq")
    width = length // seqs
    rows = 2 * seqs
    full = rows * length
    pairs = chans // 2
    f32, bf16 = jnp.float32, jnp.bfloat16

    gated = (key_gate.astype(f32) * value_input.astype(f32)).astype(bf16)
    taps = long_filter.astype(bf16)
    both = jnp.concatenate([gated[:pairs], taps[:pairs], gated[pairs:], taps[pairs:]], axis=0)
    send = both.reshape(2 * chans, seqs, width).transpose(1, 0, 2)
    got = lax.all_to_all(send, "seq", 0, 0, tiled=True).astype(f32)
    packed_real, packed_imag = got[:, :chans], got[:, chans:]

    slot_dev = lax.broadcasted_iota(jnp.int32, (seqs, 2), 0).reshape(rows, 1)
    slot_idx = lax.broadcasted_iota(jnp.int32, (seqs, 2), 1).reshape(rows, 1)
    row_of_slot = slot_rows(slot_dev, slot_idx, seqs)
    cos_a, sin_a = angles_of(row_of_slot * lax.broadcasted_iota(jnp.int32, (rows, seqs), 1), rows)
    freq_real = major(cos_a, packed_real) + major(sin_a, packed_imag)
    freq_imag = major(cos_a, packed_imag) - major(sin_a, packed_real)
    cols = lax.broadcasted_iota(jnp.int32, (rows, width), 1) + seq_index * width
    cos_t, sin_t = angles_of(row_of_slot * cols, full)
    cos_t, sin_t = cos_t[:, None, :], sin_t[:, None, :]
    spread_real = freq_real * cos_t + freq_imag * sin_t
    spread_imag = freq_imag * cos_t - freq_real * sin_t
    spread = jnp.stack([spread_real, spread_imag], axis=1).astype(bf16)
    spread = spread.reshape(seqs, 2, 2, chans, width)
    recv = lax.all_to_all(spread, "seq", 0, 0, tiled=True).astype(f32)
    rows_real, rows_imag = recv[:, :, 0], recv[:, :, 1]

    cos_o, sin_o = angle_table(seqs, seqs, seqs, 0, 0)
    cos_w, sin_w = angle_table(seqs, width, length, 0, 0)
    cos_w, sin_w = cos_w[:, None, None, :], sin_w[:, None, None, :]
    cos_i, sin_i = angle_table(width, width, width, 0, 0)
    first_real = major(cos_o, rows_real) + major(sin_o, rows_imag)
    first_imag = major(cos_o, rows_imag) - major(sin_o, rows_real)
    twist_real = first_real * cos_w + first_imag * sin_w
    twist_imag = first_imag * cos_w - first_real * sin_w
    spec_real = minor(twist_real, cos_i) + minor(twist_imag, sin_i)
    spec_imag = minor(twist_imag, cos_i) - minor(twist_real, sin_i)

    lane_in = lax.broadcasted_iota(jnp.int32, (width, width), 0)
    lane_out = lax.broadcasted_iota(jnp.int32, (width, width), 1)
    lane_flip = (lane_in == width - 1 - lane_out).astype(f32)
    lane_neg = (lane_in == (width - lane_out) % width).astype(f32)
    place = lax.broadcasted_iota(jnp.int32, (rows, rows), 0)
    source = lax.broadcasted_iota(jnp.int32, (rows, rows), 1)
    place_q, place_s = place // 2, place % 2
    cross_src = 2 * (seqs - 1 - place_q) + 1 - place_s
    self_src = jnp.where(place_s == 1, 2 * (seqs - 1 - place_q) + 1, 2 * ((seqs - place_q) % seqs))
    first_dev = seq_index == 0
    regroup = (source == jnp.where(first_dev, self_src, cross_src)).astype(f32)

    def negated(spec):
        flipped = jnp.einsum("...b,bm->...m", spec, lane_flip, precision=HIGHEST)
        moved = jnp.einsum(
            "uv,vcb->ucb", regroup, flipped.reshape(rows, chans, width), precision=HIGHEST
        ).reshape(spec.shape)
        corner = jnp.einsum("cb,bm->cm", spec[0, 0], lane_neg, precision=HIGHEST)
        return moved.at[0, 0].set(jnp.where(first_dev, corner, moved[0, 0]))

    neg_real = negated(spec_real)
    neg_imag = negated(spec_imag)

    a_real = 0.5 * (spec_real + neg_real)
    a_imag = 0.5 * (spec_imag - neg_imag)
    b_real = 0.5 * (spec_imag + neg_imag)
    b_imag = 0.5 * (neg_real - spec_real)
    sig1_r, sig1_i, filt1_r, filt1_i = (
        a_real[:, :, :pairs], a_imag[:, :, :pairs], a_real[:, :, pairs:], a_imag[:, :, pairs:]
    )
    sig2_r, sig2_i, filt2_r, filt2_i = (
        b_real[:, :, :pairs], b_imag[:, :, :pairs], b_real[:, :, pairs:], b_imag[:, :, pairs:]
    )
    prod1_r = sig1_r * filt1_r - sig1_i * filt1_i
    prod1_i = sig1_r * filt1_i + sig1_i * filt1_r
    prod2_r = sig2_r * filt2_r - sig2_i * filt2_i
    prod2_i = sig2_r * filt2_i + sig2_i * filt2_r
    prod_real = prod1_r - prod2_i
    prod_imag = prod1_i + prod2_r

    inv_real = minor(prod_real, cos_i) - minor(prod_imag, sin_i)
    inv_imag = minor(prod_imag, cos_i) + minor(prod_real, sin_i)
    untwist_real = inv_real * cos_w - inv_imag * sin_w
    untwist_imag = inv_imag * cos_w + inv_real * sin_w
    back_real = major(cos_o, untwist_real) - major(sin_o, untwist_imag)
    back_imag = major(cos_o, untwist_imag) + major(sin_o, untwist_real)

    own_rows = slot_rows(seq_index, lax.broadcasted_iota(jnp.int32, (2, length), 0), seqs)
    cos_b, sin_b = angles_of(own_rows * lax.broadcasted_iota(jnp.int32, (2, length), 1), full)
    cos_b = cos_b.reshape(2, seqs, width).transpose(1, 0, 2)[:, :, None, :]
    sin_b = sin_b.reshape(2, seqs, width).transpose(1, 0, 2)[:, :, None, :]
    reverted_real = back_real * cos_b - back_imag * sin_b
    reverted_imag = back_imag * cos_b + back_real * sin_b
    reverted = jnp.stack([reverted_real, reverted_imag], axis=2).astype(bf16)
    moved = lax.all_to_all(reverted, "seq", 0, 0, tiled=True).astype(f32)
    moved = moved.reshape(rows, 2, pairs, width)

    blocks = lax.broadcasted_iota(jnp.int32, (seqs, rows), 0)
    cos_l, sin_l = angles_of(blocks * row_of_slot.reshape(1, rows), rows)
    merged_real = major(cos_l, moved[:, 0]) - major(sin_l, moved[:, 1])
    merged_imag = major(cos_l, moved[:, 1]) + major(sin_l, moved[:, 0])
    merged = jnp.concatenate([merged_real, merged_imag], axis=1) * (1.0 / full)
    arrived = lax.all_to_all(merged.astype(bf16), "seq", 0, 0, tiled=True)
    conv = arrived.astype(f32).transpose(1, 0, 2).reshape(chans, length)
    gated_out = (query_gate.astype(f32) * conv).astype(bf16)

    tp_index = lax.axis_index("tp")
    core = tp_index % 2
    half = tp_index // 2
    tps = lax.axis_size("tp")
    columns = lax.dynamic_slice_in_dim(out_weight, tp_index * chans, chans, 1)
    grouped = columns.reshape(2, 2, chans, chans)
    keep_w = lax.dynamic_index_in_dim(grouped, core, 1, keepdims=False)
    send_w = lax.dynamic_index_in_dim(grouped, 1 - core, 1, keepdims=False)
    send_part = jnp.einsum("hoc,cp->hop", send_w, gated_out, preferred_element_type=f32)
    keep_part = jnp.einsum("hoc,cp->hop", keep_w, gated_out, preferred_element_type=f32)
    pair = [(i, i ^ 1) for i in range(tps)]
    chip_sum = keep_part + lax.ppermute(send_part.astype(bf16), "tp", pair).astype(f32)
    keep_chip = lax.dynamic_index_in_dim(chip_sum, half, 0, keepdims=False)
    send_chip = lax.dynamic_index_in_dim(chip_sum, 1 - half, 0, keepdims=False)
    cross = [(i, i ^ 2) for i in range(tps)]
    total = keep_chip + lax.ppermute(send_chip.astype(bf16), "tp", cross).astype(f32)
    return total.astype(bf16)


def solution(mesh):
    return jax.shard_map(
        body,
        mesh=mesh,
        in_specs=(P("tp", "seq"), P("tp", "seq"), P("tp", "seq"), P("tp", "seq"), P()),
        out_specs=P("tp", "seq"),
        check_vma=False,
    )
```

```python
import math

import jax
import numpy as np
import jax.numpy as jnp
from jax import lax
from jax.sharding import PartitionSpec as P

HIGH = lax.Precision.HIGH
HIGHEST = lax.Precision.HIGHEST


def turn_table(row_ids, col_ids, modulus):
    turns = (np.asarray(row_ids, np.int64)[:, None] * np.asarray(col_ids, np.int64)[None, :]) % modulus
    angles = turns.astype(np.float64) * (2.0 * math.pi / modulus)
    return (jnp.asarray(np.cos(angles), jnp.float32), jnp.asarray(np.sin(angles), jnp.float32))


def row_list(seqs):
    return np.array([d if s == 0 else (seqs if d == 0 else 2 * seqs - d) for d in range(seqs) for s in range(2)])


def slot_rows(device, slot, seqs):
    return jnp.where(slot == 0, device, jnp.where(device == 0, seqs, 2 * seqs - device))


def major(table, data):
    return jnp.einsum("qk,k...->q...", table, data, precision=HIGH)


def minor(data, table):
    return jnp.einsum("...b,bm->...m", data, table, precision=HIGH)


def body(query_gate, key_gate, value_input, long_filter, out_weight):
    chans, length = key_gate.shape
    seqs = lax.axis_size("seq")
    seq_index = lax.axis_index("seq")
    width = length // seqs
    rows = 2 * seqs
    full = rows * length
    pairs = chans // 2
    f32, bf16 = jnp.float32, jnp.bfloat16

    gated = (key_gate.astype(f32) * value_input.astype(f32)).astype(bf16)
    taps = long_filter.astype(bf16)
    both = jnp.concatenate([gated[:pairs], taps[:pairs], gated[pairs:], taps[pairs:]], axis=0)
    send = both.reshape(2 * chans, seqs, width).transpose(1, 0, 2)
    got = lax.all_to_all(send, "seq", 0, 0, tiled=True).astype(f32)
    packed_real, packed_imag = got[:, :chans], got[:, chans:]

    row_ids = row_list(seqs)
    cos_a, sin_a = turn_table(row_ids, np.arange(seqs), rows)
    freq_real = major(cos_a, packed_real) + major(sin_a, packed_imag)
    freq_imag = major(cos_a, packed_imag) - major(sin_a, packed_real)
    cos_dev, sin_dev = turn_table(np.arange(seqs) * width, row_ids, full)
    cos_dev = lax.dynamic_index_in_dim(cos_dev, seq_index, 0, keepdims=False)[:, None, None]
    sin_dev = lax.dynamic_index_in_dim(sin_dev, seq_index, 0, keepdims=False)[:, None, None]
    cos_col, sin_col = turn_table(row_ids, np.arange(width), full)
    cos_col, sin_col = cos_col[:, None, :], sin_col[:, None, :]
    cos_t = cos_dev * cos_col - sin_dev * sin_col
    sin_t = sin_dev * cos_col + cos_dev * sin_col
    spread_real = freq_real * cos_t + freq_imag * sin_t
    spread_imag = freq_imag * cos_t - freq_real * sin_t
    spread = jnp.stack([spread_real, spread_imag], axis=1).astype(bf16)
    spread = spread.reshape(seqs, 2, 2, chans, width)
    recv = lax.all_to_all(spread, "seq", 0, 0, tiled=True).astype(f32)
    rows_real, rows_imag = recv[:, :, 0], recv[:, :, 1]

    cos_o, sin_o = turn_table(np.arange(seqs), np.arange(seqs), seqs)
    cos_w, sin_w = turn_table(np.arange(seqs), np.arange(width), length)
    cos_w, sin_w = cos_w[:, None, None, :], sin_w[:, None, None, :]
    cos_i, sin_i = turn_table(np.arange(width), np.arange(width), width)
    first_real = major(cos_o, rows_real) + major(sin_o, rows_imag)
    first_imag = major(cos_o, rows_imag) - major(sin_o, rows_real)
    twist_real = first_real * cos_w + first_imag * sin_w
    twist_imag = first_imag * cos_w - first_real * sin_w
    spec_real = minor(twist_real, cos_i) + minor(twist_imag, sin_i)
    spec_imag = minor(twist_imag, cos_i) - minor(twist_real, sin_i)

    lane_in = lax.broadcasted_iota(jnp.int32, (width, width), 0)
    lane_out = lax.broadcasted_iota(jnp.int32, (width, width), 1)
    lane_flip = (lane_in == width - 1 - lane_out).astype(f32)
    lane_neg = (lane_in == (width - lane_out) % width).astype(f32)
    place = lax.broadcasted_iota(jnp.int32, (rows, rows), 0)
    source = lax.broadcasted_iota(jnp.int32, (rows, rows), 1)
    place_q, place_s = place // 2, place % 2
    cross_src = 2 * (seqs - 1 - place_q) + 1 - place_s
    self_src = jnp.where(place_s == 1, 2 * (seqs - 1 - place_q) + 1, 2 * ((seqs - place_q) % seqs))
    first_dev = seq_index == 0
    regroup = (source == jnp.where(first_dev, self_src, cross_src)).astype(f32)

    def negated(spec):
        flipped = jnp.einsum("...b,bm->...m", spec, lane_flip, precision=HIGHEST)
        moved = jnp.einsum(
            "uv,vcb->ucb", regroup, flipped.reshape(rows, chans, width), precision=HIGHEST
        ).reshape(spec.shape)
        corner = jnp.einsum("cb,bm->cm", spec[0, 0], lane_neg, precision=HIGHEST)
        return moved.at[0, 0].set(jnp.where(first_dev, corner, moved[0, 0]))

    neg_real = negated(spec_real)
    neg_imag = negated(spec_imag)

    a_real = 0.5 * (spec_real + neg_real)
    a_imag = 0.5 * (spec_imag - neg_imag)
    b_real = 0.5 * (spec_imag + neg_imag)
    b_imag = 0.5 * (neg_real - spec_real)
    sig1_r, sig1_i, filt1_r, filt1_i = (
        a_real[:, :, :pairs], a_imag[:, :, :pairs], a_real[:, :, pairs:], a_imag[:, :, pairs:]
    )
    sig2_r, sig2_i, filt2_r, filt2_i = (
        b_real[:, :, :pairs], b_imag[:, :, :pairs], b_real[:, :, pairs:], b_imag[:, :, pairs:]
    )
    prod1_r = sig1_r * filt1_r - sig1_i * filt1_i
    prod1_i = sig1_r * filt1_i + sig1_i * filt1_r
    prod2_r = sig2_r * filt2_r - sig2_i * filt2_i
    prod2_i = sig2_r * filt2_i + sig2_i * filt2_r
    prod_real = prod1_r - prod2_i
    prod_imag = prod1_i + prod2_r

    inv_real = minor(prod_real, cos_i) - minor(prod_imag, sin_i)
    inv_imag = minor(prod_imag, cos_i) + minor(prod_real, sin_i)
    untwist_real = inv_real * cos_w - inv_imag * sin_w
    untwist_imag = inv_imag * cos_w + inv_real * sin_w
    back_real = major(cos_o, untwist_real) - major(sin_o, untwist_imag)
    back_imag = major(cos_o, untwist_imag) + major(sin_o, untwist_real)

    own_rows = slot_rows(seq_index, jnp.arange(2), seqs)
    cos_blk, sin_blk = turn_table(np.arange(rows), np.arange(seqs) * width, full)
    cos_off, sin_off = turn_table(np.arange(rows), np.arange(width), full)
    cos_blk, sin_blk = jnp.take(cos_blk, own_rows, axis=0).T, jnp.take(sin_blk, own_rows, axis=0).T
    cos_off, sin_off = jnp.take(cos_off, own_rows, axis=0), jnp.take(sin_off, own_rows, axis=0)
    cos_b = (cos_blk[:, :, None] * cos_off[None] - sin_blk[:, :, None] * sin_off[None])[:, :, None, :]
    sin_b = (sin_blk[:, :, None] * cos_off[None] + cos_blk[:, :, None] * sin_off[None])[:, :, None, :]
    reverted_real = back_real * cos_b - back_imag * sin_b
    reverted_imag = back_imag * cos_b + back_real * sin_b
    reverted = jnp.stack([reverted_real, reverted_imag], axis=2).astype(bf16)
    moved = lax.all_to_all(reverted, "seq", 0, 0, tiled=True).astype(f32)
    moved = moved.reshape(rows, 2, pairs, width)

    cos_l, sin_l = turn_table(np.arange(seqs), row_ids, rows)
    merged_real = major(cos_l, moved[:, 0]) - major(sin_l, moved[:, 1])
    merged_imag = major(cos_l, moved[:, 1]) + major(sin_l, moved[:, 0])
    merged = jnp.concatenate([merged_real, merged_imag], axis=1) * (1.0 / full)
    arrived = lax.all_to_all(merged.astype(bf16), "seq", 0, 0, tiled=True)
    conv = arrived.astype(f32).transpose(1, 0, 2).reshape(chans, length)
    gated_out = (query_gate.astype(f32) * conv).astype(bf16)

    tp_index = lax.axis_index("tp")
    core = tp_index % 2
    half = tp_index // 2
    tps = lax.axis_size("tp")
    columns = lax.dynamic_slice_in_dim(out_weight, tp_index * chans, chans, 1)
    grouped = columns.reshape(2, 2, chans, chans)
    keep_w = lax.dynamic_index_in_dim(grouped, core, 1, keepdims=False)
    send_w = lax.dynamic_index_in_dim(grouped, 1 - core, 1, keepdims=False)
    send_part = jnp.einsum("hoc,cp->hop", send_w, gated_out, preferred_element_type=f32)
    keep_part = jnp.einsum("hoc,cp->hop", keep_w, gated_out, preferred_element_type=f32)
    pair = [(i, i ^ 1) for i in range(tps)]
    chip_sum = keep_part + lax.ppermute(send_part.astype(bf16), "tp", pair).astype(f32)
    keep_chip = lax.dynamic_index_in_dim(chip_sum, half, 0, keepdims=False)
    send_chip = lax.dynamic_index_in_dim(chip_sum, 1 - half, 0, keepdims=False)
    cross = [(i, i ^ 2) for i in range(tps)]
    total = keep_chip + lax.ppermute(send_chip.astype(bf16), "tp", cross).astype(f32)
    return total.astype(bf16)


def solution(mesh):
    return jax.shard_map(
        body,
        mesh=mesh,
        in_specs=(P("tp", "seq"), P("tp", "seq"), P("tp", "seq"), P("tp", "seq"), P()),
        out_specs=P("tp", "seq"),
        check_vma=False,
    )
```

```python
import math

import jax
import numpy as np
import jax.numpy as jnp
from jax import lax
from jax.experimental import pallas as pl
from jax.sharding import PartitionSpec as P

HIGH = lax.Precision.HIGH
HIGHEST = lax.Precision.HIGHEST


def turn_table(row_ids, col_ids, modulus):
    turns = (np.asarray(row_ids, np.int64)[:, None] * np.asarray(col_ids, np.int64)[None, :]) % modulus
    angles = turns.astype(np.float64) * (2.0 * math.pi / modulus)
    return (jnp.asarray(np.cos(angles), jnp.float32), jnp.asarray(np.sin(angles), jnp.float32))


def row_list(seqs):
    return np.array([d if s == 0 else (seqs if d == 0 else 2 * seqs - d) for d in range(seqs) for s in range(2)])


def slot_rows(device, slot, seqs):
    return jnp.where(slot == 0, device, jnp.where(device == 0, seqs, 2 * seqs - device))


def major(table, data):
    return jnp.einsum("qk,k...->q...", table, data, precision=HIGH)


def minor(data, table):
    return jnp.einsum("...b,bm->...m", data, table, precision=HIGH)


def send_blocks(key_gate, value_input, long_filter, seqs, interpret=False):
    chans, length = key_gate.shape
    width = length // seqs
    pairs = chans // 2

    def kernel(key_ref, value_ref, taps_ref, out_ref):
        gated = (key_ref[...].astype(jnp.float32) * value_ref[...].astype(jnp.float32)).astype(jnp.bfloat16)
        taps = taps_ref[...].astype(jnp.bfloat16)
        out_ref[0, 0:pairs] = gated[:pairs]
        out_ref[0, pairs:chans] = taps[:pairs]
        out_ref[0, chans:chans + pairs] = gated[pairs:]
        out_ref[0, chans + pairs:2 * chans] = taps[pairs:]

    block = pl.BlockSpec((chans, width), lambda d: (0, d))
    return pl.pallas_call(
        kernel,
        grid=(seqs,),
        in_specs=[block, block, block],
        out_specs=pl.BlockSpec((1, 2 * chans, width), lambda d: (d, 0, 0)),
        out_shape=jax.ShapeDtypeStruct((seqs, 2 * chans, width), jnp.bfloat16),
        interpret=interpret,
    )(key_gate, value_input, long_filter)


def body(query_gate, key_gate, value_input, long_filter, out_weight):
    chans, length = key_gate.shape
    seqs = lax.axis_size("seq")
    seq_index = lax.axis_index("seq")
    width = length // seqs
    rows = 2 * seqs
    full = rows * length
    pairs = chans // 2
    f32, bf16 = jnp.float32, jnp.bfloat16

    send = send_blocks(key_gate, value_input, long_filter, seqs)
    got = lax.all_to_all(send, "seq", 0, 0, tiled=True).astype(f32)
    packed_real, packed_imag = got[:, :chans], got[:, chans:]

    row_ids = row_list(seqs)
    cos_a, sin_a = turn_table(row_ids, np.arange(seqs), rows)
    freq_real = major(cos_a, packed_real) + major(sin_a, packed_imag)
    freq_imag = major(cos_a, packed_imag) - major(sin_a, packed_real)
    cos_dev, sin_dev = turn_table(np.arange(seqs) * width, row_ids, full)
    cos_dev = lax.dynamic_index_in_dim(cos_dev, seq_index, 0, keepdims=False)[:, None, None]
    sin_dev = lax.dynamic_index_in_dim(sin_dev, seq_index, 0, keepdims=False)[:, None, None]
    cos_col, sin_col = turn_table(row_ids, np.arange(width), full)
    cos_col, sin_col = cos_col[:, None, :], sin_col[:, None, :]
    cos_t = cos_dev * cos_col - sin_dev * sin_col
    sin_t = sin_dev * cos_col + cos_dev * sin_col
    spread_real = freq_real * cos_t + freq_imag * sin_t
    spread_imag = freq_imag * cos_t - freq_real * sin_t
    spread = jnp.stack([spread_real, spread_imag], axis=1).astype(bf16)
    spread = spread.reshape(seqs, 2, 2, chans, width)
    recv = lax.all_to_all(spread, "seq", 0, 0, tiled=True).astype(f32)
    rows_real, rows_imag = recv[:, :, 0], recv[:, :, 1]

    cos_o, sin_o = turn_table(np.arange(seqs), np.arange(seqs), seqs)
    cos_w, sin_w = turn_table(np.arange(seqs), np.arange(width), length)
    cos_w, sin_w = cos_w[:, None, None, :], sin_w[:, None, None, :]
    cos_i, sin_i = turn_table(np.arange(width), np.arange(width), width)
    first_real = major(cos_o, rows_real) + major(sin_o, rows_imag)
    first_imag = major(cos_o, rows_imag) - major(sin_o, rows_real)
    twist_real = first_real * cos_w + first_imag * sin_w
    twist_imag = first_imag * cos_w - first_real * sin_w
    spec_real = minor(twist_real, cos_i) + minor(twist_imag, sin_i)
    spec_imag = minor(twist_imag, cos_i) - minor(twist_real, sin_i)

    lane_in = lax.broadcasted_iota(jnp.int32, (width, width), 0)
    lane_out = lax.broadcasted_iota(jnp.int32, (width, width), 1)
    lane_flip = (lane_in == width - 1 - lane_out).astype(f32)
    lane_neg = (lane_in == (width - lane_out) % width).astype(f32)
    place = lax.broadcasted_iota(jnp.int32, (rows, rows), 0)
    source = lax.broadcasted_iota(jnp.int32, (rows, rows), 1)
    place_q, place_s = place // 2, place % 2
    cross_src = 2 * (seqs - 1 - place_q) + 1 - place_s
    self_src = jnp.where(place_s == 1, 2 * (seqs - 1 - place_q) + 1, 2 * ((seqs - place_q) % seqs))
    first_dev = seq_index == 0
    regroup = (source == jnp.where(first_dev, self_src, cross_src)).astype(f32)

    def negated(spec):
        flipped = jnp.einsum("...b,bm->...m", spec, lane_flip, precision=HIGHEST)
        moved = jnp.einsum(
            "uv,vcb->ucb", regroup, flipped.reshape(rows, chans, width), precision=HIGHEST
        ).reshape(spec.shape)
        corner = jnp.einsum("cb,bm->cm", spec[0, 0], lane_neg, precision=HIGHEST)
        return moved.at[0, 0].set(jnp.where(first_dev, corner, moved[0, 0]))

    neg_real = negated(spec_real)
    neg_imag = negated(spec_imag)

    a_real = 0.5 * (spec_real + neg_real)
    a_imag = 0.5 * (spec_imag - neg_imag)
    b_real = 0.5 * (spec_imag + neg_imag)
    b_imag = 0.5 * (neg_real - spec_real)
    sig1_r, sig1_i, filt1_r, filt1_i = (
        a_real[:, :, :pairs], a_imag[:, :, :pairs], a_real[:, :, pairs:], a_imag[:, :, pairs:]
    )
    sig2_r, sig2_i, filt2_r, filt2_i = (
        b_real[:, :, :pairs], b_imag[:, :, :pairs], b_real[:, :, pairs:], b_imag[:, :, pairs:]
    )
    prod1_r = sig1_r * filt1_r - sig1_i * filt1_i
    prod1_i = sig1_r * filt1_i + sig1_i * filt1_r
    prod2_r = sig2_r * filt2_r - sig2_i * filt2_i
    prod2_i = sig2_r * filt2_i + sig2_i * filt2_r
    prod_real = prod1_r - prod2_i
    prod_imag = prod1_i + prod2_r

    inv_real = minor(prod_real, cos_i) - minor(prod_imag, sin_i)
    inv_imag = minor(prod_imag, cos_i) + minor(prod_real, sin_i)
    untwist_real = inv_real * cos_w - inv_imag * sin_w
    untwist_imag = inv_imag * cos_w + inv_real * sin_w
    back_real = major(cos_o, untwist_real) - major(sin_o, untwist_imag)
    back_imag = major(cos_o, untwist_imag) + major(sin_o, untwist_real)

    own_rows = slot_rows(seq_index, jnp.arange(2), seqs)
    cos_blk, sin_blk = turn_table(np.arange(rows), np.arange(seqs) * width, full)
    cos_off, sin_off = turn_table(np.arange(rows), np.arange(width), full)
    cos_blk, sin_blk = jnp.take(cos_blk, own_rows, axis=0).T, jnp.take(sin_blk, own_rows, axis=0).T
    cos_off, sin_off = jnp.take(cos_off, own_rows, axis=0), jnp.take(sin_off, own_rows, axis=0)
    cos_b = (cos_blk[:, :, None] * cos_off[None] - sin_blk[:, :, None] * sin_off[None])[:, :, None, :]
    sin_b = (sin_blk[:, :, None] * cos_off[None] + cos_blk[:, :, None] * sin_off[None])[:, :, None, :]
    reverted_real = back_real * cos_b - back_imag * sin_b
    reverted_imag = back_imag * cos_b + back_real * sin_b
    reverted = jnp.stack([reverted_real, reverted_imag], axis=2).astype(bf16)
    moved = lax.all_to_all(reverted, "seq", 0, 0, tiled=True).astype(f32)
    moved = moved.reshape(rows, 2, pairs, width)

    cos_l, sin_l = turn_table(np.arange(seqs), row_ids, rows)
    merged_real = major(cos_l, moved[:, 0]) - major(sin_l, moved[:, 1])
    merged_imag = major(cos_l, moved[:, 1]) + major(sin_l, moved[:, 0])
    merged = jnp.concatenate([merged_real, merged_imag], axis=1) * (1.0 / full)
    arrived = lax.all_to_all(merged.astype(bf16), "seq", 0, 0, tiled=True)
    conv = arrived.astype(f32).transpose(1, 0, 2).reshape(chans, length)
    gated_out = (query_gate.astype(f32) * conv).astype(bf16)

    tp_index = lax.axis_index("tp")
    core = tp_index % 2
    half = tp_index // 2
    tps = lax.axis_size("tp")
    columns = lax.dynamic_slice_in_dim(out_weight, tp_index * chans, chans, 1)
    grouped = columns.reshape(2, 2, chans, chans)
    keep_w = lax.dynamic_index_in_dim(grouped, core, 1, keepdims=False)
    send_w = lax.dynamic_index_in_dim(grouped, 1 - core, 1, keepdims=False)
    send_part = jnp.einsum("hoc,cp->hop", send_w, gated_out, preferred_element_type=f32)
    keep_part = jnp.einsum("hoc,cp->hop", keep_w, gated_out, preferred_element_type=f32)
    pair = [(i, i ^ 1) for i in range(tps)]
    chip_sum = keep_part + lax.ppermute(send_part.astype(bf16), "tp", pair).astype(f32)
    keep_chip = lax.dynamic_index_in_dim(chip_sum, half, 0, keepdims=False)
    send_chip = lax.dynamic_index_in_dim(chip_sum, 1 - half, 0, keepdims=False)
    cross = [(i, i ^ 2) for i in range(tps)]
    total = keep_chip + lax.ppermute(send_chip.astype(bf16), "tp", cross).astype(f32)
    return total.astype(bf16)


def solution(mesh):
    return jax.shard_map(
        body,
        mesh=mesh,
        in_specs=(P("tp", "seq"), P("tp", "seq"), P("tp", "seq"), P("tp", "seq"), P()),
        out_specs=P("tp", "seq"),
        check_vma=False,
    )
```

```python
import math

import jax
import numpy as np
import jax.numpy as jnp
from jax import lax
from jax.experimental import pallas as pl
from jax.sharding import PartitionSpec as P

HIGH = lax.Precision.HIGH
HIGHEST = lax.Precision.HIGHEST


def turn_table(row_ids, col_ids, modulus):
    turns = (np.asarray(row_ids, np.int64)[:, None] * np.asarray(col_ids, np.int64)[None, :]) % modulus
    angles = turns.astype(np.float64) * (2.0 * math.pi / modulus)
    return (jnp.asarray(np.cos(angles), jnp.float32), jnp.asarray(np.sin(angles), jnp.float32))


def row_list(seqs):
    return np.array([d if s == 0 else (seqs if d == 0 else 2 * seqs - d) for d in range(seqs) for s in range(2)])


def slot_rows(device, slot, seqs):
    return jnp.where(slot == 0, device, jnp.where(device == 0, seqs, 2 * seqs - device))


def major(table, data):
    return jnp.einsum("qk,k...->q...", table, data, precision=HIGH)


def minor(data, table):
    return jnp.einsum("...b,bm->...m", data, table, precision=HIGH)


def send_blocks(key_gate, value_input, long_filter, seqs, interpret=False):
    chans, length = key_gate.shape
    width = length // seqs
    pairs = chans // 2

    def kernel(key_ref, value_ref, taps_ref, out_ref):
        for d in range(seqs):
            cols = slice(d * width, (d + 1) * width)
            gated = key_ref[:, cols].astype(jnp.float32) * value_ref[:, cols].astype(jnp.float32)
            gated = gated.astype(jnp.bfloat16)
            taps = taps_ref[:, cols].astype(jnp.bfloat16)
            out_ref[d, 0:pairs] = gated[:pairs]
            out_ref[d, pairs:chans] = taps[:pairs]
            out_ref[d, chans:chans + pairs] = gated[pairs:]
            out_ref[d, chans + pairs:2 * chans] = taps[pairs:]

    return pl.pallas_call(
        kernel,
        out_shape=jax.ShapeDtypeStruct((seqs, 2 * chans, width), jnp.bfloat16),
        interpret=interpret,
    )(key_gate, value_input, long_filter)


def body(query_gate, key_gate, value_input, long_filter, out_weight):
    chans, length = key_gate.shape
    seqs = lax.axis_size("seq")
    seq_index = lax.axis_index("seq")
    width = length // seqs
    rows = 2 * seqs
    full = rows * length
    pairs = chans // 2
    f32, bf16 = jnp.float32, jnp.bfloat16

    send = send_blocks(key_gate, value_input, long_filter, seqs)
    got = lax.all_to_all(send, "seq", 0, 0, tiled=True).astype(f32)
    packed_real, packed_imag = got[:, :chans], got[:, chans:]

    row_ids = row_list(seqs)
    cos_a, sin_a = turn_table(row_ids, np.arange(seqs), rows)
    freq_real = major(cos_a, packed_real) + major(sin_a, packed_imag)
    freq_imag = major(cos_a, packed_imag) - major(sin_a, packed_real)
    cos_dev, sin_dev = turn_table(np.arange(seqs) * width, row_ids, full)
    cos_dev = lax.dynamic_index_in_dim(cos_dev, seq_index, 0, keepdims=False)[:, None, None]
    sin_dev = lax.dynamic_index_in_dim(sin_dev, seq_index, 0, keepdims=False)[:, None, None]
    cos_col, sin_col = turn_table(row_ids, np.arange(width), full)
    cos_col, sin_col = cos_col[:, None, :], sin_col[:, None, :]
    cos_t = cos_dev * cos_col - sin_dev * sin_col
    sin_t = sin_dev * cos_col + cos_dev * sin_col
    spread_real = freq_real * cos_t + freq_imag * sin_t
    spread_imag = freq_imag * cos_t - freq_real * sin_t
    spread = jnp.stack([spread_real, spread_imag], axis=1).astype(bf16)
    spread = spread.reshape(seqs, 2, 2, chans, width)
    recv = lax.all_to_all(spread, "seq", 0, 0, tiled=True).astype(f32)
    rows_real, rows_imag = recv[:, :, 0], recv[:, :, 1]

    cos_o, sin_o = turn_table(np.arange(seqs), np.arange(seqs), seqs)
    cos_w, sin_w = turn_table(np.arange(seqs), np.arange(width), length)
    cos_w, sin_w = cos_w[:, None, None, :], sin_w[:, None, None, :]
    cos_i, sin_i = turn_table(np.arange(width), np.arange(width), width)
    first_real = major(cos_o, rows_real) + major(sin_o, rows_imag)
    first_imag = major(cos_o, rows_imag) - major(sin_o, rows_real)
    twist_real = first_real * cos_w + first_imag * sin_w
    twist_imag = first_imag * cos_w - first_real * sin_w
    spec_real = minor(twist_real, cos_i) + minor(twist_imag, sin_i)
    spec_imag = minor(twist_imag, cos_i) - minor(twist_real, sin_i)

    lane_in = lax.broadcasted_iota(jnp.int32, (width, width), 0)
    lane_out = lax.broadcasted_iota(jnp.int32, (width, width), 1)
    lane_flip = (lane_in == width - 1 - lane_out).astype(f32)
    lane_neg = (lane_in == (width - lane_out) % width).astype(f32)
    place = lax.broadcasted_iota(jnp.int32, (rows, rows), 0)
    source = lax.broadcasted_iota(jnp.int32, (rows, rows), 1)
    place_q, place_s = place // 2, place % 2
    cross_src = 2 * (seqs - 1 - place_q) + 1 - place_s
    self_src = jnp.where(place_s == 1, 2 * (seqs - 1 - place_q) + 1, 2 * ((seqs - place_q) % seqs))
    first_dev = seq_index == 0
    regroup = (source == jnp.where(first_dev, self_src, cross_src)).astype(f32)

    def negated(spec):
        flipped = jnp.einsum("...b,bm->...m", spec, lane_flip, precision=HIGHEST)
        moved = jnp.einsum(
            "uv,vcb->ucb", regroup, flipped.reshape(rows, chans, width), precision=HIGHEST
        ).reshape(spec.shape)
        corner = jnp.einsum("cb,bm->cm", spec[0, 0], lane_neg, precision=HIGHEST)
        return moved.at[0, 0].set(jnp.where(first_dev, corner, moved[0, 0]))

    neg_real = negated(spec_real)
    neg_imag = negated(spec_imag)

    a_real = 0.5 * (spec_real + neg_real)
    a_imag = 0.5 * (spec_imag - neg_imag)
    b_real = 0.5 * (spec_imag + neg_imag)
    b_imag = 0.5 * (neg_real - spec_real)
    sig1_r, sig1_i, filt1_r, filt1_i = (
        a_real[:, :, :pairs], a_imag[:, :, :pairs], a_real[:, :, pairs:], a_imag[:, :, pairs:]
    )
    sig2_r, sig2_i, filt2_r, filt2_i = (
        b_real[:, :, :pairs], b_imag[:, :, :pairs], b_real[:, :, pairs:], b_imag[:, :, pairs:]
    )
    prod1_r = sig1_r * filt1_r - sig1_i * filt1_i
    prod1_i = sig1_r * filt1_i + sig1_i * filt1_r
    prod2_r = sig2_r * filt2_r - sig2_i * filt2_i
    prod2_i = sig2_r * filt2_i + sig2_i * filt2_r
    prod_real = prod1_r - prod2_i
    prod_imag = prod1_i + prod2_r

    inv_real = minor(prod_real, cos_i) - minor(prod_imag, sin_i)
    inv_imag = minor(prod_imag, cos_i) + minor(prod_real, sin_i)
    untwist_real = inv_real * cos_w - inv_imag * sin_w
    untwist_imag = inv_imag * cos_w + inv_real * sin_w
    back_real = major(cos_o, untwist_real) - major(sin_o, untwist_imag)
    back_imag = major(cos_o, untwist_imag) + major(sin_o, untwist_real)

    own_rows = slot_rows(seq_index, jnp.arange(2), seqs)
    cos_blk, sin_blk = turn_table(np.arange(rows), np.arange(seqs) * width, full)
    cos_off, sin_off = turn_table(np.arange(rows), np.arange(width), full)
    cos_blk, sin_blk = jnp.take(cos_blk, own_rows, axis=0).T, jnp.take(sin_blk, own_rows, axis=0).T
    cos_off, sin_off = jnp.take(cos_off, own_rows, axis=0), jnp.take(sin_off, own_rows, axis=0)
    cos_b = (cos_blk[:, :, None] * cos_off[None] - sin_blk[:, :, None] * sin_off[None])[:, :, None, :]
    sin_b = (sin_blk[:, :, None] * cos_off[None] + cos_blk[:, :, None] * sin_off[None])[:, :, None, :]
    reverted_real = back_real * cos_b - back_imag * sin_b
    reverted_imag = back_imag * cos_b + back_real * sin_b
    reverted = jnp.stack([reverted_real, reverted_imag], axis=2).astype(bf16)
    moved = lax.all_to_all(reverted, "seq", 0, 0, tiled=True).astype(f32)
    moved = moved.reshape(rows, 2, pairs, width)

    cos_l, sin_l = turn_table(np.arange(seqs), row_ids, rows)
    merged_real = major(cos_l, moved[:, 0]) - major(sin_l, moved[:, 1])
    merged_imag = major(cos_l, moved[:, 1]) + major(sin_l, moved[:, 0])
    merged = jnp.concatenate([merged_real, merged_imag], axis=1) * (1.0 / full)
    arrived = lax.all_to_all(merged.astype(bf16), "seq", 0, 0, tiled=True)
    conv = arrived.astype(f32).transpose(1, 0, 2).reshape(chans, length)
    gated_out = (query_gate.astype(f32) * conv).astype(bf16)

    tp_index = lax.axis_index("tp")
    core = tp_index % 2
    half = tp_index // 2
    tps = lax.axis_size("tp")
    columns = lax.dynamic_slice_in_dim(out_weight, tp_index * chans, chans, 1)
    grouped = columns.reshape(2, 2, chans, chans)
    keep_w = lax.dynamic_index_in_dim(grouped, core, 1, keepdims=False)
    send_w = lax.dynamic_index_in_dim(grouped, 1 - core, 1, keepdims=False)
    send_part = jnp.einsum("hoc,cp->hop", send_w, gated_out, preferred_element_type=f32)
    keep_part = jnp.einsum("hoc,cp->hop", keep_w, gated_out, preferred_element_type=f32)
    pair = [(i, i ^ 1) for i in range(tps)]
    chip_sum = keep_part + lax.ppermute(send_part.astype(bf16), "tp", pair).astype(f32)
    keep_chip = lax.dynamic_index_in_dim(chip_sum, half, 0, keepdims=False)
    send_chip = lax.dynamic_index_in_dim(chip_sum, 1 - half, 0, keepdims=False)
    cross = [(i, i ^ 2) for i in range(tps)]
    total = keep_chip + lax.ppermute(send_chip.astype(bf16), "tp", cross).astype(f32)
    return total.astype(bf16)


def solution(mesh):
    return jax.shard_map(
        body,
        mesh=mesh,
        in_specs=(P("tp", "seq"), P("tp", "seq"), P("tp", "seq"), P("tp", "seq"), P()),
        out_specs=P("tp", "seq"),
        check_vma=False,
    )
```

```python
import math

import jax
import numpy as np
import jax.numpy as jnp
from jax import lax
from jax.experimental import pallas as pl
from jax.sharding import PartitionSpec as P

HIGH = lax.Precision.HIGH


def turn_table(row_ids, col_ids, modulus):
    turns = (np.asarray(row_ids, np.int64)[:, None] * np.asarray(col_ids, np.int64)[None, :]) % modulus
    angles = turns.astype(np.float64) * (2.0 * math.pi / modulus)
    return (jnp.asarray(np.cos(angles), jnp.float32), jnp.asarray(np.sin(angles), jnp.float32))


def row_list(seqs):
    return np.array([d if s == 0 else (seqs if d == 0 else 2 * seqs - d) for d in range(seqs) for s in range(2)])


def slot_rows(device, slot, seqs):
    return jnp.where(slot == 0, device, jnp.where(device == 0, seqs, 2 * seqs - device))


def major(table, data):
    return jnp.einsum("qk,k...->q...", table, data, precision=HIGH)


def minor(data, table):
    return jnp.einsum("...b,bm->...m", data, table, precision=HIGH)


def send_blocks(key_gate, value_input, long_filter, seqs, interpret=False):
    chans, length = key_gate.shape
    width = length // seqs
    pairs = chans // 2

    def kernel(key_ref, value_ref, taps_ref, out_ref):
        for d in range(seqs):
            cols = slice(d * width, (d + 1) * width)
            gated = key_ref[:, cols].astype(jnp.float32) * value_ref[:, cols].astype(jnp.float32)
            gated = gated.astype(jnp.bfloat16)
            taps = taps_ref[:, cols].astype(jnp.bfloat16)
            out_ref[d, 0:pairs] = gated[:pairs]
            out_ref[d, pairs:chans] = taps[:pairs]
            out_ref[d, chans:chans + pairs] = gated[pairs:]
            out_ref[d, chans + pairs:2 * chans] = taps[pairs:]

    return pl.pallas_call(
        kernel,
        out_shape=jax.ShapeDtypeStruct((seqs, 2 * chans, width), jnp.bfloat16),
        interpret=interpret,
    )(key_gate, value_input, long_filter)


def body(query_gate, key_gate, value_input, long_filter, out_weight):
    chans, length = key_gate.shape
    seqs = lax.axis_size("seq")
    seq_index = lax.axis_index("seq")
    width = length // seqs
    rows = 2 * seqs
    full = rows * length
    pairs = chans // 2
    f32, bf16 = jnp.float32, jnp.bfloat16

    send = send_blocks(key_gate, value_input, long_filter, seqs)
    got = lax.all_to_all(send, "seq", 0, 0, tiled=True).astype(f32)
    packed_real, packed_imag = got[:, :chans], got[:, chans:]

    row_ids = row_list(seqs)
    cos_a, sin_a = turn_table(row_ids, np.arange(seqs), rows)
    freq_real = major(cos_a, packed_real) + major(sin_a, packed_imag)
    freq_imag = major(cos_a, packed_imag) - major(sin_a, packed_real)
    cos_dev, sin_dev = turn_table(np.arange(seqs) * width, row_ids, full)
    cos_dev = lax.dynamic_index_in_dim(cos_dev, seq_index, 0, keepdims=False)[:, None, None]
    sin_dev = lax.dynamic_index_in_dim(sin_dev, seq_index, 0, keepdims=False)[:, None, None]
    cos_col, sin_col = turn_table(row_ids, np.arange(width), full)
    cos_col, sin_col = cos_col[:, None, :], sin_col[:, None, :]
    cos_t = cos_dev * cos_col - sin_dev * sin_col
    sin_t = sin_dev * cos_col + cos_dev * sin_col
    spread_real = freq_real * cos_t + freq_imag * sin_t
    spread_imag = freq_imag * cos_t - freq_real * sin_t
    spread = jnp.stack([spread_real, spread_imag], axis=1).astype(bf16)
    spread = spread.reshape(seqs, 2, 2, chans, width)
    recv = lax.all_to_all(spread, "seq", 0, 0, tiled=True).astype(f32)
    rows_real, rows_imag = recv[:, :, 0], recv[:, :, 1]

    cos_o, sin_o = turn_table(np.arange(seqs), np.arange(seqs), seqs)
    cos_w, sin_w = turn_table(np.arange(seqs), np.arange(width), length)
    cos_w, sin_w = cos_w[:, None, None, :], sin_w[:, None, None, :]
    cos_i, sin_i = turn_table(np.arange(width), np.arange(width), width)
    first_real = major(cos_o, rows_real) + major(sin_o, rows_imag)
    first_imag = major(cos_o, rows_imag) - major(sin_o, rows_real)
    twist_real = first_real * cos_w + first_imag * sin_w
    twist_imag = first_imag * cos_w - first_real * sin_w
    spec_real = minor(twist_real, cos_i) + minor(twist_imag, sin_i)
    spec_imag = minor(twist_imag, cos_i) - minor(twist_real, sin_i)

    lane_in = lax.broadcasted_iota(jnp.int32, (width, width), 0)
    lane_out = lax.broadcasted_iota(jnp.int32, (width, width), 1)
    lane_flip = (lane_in == width - 1 - lane_out).astype(f32)
    lane_neg = (lane_in == (width - lane_out) % width).astype(f32)
    place = lax.broadcasted_iota(jnp.int32, (rows, rows), 0)
    source = lax.broadcasted_iota(jnp.int32, (rows, rows), 1)
    place_q, place_s = place // 2, place % 2
    cross_src = 2 * (seqs - 1 - place_q) + 1 - place_s
    self_src = jnp.where(place_s == 1, 2 * (seqs - 1 - place_q) + 1, 2 * ((seqs - place_q) % seqs))
    first_dev = seq_index == 0
    regroup = (source == jnp.where(first_dev, self_src, cross_src)).astype(f32)

    def negated(spec):
        flipped = jnp.einsum("...b,bm->...m", spec, lane_flip, precision=HIGH)
        moved = jnp.einsum(
            "uv,vcb->ucb", regroup, flipped.reshape(rows, chans, width), precision=HIGH
        ).reshape(spec.shape)
        corner = jnp.einsum("cb,bm->cm", spec[0, 0], lane_neg, precision=HIGH)
        return moved.at[0, 0].set(jnp.where(first_dev, corner, moved[0, 0]))

    neg_real = negated(spec_real)
    neg_imag = negated(spec_imag)

    a_real = 0.5 * (spec_real + neg_real)
    a_imag = 0.5 * (spec_imag - neg_imag)
    b_real = 0.5 * (spec_imag + neg_imag)
    b_imag = 0.5 * (neg_real - spec_real)
    sig1_r, sig1_i, filt1_r, filt1_i = (
        a_real[:, :, :pairs], a_imag[:, :, :pairs], a_real[:, :, pairs:], a_imag[:, :, pairs:]
    )
    sig2_r, sig2_i, filt2_r, filt2_i = (
        b_real[:, :, :pairs], b_imag[:, :, :pairs], b_real[:, :, pairs:], b_imag[:, :, pairs:]
    )
    prod1_r = sig1_r * filt1_r - sig1_i * filt1_i
    prod1_i = sig1_r * filt1_i + sig1_i * filt1_r
    prod2_r = sig2_r * filt2_r - sig2_i * filt2_i
    prod2_i = sig2_r * filt2_i + sig2_i * filt2_r
    prod_real = prod1_r - prod2_i
    prod_imag = prod1_i + prod2_r

    inv_real = minor(prod_real, cos_i) - minor(prod_imag, sin_i)
    inv_imag = minor(prod_imag, cos_i) + minor(prod_real, sin_i)
    untwist_real = inv_real * cos_w - inv_imag * sin_w
    untwist_imag = inv_imag * cos_w + inv_real * sin_w
    back_real = major(cos_o, untwist_real) - major(sin_o, untwist_imag)
    back_imag = major(cos_o, untwist_imag) + major(sin_o, untwist_real)

    own_rows = slot_rows(seq_index, jnp.arange(2), seqs)
    cos_blk, sin_blk = turn_table(np.arange(rows), np.arange(seqs) * width, full)
    cos_off, sin_off = turn_table(np.arange(rows), np.arange(width), full)
    cos_blk, sin_blk = jnp.take(cos_blk, own_rows, axis=0).T, jnp.take(sin_blk, own_rows, axis=0).T
    cos_off, sin_off = jnp.take(cos_off, own_rows, axis=0), jnp.take(sin_off, own_rows, axis=0)
    cos_b = (cos_blk[:, :, None] * cos_off[None] - sin_blk[:, :, None] * sin_off[None])[:, :, None, :]
    sin_b = (sin_blk[:, :, None] * cos_off[None] + cos_blk[:, :, None] * sin_off[None])[:, :, None, :]
    reverted_real = back_real * cos_b - back_imag * sin_b
    reverted_imag = back_imag * cos_b + back_real * sin_b
    reverted = jnp.stack([reverted_real, reverted_imag], axis=2).astype(bf16)
    moved = lax.all_to_all(reverted, "seq", 0, 0, tiled=True).astype(f32)
    moved = moved.reshape(rows, 2, pairs, width)

    cos_l, sin_l = turn_table(np.arange(seqs), row_ids, rows)
    merged_real = major(cos_l, moved[:, 0]) - major(sin_l, moved[:, 1])
    merged_imag = major(cos_l, moved[:, 1]) + major(sin_l, moved[:, 0])
    merged = jnp.concatenate([merged_real, merged_imag], axis=1) * (1.0 / full)
    arrived = lax.all_to_all(merged.astype(bf16), "seq", 0, 0, tiled=True)
    conv = arrived.astype(f32).transpose(1, 0, 2).reshape(chans, length)
    gated_out = (query_gate.astype(f32) * conv).astype(bf16)

    tp_index = lax.axis_index("tp")
    core = tp_index % 2
    half = tp_index // 2
    tps = lax.axis_size("tp")
    columns = lax.dynamic_slice_in_dim(out_weight, tp_index * chans, chans, 1)
    grouped = columns.reshape(2, 2, chans, chans)
    keep_w = lax.dynamic_index_in_dim(grouped, core, 1, keepdims=False)
    send_w = lax.dynamic_index_in_dim(grouped, 1 - core, 1, keepdims=False)
    send_part = jnp.einsum("hoc,cp->hop", send_w, gated_out, preferred_element_type=f32)
    keep_part = jnp.einsum("hoc,cp->hop", keep_w, gated_out, preferred_element_type=f32)
    pair = [(i, i ^ 1) for i in range(tps)]
    chip_sum = keep_part + lax.ppermute(send_part.astype(bf16), "tp", pair).astype(f32)
    keep_chip = lax.dynamic_index_in_dim(chip_sum, half, 0, keepdims=False)
    send_chip = lax.dynamic_index_in_dim(chip_sum, 1 - half, 0, keepdims=False)
    cross = [(i, i ^ 2) for i in range(tps)]
    total = keep_chip + lax.ppermute(send_chip.astype(bf16), "tp", cross).astype(f32)
    return total.astype(bf16)


def solution(mesh):
    return jax.shard_map(
        body,
        mesh=mesh,
        in_specs=(P("tp", "seq"), P("tp", "seq"), P("tp", "seq"), P("tp", "seq"), P()),
        out_specs=P("tp", "seq"),
        check_vma=False,
    )
```

```python
import math

import jax
import numpy as np
import jax.numpy as jnp
from jax import lax
from jax.experimental import pallas as pl
from jax.sharding import PartitionSpec as P

HIGH = lax.Precision.HIGH


def turn_table(row_ids, col_ids, modulus):
    turns = (np.asarray(row_ids, np.int64)[:, None] * np.asarray(col_ids, np.int64)[None, :]) % modulus
    angles = turns.astype(np.float64) * (2.0 * math.pi / modulus)
    return (jnp.asarray(np.cos(angles), jnp.float32), jnp.asarray(np.sin(angles), jnp.float32))


def row_list(seqs):
    return np.array([d if s == 0 else (seqs if d == 0 else 2 * seqs - d) for d in range(seqs) for s in range(2)])


def slot_rows(device, slot, seqs):
    return jnp.where(slot == 0, device, jnp.where(device == 0, seqs, 2 * seqs - device))


def major(table, data):
    return jnp.einsum("qk,k...->q...", table, data, precision=HIGH)


def minor(data, table):
    return jnp.einsum("...b,bm->...m", data, table, precision=HIGH)


def send_blocks(key_gate, value_input, long_filter, seqs, interpret=False):
    chans, length = key_gate.shape
    width = length // seqs
    pairs = chans // 2

    def kernel(key_ref, value_ref, taps_ref, out_ref):
        for d in range(seqs):
            cols = slice(d * width, (d + 1) * width)
            gated = key_ref[:, cols].astype(jnp.float32) * value_ref[:, cols].astype(jnp.float32)
            gated = gated.astype(jnp.bfloat16)
            taps = taps_ref[:, cols].astype(jnp.bfloat16)
            out_ref[d, 0:pairs] = gated[:pairs]
            out_ref[d, pairs:chans] = taps[:pairs]
            out_ref[d, chans:chans + pairs] = gated[pairs:]
            out_ref[d, chans + pairs:2 * chans] = taps[pairs:]

    return pl.pallas_call(
        kernel,
        out_shape=jax.ShapeDtypeStruct((seqs, 2 * chans, width), jnp.bfloat16),
        interpret=interpret,
    )(key_gate, value_input, long_filter)


def body(query_gate, key_gate, value_input, long_filter, out_weight):
    chans, length = key_gate.shape
    seqs = lax.axis_size("seq")
    seq_index = lax.axis_index("seq")
    width = length // seqs
    rows = 2 * seqs
    full = rows * length
    pairs = chans // 2
    f32, bf16 = jnp.float32, jnp.bfloat16

    send = send_blocks(key_gate, value_input, long_filter, seqs)
    got = lax.all_to_all(send, "seq", 0, 0, tiled=True).astype(f32)
    packed_real, packed_imag = got[:, :chans], got[:, chans:]

    row_ids = row_list(seqs)
    cos_a, sin_a = turn_table(row_ids, np.arange(seqs), rows)
    freq_real = major(cos_a, packed_real) + major(sin_a, packed_imag)
    freq_imag = major(cos_a, packed_imag) - major(sin_a, packed_real)
    cos_dev, sin_dev = turn_table(np.arange(seqs) * width, row_ids, full)
    cos_dev = lax.dynamic_index_in_dim(cos_dev, seq_index, 0, keepdims=False)[:, None, None]
    sin_dev = lax.dynamic_index_in_dim(sin_dev, seq_index, 0, keepdims=False)[:, None, None]
    cos_col, sin_col = turn_table(row_ids, np.arange(width), full)
    cos_col, sin_col = cos_col[:, None, :], sin_col[:, None, :]
    cos_t = cos_dev * cos_col - sin_dev * sin_col
    sin_t = sin_dev * cos_col + cos_dev * sin_col
    spread_real = freq_real * cos_t + freq_imag * sin_t
    spread_imag = freq_imag * cos_t - freq_real * sin_t
    spread = jnp.stack([spread_real, spread_imag], axis=1).astype(bf16)
    spread = spread.reshape(seqs, 2, 2, chans, width)
    recv = lax.all_to_all(spread, "seq", 0, 0, tiled=True).astype(f32)
    rows_real, rows_imag = recv[:, :, 0], recv[:, :, 1]

    cos_o, sin_o = turn_table(np.arange(seqs), np.arange(seqs), seqs)
    cos_w, sin_w = turn_table(np.arange(seqs), np.arange(width), length)
    cos_w, sin_w = cos_w[:, None, None, :], sin_w[:, None, None, :]
    cos_i, sin_i = turn_table(np.arange(width), np.arange(width), width)
    first_real = major(cos_o, rows_real) + major(sin_o, rows_imag)
    first_imag = major(cos_o, rows_imag) - major(sin_o, rows_real)
    twist_real = first_real * cos_w + first_imag * sin_w
    twist_imag = first_imag * cos_w - first_real * sin_w
    cos_ext = jnp.concatenate([cos_i, cos_i[:, ::-1]], axis=1)
    sin_ext = jnp.concatenate([sin_i, sin_i[:, ::-1]], axis=1)
    ext_real = minor(twist_real, cos_ext) + minor(twist_imag, sin_ext)
    ext_imag = minor(twist_imag, cos_ext) - minor(twist_real, sin_ext)
    spec_real, spec_imag = ext_real[..., :width], ext_imag[..., :width]

    lane_in = lax.broadcasted_iota(jnp.int32, (width, width), 0)
    lane_out = lax.broadcasted_iota(jnp.int32, (width, width), 1)
    lane_neg = (lane_in == (width - lane_out) % width).astype(f32)
    place = lax.broadcasted_iota(jnp.int32, (rows, rows), 0)
    source = lax.broadcasted_iota(jnp.int32, (rows, rows), 1)
    place_q, place_s = place // 2, place % 2
    cross_src = 2 * (seqs - 1 - place_q) + 1 - place_s
    self_src = jnp.where(place_s == 1, 2 * (seqs - 1 - place_q) + 1, 2 * ((seqs - place_q) % seqs))
    first_dev = seq_index == 0
    regroup = (source == jnp.where(first_dev, self_src, cross_src)).astype(f32)

    def negated(spec, flipped):
        moved = jnp.einsum(
            "uv,vcb->ucb", regroup, flipped.reshape(rows, chans, width), precision=HIGH
        ).reshape(spec.shape)
        corner = jnp.einsum("cb,bm->cm", spec[0, 0], lane_neg, precision=HIGH)
        return moved.at[0, 0].set(jnp.where(first_dev, corner, moved[0, 0]))

    neg_real = negated(spec_real, ext_real[..., width:])
    neg_imag = negated(spec_imag, ext_imag[..., width:])

    a_real = 0.5 * (spec_real + neg_real)
    a_imag = 0.5 * (spec_imag - neg_imag)
    b_real = 0.5 * (spec_imag + neg_imag)
    b_imag = 0.5 * (neg_real - spec_real)
    sig1_r, sig1_i, filt1_r, filt1_i = (
        a_real[:, :, :pairs], a_imag[:, :, :pairs], a_real[:, :, pairs:], a_imag[:, :, pairs:]
    )
    sig2_r, sig2_i, filt2_r, filt2_i = (
        b_real[:, :, :pairs], b_imag[:, :, :pairs], b_real[:, :, pairs:], b_imag[:, :, pairs:]
    )
    prod1_r = sig1_r * filt1_r - sig1_i * filt1_i
    prod1_i = sig1_r * filt1_i + sig1_i * filt1_r
    prod2_r = sig2_r * filt2_r - sig2_i * filt2_i
    prod2_i = sig2_r * filt2_i + sig2_i * filt2_r
    prod_real = prod1_r - prod2_i
    prod_imag = prod1_i + prod2_r

    inv_real = minor(prod_real, cos_i) - minor(prod_imag, sin_i)
    inv_imag = minor(prod_imag, cos_i) + minor(prod_real, sin_i)
    untwist_real = inv_real * cos_w - inv_imag * sin_w
    untwist_imag = inv_imag * cos_w + inv_real * sin_w
    back_real = major(cos_o, untwist_real) - major(sin_o, untwist_imag)
    back_imag = major(cos_o, untwist_imag) + major(sin_o, untwist_real)

    own_rows = slot_rows(seq_index, jnp.arange(2), seqs)
    cos_blk, sin_blk = turn_table(np.arange(rows), np.arange(seqs) * width, full)
    cos_off, sin_off = turn_table(np.arange(rows), np.arange(width), full)
    cos_blk, sin_blk = jnp.take(cos_blk, own_rows, axis=0).T, jnp.take(sin_blk, own_rows, axis=0).T
    cos_off, sin_off = jnp.take(cos_off, own_rows, axis=0), jnp.take(sin_off, own_rows, axis=0)
    cos_b = (cos_blk[:, :, None] * cos_off[None] - sin_blk[:, :, None] * sin_off[None])[:, :, None, :]
    sin_b = (sin_blk[:, :, None] * cos_off[None] + cos_blk[:, :, None] * sin_off[None])[:, :, None, :]
    reverted_real = back_real * cos_b - back_imag * sin_b
    reverted_imag = back_imag * cos_b + back_real * sin_b
    reverted = jnp.stack([reverted_real, reverted_imag], axis=2).astype(bf16)
    moved = lax.all_to_all(reverted, "seq", 0, 0, tiled=True).astype(f32)
    moved = moved.reshape(rows, 2, pairs, width)

    cos_l, sin_l = turn_table(np.arange(seqs), row_ids, rows)
    merged_real = major(cos_l, moved[:, 0]) - major(sin_l, moved[:, 1])
    merged_imag = major(cos_l, moved[:, 1]) + major(sin_l, moved[:, 0])
    merged = jnp.concatenate([merged_real, merged_imag], axis=1) * (1.0 / full)
    arrived = lax.all_to_all(merged.astype(bf16), "seq", 0, 0, tiled=True)
    conv = arrived.astype(f32).transpose(1, 0, 2).reshape(chans, length)
    gated_out = (query_gate.astype(f32) * conv).astype(bf16)

    tp_index = lax.axis_index("tp")
    core = tp_index % 2
    half = tp_index // 2
    tps = lax.axis_size("tp")
    columns = lax.dynamic_slice_in_dim(out_weight, tp_index * chans, chans, 1)
    grouped = columns.reshape(2, 2, chans, chans)
    keep_w = lax.dynamic_index_in_dim(grouped, core, 1, keepdims=False)
    send_w = lax.dynamic_index_in_dim(grouped, 1 - core, 1, keepdims=False)
    send_part = jnp.einsum("hoc,cp->hop", send_w, gated_out, preferred_element_type=f32)
    keep_part = jnp.einsum("hoc,cp->hop", keep_w, gated_out, preferred_element_type=f32)
    pair = [(i, i ^ 1) for i in range(tps)]
    chip_sum = keep_part + lax.ppermute(send_part.astype(bf16), "tp", pair).astype(f32)
    keep_chip = lax.dynamic_index_in_dim(chip_sum, half, 0, keepdims=False)
    send_chip = lax.dynamic_index_in_dim(chip_sum, 1 - half, 0, keepdims=False)
    cross = [(i, i ^ 2) for i in range(tps)]
    total = keep_chip + lax.ppermute(send_chip.astype(bf16), "tp", cross).astype(f32)
    return total.astype(bf16)


def solution(mesh):
    return jax.shard_map(
        body,
        mesh=mesh,
        in_specs=(P("tp", "seq"), P("tp", "seq"), P("tp", "seq"), P("tp", "seq"), P()),
        out_specs=P("tp", "seq"),
        check_vma=False,
    )
```

```python
import math

import jax
import numpy as np
import jax.numpy as jnp
from jax import lax
from jax.experimental import pallas as pl
from jax.sharding import PartitionSpec as P

HIGH = lax.Precision.HIGH


def turn_table(row_ids, col_ids, modulus):
    turns = (np.asarray(row_ids, np.int64)[:, None] * np.asarray(col_ids, np.int64)[None, :]) % modulus
    angles = turns.astype(np.float64) * (2.0 * math.pi / modulus)
    return (jnp.asarray(np.cos(angles), jnp.float32), jnp.asarray(np.sin(angles), jnp.float32))


def row_list(seqs):
    return np.array([d if s == 0 else (seqs if d == 0 else 2 * seqs - d) for d in range(seqs) for s in range(2)])


def slot_rows(device, slot, seqs):
    return jnp.where(slot == 0, device, jnp.where(device == 0, seqs, 2 * seqs - device))


def major(table, data):
    return jnp.einsum("qk,k...->q...", table, data, precision=HIGH)


def minor(data, table):
    return jnp.einsum("...b,bm->...m", data, table, precision=HIGH)


def send_blocks(key_gate, value_input, long_filter, seqs, interpret=False):
    chans, length = key_gate.shape
    width = length // seqs
    pairs = chans // 2

    def kernel(key_ref, value_ref, taps_ref, out_ref):
        for d in range(seqs):
            cols = slice(d * width, (d + 1) * width)
            gated = key_ref[:, cols].astype(jnp.float32) * value_ref[:, cols].astype(jnp.float32)
            gated = gated.astype(jnp.bfloat16)
            taps = taps_ref[:, cols].astype(jnp.bfloat16)
            out_ref[d, 0:pairs] = gated[:pairs]
            out_ref[d, pairs:chans] = taps[:pairs]
            out_ref[d, chans:chans + pairs] = gated[pairs:]
            out_ref[d, chans + pairs:2 * chans] = taps[pairs:]

    return pl.pallas_call(
        kernel,
        out_shape=jax.ShapeDtypeStruct((seqs, 2 * chans, width), jnp.bfloat16),
        interpret=interpret,
    )(key_gate, value_input, long_filter)


def body(query_gate, key_gate, value_input, long_filter, out_weight):
    chans, length = key_gate.shape
    seqs = lax.axis_size("seq")
    seq_index = lax.axis_index("seq")
    width = length // seqs
    rows = 2 * seqs
    full = rows * length
    pairs = chans // 2
    f32, bf16 = jnp.float32, jnp.bfloat16

    send = send_blocks(key_gate, value_input, long_filter, seqs)
    got = lax.all_to_all(send, "seq", 0, 0, tiled=True).astype(f32)
    packed_real, packed_imag = got[:, :chans], got[:, chans:]

    row_ids = row_list(seqs)
    cos_a, sin_a = turn_table(row_ids, np.arange(seqs), rows)
    freq_real = major(cos_a, packed_real) + major(sin_a, packed_imag)
    freq_imag = major(cos_a, packed_imag) - major(sin_a, packed_real)
    cos_dev, sin_dev = turn_table(np.arange(seqs) * width, row_ids, full)
    cos_dev = lax.dynamic_index_in_dim(cos_dev, seq_index, 0, keepdims=False)[:, None, None]
    sin_dev = lax.dynamic_index_in_dim(sin_dev, seq_index, 0, keepdims=False)[:, None, None]
    cos_col, sin_col = turn_table(row_ids, np.arange(width), full)
    cos_col, sin_col = cos_col[:, None, :], sin_col[:, None, :]
    cos_t = cos_dev * cos_col - sin_dev * sin_col
    sin_t = sin_dev * cos_col + cos_dev * sin_col
    spread_real = freq_real * cos_t + freq_imag * sin_t
    spread_imag = freq_imag * cos_t - freq_real * sin_t
    spread = jnp.stack([spread_real, spread_imag], axis=1).astype(bf16)
    spread = spread.reshape(seqs, 2, 2, chans, width)
    recv = lax.all_to_all(spread, "seq", 0, 0, tiled=True).astype(f32)
    rows_real, rows_imag = recv[:, :, 0], recv[:, :, 1]

    cos_o, sin_o = turn_table(np.arange(seqs), np.arange(seqs), seqs)
    cos_w, sin_w = turn_table(np.arange(seqs), np.arange(width), length)
    cos_w, sin_w = cos_w[:, None, None, :], sin_w[:, None, None, :]
    cos_i, sin_i = turn_table(np.arange(width), np.arange(width), width)
    first_real = major(cos_o, rows_real) + major(sin_o, rows_imag)
    first_imag = major(cos_o, rows_imag) - major(sin_o, rows_real)
    twist_real = first_real * cos_w + first_imag * sin_w
    twist_imag = first_imag * cos_w - first_real * sin_w
    spec_real = minor(twist_real, cos_i) + minor(twist_imag, sin_i)
    spec_imag = minor(twist_imag, cos_i) - minor(twist_real, sin_i)

    lane_in = lax.broadcasted_iota(jnp.int32, (width, width), 0)
    lane_out = lax.broadcasted_iota(jnp.int32, (width, width), 1)
    lane_flip = (lane_in == width - 1 - lane_out).astype(f32)
    lane_neg = (lane_in == (width - lane_out) % width).astype(f32)
    place = lax.broadcasted_iota(jnp.int32, (rows, rows), 0)
    source = lax.broadcasted_iota(jnp.int32, (rows, rows), 1)
    place_q, place_s = place // 2, place % 2
    cross_src = 2 * (seqs - 1 - place_q) + 1 - place_s
    self_src = jnp.where(place_s == 1, 2 * (seqs - 1 - place_q) + 1, 2 * ((seqs - place_q) % seqs))
    first_dev = seq_index == 0
    regroup = (source == jnp.where(first_dev, self_src, cross_src)).astype(f32)

    def negated(spec):
        flipped = jnp.einsum("...b,bm->...m", spec, lane_flip, precision=HIGH)
        moved = jnp.einsum(
            "uv,vcb->ucb", regroup, flipped.reshape(rows, chans, width), precision=HIGH
        ).reshape(spec.shape)
        corner = jnp.einsum("cb,bm->cm", spec[0, 0], lane_neg, precision=HIGH)
        return moved.at[0, 0].set(jnp.where(first_dev, corner, moved[0, 0]))

    neg_real = negated(spec_real)
    neg_imag = negated(spec_imag)

    a_real = 0.5 * (spec_real + neg_real)
    a_imag = 0.5 * (spec_imag - neg_imag)
    b_real = 0.5 * (spec_imag + neg_imag)
    b_imag = 0.5 * (neg_real - spec_real)
    sig1_r, sig1_i, filt1_r, filt1_i = (
        a_real[:, :, :pairs], a_imag[:, :, :pairs], a_real[:, :, pairs:], a_imag[:, :, pairs:]
    )
    sig2_r, sig2_i, filt2_r, filt2_i = (
        b_real[:, :, :pairs], b_imag[:, :, :pairs], b_real[:, :, pairs:], b_imag[:, :, pairs:]
    )
    prod1_r = sig1_r * filt1_r - sig1_i * filt1_i
    prod1_i = sig1_r * filt1_i + sig1_i * filt1_r
    prod2_r = sig2_r * filt2_r - sig2_i * filt2_i
    prod2_i = sig2_r * filt2_i + sig2_i * filt2_r
    prod_real = prod1_r - prod2_i
    prod_imag = prod1_i + prod2_r

    inv_real = minor(prod_real, cos_i) - minor(prod_imag, sin_i)
    inv_imag = minor(prod_imag, cos_i) + minor(prod_real, sin_i)
    untwist_real = inv_real * cos_w - inv_imag * sin_w
    untwist_imag = inv_imag * cos_w + inv_real * sin_w
    back_real = major(cos_o, untwist_real) - major(sin_o, untwist_imag)
    back_imag = major(cos_o, untwist_imag) + major(sin_o, untwist_real)

    own_rows = slot_rows(seq_index, jnp.arange(2), seqs)
    cos_blk, sin_blk = turn_table(np.arange(rows), np.arange(seqs) * width, full)
    cos_off, sin_off = turn_table(np.arange(rows), np.arange(width), full)
    cos_blk, sin_blk = jnp.take(cos_blk, own_rows, axis=0).T, jnp.take(sin_blk, own_rows, axis=0).T
    cos_off, sin_off = jnp.take(cos_off, own_rows, axis=0), jnp.take(sin_off, own_rows, axis=0)
    cos_b = (cos_blk[:, :, None] * cos_off[None] - sin_blk[:, :, None] * sin_off[None])[:, :, None, :]
    sin_b = (sin_blk[:, :, None] * cos_off[None] + cos_blk[:, :, None] * sin_off[None])[:, :, None, :]
    reverted_real = back_real * cos_b - back_imag * sin_b
    reverted_imag = back_imag * cos_b + back_real * sin_b
    reverted = jnp.stack([reverted_real, reverted_imag], axis=2).astype(bf16)
    moved = lax.all_to_all(reverted, "seq", 0, 0, tiled=True).astype(f32)
    moved = moved.reshape(rows, 2, pairs, width)

    cos_l, sin_l = turn_table(np.arange(seqs), row_ids, rows)
    merged_real = major(cos_l, moved[:, 0]) - major(sin_l, moved[:, 1])
    merged_imag = major(cos_l, moved[:, 1]) + major(sin_l, moved[:, 0])
    merged = jnp.concatenate([merged_real, merged_imag], axis=1) * (1.0 / full)
    arrived = lax.all_to_all(merged.astype(bf16), "seq", 0, 0, tiled=True)
    conv = arrived.astype(f32).transpose(1, 0, 2).reshape(chans, length)
    gated_out = (query_gate.astype(f32) * conv).astype(bf16)

    tp_index = lax.axis_index("tp")
    tps = lax.axis_size("tp")
    other_chip = tp_index ^ 2
    other_core = tp_index ^ 1
    cross = [(i, i ^ 2) for i in range(tps)]
    gated_far = lax.ppermute(gated_out, "tp", cross)

    def weights(rows_of, cols_of):
        return lax.dynamic_slice(out_weight, (rows_of * chans, cols_of * chans), (chans, chans))

    def partial(rows_of):
        near = jnp.dot(weights(rows_of, tp_index), gated_out, preferred_element_type=f32)
        far = jnp.dot(weights(rows_of, other_chip), gated_far, preferred_element_type=f32)
        return near + far

    pair = [(i, i ^ 1) for i in range(tps)]
    send_part = partial(other_core)
    keep_part = partial(tp_index)
    total = keep_part + lax.ppermute(send_part.astype(bf16), "tp", pair).astype(f32)
    return total.astype(bf16)


def solution(mesh):
    return jax.shard_map(
        body,
        mesh=mesh,
        in_specs=(P("tp", "seq"), P("tp", "seq"), P("tp", "seq"), P("tp", "seq"), P()),
        out_specs=P("tp", "seq"),
        check_vma=False,
    )
```

```python
import math

import jax
import numpy as np
import jax.numpy as jnp
from jax import lax
from jax.experimental import pallas as pl
from jax.sharding import PartitionSpec as P

HIGH = lax.Precision.HIGH


def turn_table(row_ids, col_ids, modulus):
    turns = (np.asarray(row_ids, np.int64)[:, None] * np.asarray(col_ids, np.int64)[None, :]) % modulus
    angles = turns.astype(np.float64) * (2.0 * math.pi / modulus)
    return (jnp.asarray(np.cos(angles), jnp.float32), jnp.asarray(np.sin(angles), jnp.float32))


def row_list(seqs):
    return np.array([d if s == 0 else (seqs if d == 0 else 2 * seqs - d) for d in range(seqs) for s in range(2)])


def slot_rows(device, slot, seqs):
    return jnp.where(slot == 0, device, jnp.where(device == 0, seqs, 2 * seqs - device))


def major(table, data):
    return jnp.einsum("qk,k...->q...", table, data, precision=HIGH)


def minor(data, table):
    return jnp.einsum("...b,bm->...m", data, table, precision=HIGH)


def send_blocks(key_gate, value_input, long_filter, seqs, interpret=False):
    chans, length = key_gate.shape
    width = length // seqs
    pairs = chans // 2

    def kernel(key_ref, value_ref, taps_ref, out_ref):
        for d in range(seqs):
            cols = slice(d * width, (d + 1) * width)
            gated = key_ref[:, cols].astype(jnp.float32) * value_ref[:, cols].astype(jnp.float32)
            gated = gated.astype(jnp.bfloat16)
            taps = taps_ref[:, cols].astype(jnp.bfloat16)
            out_ref[d, 0:pairs] = gated[:pairs]
            out_ref[d, pairs:chans] = taps[:pairs]
            out_ref[d, chans:chans + pairs] = gated[pairs:]
            out_ref[d, chans + pairs:2 * chans] = taps[pairs:]

    return pl.pallas_call(
        kernel,
        out_shape=jax.ShapeDtypeStruct((seqs, 2 * chans, width), jnp.bfloat16),
        interpret=interpret,
    )(key_gate, value_input, long_filter)


def body(query_gate, key_gate, value_input, long_filter, out_weight):
    chans, length = key_gate.shape
    seqs = lax.axis_size("seq")
    seq_index = lax.axis_index("seq")
    width = length // seqs
    rows = 2 * seqs
    full = rows * length
    pairs = chans // 2
    f32, bf16 = jnp.float32, jnp.bfloat16

    send = send_blocks(key_gate, value_input, long_filter, seqs)
    got = lax.all_to_all(send, "seq", 0, 0, tiled=True).astype(f32)
    packed_real, packed_imag = got[:, :chans], got[:, chans:]

    row_ids = row_list(seqs)
    cos_a, sin_a = turn_table(row_ids, np.arange(seqs), rows)
    freq_real = major(cos_a, packed_real) + major(sin_a, packed_imag)
    freq_imag = major(cos_a, packed_imag) - major(sin_a, packed_real)
    cos_dev, sin_dev = turn_table(np.arange(seqs) * width, row_ids, full)
    cos_dev = lax.dynamic_index_in_dim(cos_dev, seq_index, 0, keepdims=False)[:, None, None]
    sin_dev = lax.dynamic_index_in_dim(sin_dev, seq_index, 0, keepdims=False)[:, None, None]
    cos_col, sin_col = turn_table(row_ids, np.arange(width), full)
    cos_col, sin_col = cos_col[:, None, :], sin_col[:, None, :]
    cos_t = cos_dev * cos_col - sin_dev * sin_col
    sin_t = sin_dev * cos_col + cos_dev * sin_col
    spread_real = freq_real * cos_t + freq_imag * sin_t
    spread_imag = freq_imag * cos_t - freq_real * sin_t
    spread = jnp.stack([spread_real, spread_imag], axis=1).astype(bf16)
    spread = spread.reshape(seqs, 2, 2, chans, width)
    recv = lax.all_to_all(spread, "seq", 0, 0, tiled=True).astype(f32)
    rows_real, rows_imag = recv[:, :, 0], recv[:, :, 1]

    cos_o, sin_o = turn_table(np.arange(seqs), np.arange(seqs), seqs)
    cos_w, sin_w = turn_table(np.arange(seqs), np.arange(width), length)
    cos_w, sin_w = cos_w[:, None, None, :], sin_w[:, None, None, :]
    cos_i, sin_i = turn_table(np.arange(width), np.arange(width), width)
    first_real = major(cos_o, rows_real) + major(sin_o, rows_imag)
    first_imag = major(cos_o, rows_imag) - major(sin_o, rows_real)
    twist_real = first_real * cos_w + first_imag * sin_w
    twist_imag = first_imag * cos_w - first_real * sin_w
    fwd_block = jnp.concatenate(
        [jnp.concatenate([cos_i, -sin_i], axis=1), jnp.concatenate([sin_i, cos_i], axis=1)], axis=0
    )
    inv_block = jnp.concatenate(
        [jnp.concatenate([cos_i, sin_i], axis=1), jnp.concatenate([-sin_i, cos_i], axis=1)], axis=0
    )
    spec = minor(jnp.concatenate([twist_real, twist_imag], axis=-1), fwd_block)
    spec_real, spec_imag = spec[..., :width], spec[..., width:]

    lane_in = lax.broadcasted_iota(jnp.int32, (width, width), 0)
    lane_out = lax.broadcasted_iota(jnp.int32, (width, width), 1)
    lane_flip = (lane_in == width - 1 - lane_out).astype(f32)
    lane_neg = (lane_in == (width - lane_out) % width).astype(f32)
    place = lax.broadcasted_iota(jnp.int32, (rows, rows), 0)
    source = lax.broadcasted_iota(jnp.int32, (rows, rows), 1)
    place_q, place_s = place // 2, place % 2
    cross_src = 2 * (seqs - 1 - place_q) + 1 - place_s
    self_src = jnp.where(place_s == 1, 2 * (seqs - 1 - place_q) + 1, 2 * ((seqs - place_q) % seqs))
    first_dev = seq_index == 0
    regroup = (source == jnp.where(first_dev, self_src, cross_src)).astype(f32)

    def negated(spec):
        flipped = jnp.einsum("...b,bm->...m", spec, lane_flip, precision=HIGH)
        moved = jnp.einsum(
            "uv,vcb->ucb", regroup, flipped.reshape(rows, chans, width), precision=HIGH
        ).reshape(spec.shape)
        corner = jnp.einsum("cb,bm->cm", spec[0, 0], lane_neg, precision=HIGH)
        return moved.at[0, 0].set(jnp.where(first_dev, corner, moved[0, 0]))

    neg_real = negated(spec_real)
    neg_imag = negated(spec_imag)

    a_real = 0.5 * (spec_real + neg_real)
    a_imag = 0.5 * (spec_imag - neg_imag)
    b_real = 0.5 * (spec_imag + neg_imag)
    b_imag = 0.5 * (neg_real - spec_real)
    sig1_r, sig1_i, filt1_r, filt1_i = (
        a_real[:, :, :pairs], a_imag[:, :, :pairs], a_real[:, :, pairs:], a_imag[:, :, pairs:]
    )
    sig2_r, sig2_i, filt2_r, filt2_i = (
        b_real[:, :, :pairs], b_imag[:, :, :pairs], b_real[:, :, pairs:], b_imag[:, :, pairs:]
    )
    prod1_r = sig1_r * filt1_r - sig1_i * filt1_i
    prod1_i = sig1_r * filt1_i + sig1_i * filt1_r
    prod2_r = sig2_r * filt2_r - sig2_i * filt2_i
    prod2_i = sig2_r * filt2_i + sig2_i * filt2_r
    prod_real = prod1_r - prod2_i
    prod_imag = prod1_i + prod2_r

    inv = minor(jnp.concatenate([prod_real, prod_imag], axis=-1), inv_block)
    inv_real, inv_imag = inv[..., :width], inv[..., width:]
    untwist_real = inv_real * cos_w - inv_imag * sin_w
    untwist_imag = inv_imag * cos_w + inv_real * sin_w
    back_real = major(cos_o, untwist_real) - major(sin_o, untwist_imag)
    back_imag = major(cos_o, untwist_imag) + major(sin_o, untwist_real)

    own_rows = slot_rows(seq_index, jnp.arange(2), seqs)
    cos_blk, sin_blk = turn_table(np.arange(rows), np.arange(seqs) * width, full)
    cos_off, sin_off = turn_table(np.arange(rows), np.arange(width), full)
    cos_blk, sin_blk = jnp.take(cos_blk, own_rows, axis=0).T, jnp.take(sin_blk, own_rows, axis=0).T
    cos_off, sin_off = jnp.take(cos_off, own_rows, axis=0), jnp.take(sin_off, own_rows, axis=0)
    cos_b = (cos_blk[:, :, None] * cos_off[None] - sin_blk[:, :, None] * sin_off[None])[:, :, None, :]
    sin_b = (sin_blk[:, :, None] * cos_off[None] + cos_blk[:, :, None] * sin_off[None])[:, :, None, :]
    reverted_real = back_real * cos_b - back_imag * sin_b
    reverted_imag = back_imag * cos_b + back_real * sin_b
    reverted = jnp.stack([reverted_real, reverted_imag], axis=2).astype(bf16)
    moved = lax.all_to_all(reverted, "seq", 0, 0, tiled=True).astype(f32)
    moved = moved.reshape(rows, 2, pairs, width)

    cos_l, sin_l = turn_table(np.arange(seqs), row_ids, rows)
    merged_real = major(cos_l, moved[:, 0]) - major(sin_l, moved[:, 1])
    merged_imag = major(cos_l, moved[:, 1]) + major(sin_l, moved[:, 0])
    merged = jnp.concatenate([merged_real, merged_imag], axis=1) * (1.0 / full)
    arrived = lax.all_to_all(merged.astype(bf16), "seq", 0, 0, tiled=True)
    conv = arrived.astype(f32).transpose(1, 0, 2).reshape(chans, length)
    gated_out = (query_gate.astype(f32) * conv).astype(bf16)

    tp_index = lax.axis_index("tp")
    tps = lax.axis_size("tp")
    other_chip = tp_index ^ 2
    other_core = tp_index ^ 1
    cross = [(i, i ^ 2) for i in range(tps)]
    gated_far = lax.ppermute(gated_out, "tp", cross)

    def weights(rows_of, cols_of):
        return lax.dynamic_slice(out_weight, (rows_of * chans, cols_of * chans), (chans, chans))

    def partial(rows_of):
        near = jnp.dot(weights(rows_of, tp_index), gated_out, preferred_element_type=f32)
        far = jnp.dot(weights(rows_of, other_chip), gated_far, preferred_element_type=f32)
        return near + far

    pair = [(i, i ^ 1) for i in range(tps)]
    send_part = partial(other_core)
    keep_part = partial(tp_index)
    total = keep_part + lax.ppermute(send_part.astype(bf16), "tp", pair).astype(f32)
    return total.astype(bf16)


def solution(mesh):
    return jax.shard_map(
        body,
        mesh=mesh,
        in_specs=(P("tp", "seq"), P("tp", "seq"), P("tp", "seq"), P("tp", "seq"), P()),
        out_specs=P("tp", "seq"),
        check_vma=False,
    )
```

```python
import math

import jax
import numpy as np
import jax.numpy as jnp
from jax import lax
from jax.experimental import pallas as pl
from jax.sharding import PartitionSpec as P

HIGH = lax.Precision.HIGH


def turn_table(row_ids, col_ids, modulus):
    turns = (np.asarray(row_ids, np.int64)[:, None] * np.asarray(col_ids, np.int64)[None, :]) % modulus
    angles = turns.astype(np.float64) * (2.0 * math.pi / modulus)
    return (jnp.asarray(np.cos(angles), jnp.float32), jnp.asarray(np.sin(angles), jnp.float32))


def block_table(cos, sin, sign, cols_reim_inner, rows_reim_inner=False):
    n_out, n_in = cos.shape
    tab = np.zeros((2, n_out, 2, n_in))
    tab[0, :, 0], tab[0, :, 1] = cos, -sign * sin
    tab[1, :, 0], tab[1, :, 1] = sign * sin, cos
    if cols_reim_inner:
        tab = tab.transpose(0, 1, 3, 2)
    if rows_reim_inner:
        tab = tab.transpose(1, 0, 2, 3)
    return jnp.asarray(tab.reshape(2 * n_out, 2 * n_in), jnp.float32)


def np_turns(row_ids, col_ids, modulus):
    turns = (np.asarray(row_ids, np.int64)[:, None] * np.asarray(col_ids, np.int64)[None, :]) % modulus
    angles = turns.astype(np.float64) * (2.0 * math.pi / modulus)
    return np.cos(angles), np.sin(angles)


def row_list(seqs):
    return np.array([d if s == 0 else (seqs if d == 0 else 2 * seqs - d) for d in range(seqs) for s in range(2)])


def slot_rows(device, slot, seqs):
    return jnp.where(slot == 0, device, jnp.where(device == 0, seqs, 2 * seqs - device))


def major(table, data):
    return jnp.einsum("qk,k...->q...", table, data, precision=HIGH)


def minor(data, table):
    return jnp.einsum("...b,bm->...m", data, table, precision=HIGH)


def send_blocks(key_gate, value_input, long_filter, seqs, interpret=False):
    chans, length = key_gate.shape
    width = length // seqs
    pairs = chans // 2

    def kernel(key_ref, value_ref, taps_ref, out_ref):
        for d in range(seqs):
            cols = slice(d * width, (d + 1) * width)
            gated = key_ref[:, cols].astype(jnp.float32) * value_ref[:, cols].astype(jnp.float32)
            gated = gated.astype(jnp.bfloat16)
            taps = taps_ref[:, cols].astype(jnp.bfloat16)
            out_ref[d, 0:pairs] = gated[:pairs]
            out_ref[d, pairs:chans] = taps[:pairs]
            out_ref[d, chans:chans + pairs] = gated[pairs:]
            out_ref[d, chans + pairs:2 * chans] = taps[pairs:]

    return pl.pallas_call(
        kernel,
        out_shape=jax.ShapeDtypeStruct((seqs, 2 * chans, width), jnp.bfloat16),
        interpret=interpret,
    )(key_gate, value_input, long_filter)


def body(query_gate, key_gate, value_input, long_filter, out_weight):
    chans, length = key_gate.shape
    seqs = lax.axis_size("seq")
    seq_index = lax.axis_index("seq")
    width = length // seqs
    rows = 2 * seqs
    full = rows * length
    pairs = chans // 2
    f32, bf16 = jnp.float32, jnp.bfloat16

    send = send_blocks(key_gate, value_input, long_filter, seqs)
    got = lax.all_to_all(send, "seq", 0, 0, tiled=True).astype(f32)
    packed_real, packed_imag = got[:, :chans], got[:, chans:]

    row_ids = row_list(seqs)
    cos_a, sin_a = turn_table(row_ids, np.arange(seqs), rows)
    freq_real = major(cos_a, packed_real) + major(sin_a, packed_imag)
    freq_imag = major(cos_a, packed_imag) - major(sin_a, packed_real)
    cos_dev, sin_dev = turn_table(np.arange(seqs) * width, row_ids, full)
    cos_dev = lax.dynamic_index_in_dim(cos_dev, seq_index, 0, keepdims=False)[:, None, None]
    sin_dev = lax.dynamic_index_in_dim(sin_dev, seq_index, 0, keepdims=False)[:, None, None]
    cos_col, sin_col = turn_table(row_ids, np.arange(width), full)
    cos_col, sin_col = cos_col[:, None, :], sin_col[:, None, :]
    cos_t = cos_dev * cos_col - sin_dev * sin_col
    sin_t = sin_dev * cos_col + cos_dev * sin_col
    spread_real = freq_real * cos_t + freq_imag * sin_t
    spread_imag = freq_imag * cos_t - freq_real * sin_t
    spread = jnp.stack([spread_real, spread_imag], axis=1).astype(bf16)
    spread = spread.reshape(seqs, 2, 2, chans, width).transpose(0, 2, 1, 3, 4)
    recv = lax.all_to_all(spread, "seq", 0, 0, tiled=True).astype(f32)

    cos_o, sin_o = turn_table(np.arange(seqs), np.arange(seqs), seqs)
    cos_w, sin_w = turn_table(np.arange(seqs), np.arange(width), length)
    cos_w, sin_w = cos_w[:, None, None, :], sin_w[:, None, None, :]
    cos_i, sin_i = turn_table(np.arange(width), np.arange(width), width)
    co_np, so_np = np_turns(np.arange(seqs), np.arange(seqs), seqs)
    first = major(block_table(co_np, so_np, -1.0, True), recv.reshape((2 * seqs,) + recv.shape[2:]))
    first_real, first_imag = first[:seqs], first[seqs:]
    twist_real = first_real * cos_w + first_imag * sin_w
    twist_imag = first_imag * cos_w - first_real * sin_w
    fwd_block = jnp.concatenate(
        [jnp.concatenate([cos_i, -sin_i], axis=1), jnp.concatenate([sin_i, cos_i], axis=1)], axis=0
    )
    inv_block = jnp.concatenate(
        [jnp.concatenate([cos_i, sin_i], axis=1), jnp.concatenate([-sin_i, cos_i], axis=1)], axis=0
    )
    spec = minor(jnp.concatenate([twist_real, twist_imag], axis=-1), fwd_block)
    spec_real, spec_imag = spec[..., :width], spec[..., width:]

    lane_in = lax.broadcasted_iota(jnp.int32, (width, width), 0)
    lane_out = lax.broadcasted_iota(jnp.int32, (width, width), 1)
    lane_flip = (lane_in == width - 1 - lane_out).astype(f32)
    lane_neg = (lane_in == (width - lane_out) % width).astype(f32)
    place = lax.broadcasted_iota(jnp.int32, (rows, rows), 0)
    source = lax.broadcasted_iota(jnp.int32, (rows, rows), 1)
    place_q, place_s = place // 2, place % 2
    cross_src = 2 * (seqs - 1 - place_q) + 1 - place_s
    self_src = jnp.where(place_s == 1, 2 * (seqs - 1 - place_q) + 1, 2 * ((seqs - place_q) % seqs))
    first_dev = seq_index == 0
    regroup = (source == jnp.where(first_dev, self_src, cross_src)).astype(f32)

    def negated(spec):
        flipped = jnp.einsum("...b,bm->...m", spec, lane_flip, precision=HIGH)
        moved = jnp.einsum(
            "uv,vcb->ucb", regroup, flipped.reshape(rows, chans, width), precision=HIGH
        ).reshape(spec.shape)
        corner = jnp.einsum("cb,bm->cm", spec[0, 0], lane_neg, precision=HIGH)
        return moved.at[0, 0].set(jnp.where(first_dev, corner, moved[0, 0]))

    neg_real = negated(spec_real)
    neg_imag = negated(spec_imag)

    a_real = 0.5 * (spec_real + neg_real)
    a_imag = 0.5 * (spec_imag - neg_imag)
    b_real = 0.5 * (spec_imag + neg_imag)
    b_imag = 0.5 * (neg_real - spec_real)
    sig1_r, sig1_i, filt1_r, filt1_i = (
        a_real[:, :, :pairs], a_imag[:, :, :pairs], a_real[:, :, pairs:], a_imag[:, :, pairs:]
    )
    sig2_r, sig2_i, filt2_r, filt2_i = (
        b_real[:, :, :pairs], b_imag[:, :, :pairs], b_real[:, :, pairs:], b_imag[:, :, pairs:]
    )
    prod1_r = sig1_r * filt1_r - sig1_i * filt1_i
    prod1_i = sig1_r * filt1_i + sig1_i * filt1_r
    prod2_r = sig2_r * filt2_r - sig2_i * filt2_i
    prod2_i = sig2_r * filt2_i + sig2_i * filt2_r
    prod_real = prod1_r - prod2_i
    prod_imag = prod1_i + prod2_r

    inv = minor(jnp.concatenate([prod_real, prod_imag], axis=-1), inv_block)
    inv_real, inv_imag = inv[..., :width], inv[..., width:]
    untwist_real = inv_real * cos_w - inv_imag * sin_w
    untwist_imag = inv_imag * cos_w + inv_real * sin_w
    untwist = jnp.stack([untwist_real, untwist_imag], axis=0)
    back = major(block_table(co_np, so_np, 1.0, False), untwist.reshape((2 * seqs,) + untwist.shape[2:]))
    back_real, back_imag = back[:seqs], back[seqs:]

    own_rows = slot_rows(seq_index, jnp.arange(2), seqs)
    cos_blk, sin_blk = turn_table(np.arange(rows), np.arange(seqs) * width, full)
    cos_off, sin_off = turn_table(np.arange(rows), np.arange(width), full)
    cos_blk, sin_blk = jnp.take(cos_blk, own_rows, axis=0).T, jnp.take(sin_blk, own_rows, axis=0).T
    cos_off, sin_off = jnp.take(cos_off, own_rows, axis=0), jnp.take(sin_off, own_rows, axis=0)
    cos_b = (cos_blk[:, :, None] * cos_off[None] - sin_blk[:, :, None] * sin_off[None])[:, :, None, :]
    sin_b = (sin_blk[:, :, None] * cos_off[None] + cos_blk[:, :, None] * sin_off[None])[:, :, None, :]
    reverted_real = back_real * cos_b - back_imag * sin_b
    reverted_imag = back_imag * cos_b + back_real * sin_b
    reverted = jnp.stack([reverted_real, reverted_imag], axis=2).astype(bf16)
    moved = lax.all_to_all(reverted, "seq", 0, 0, tiled=True).astype(f32)
    moved = moved.reshape(2 * rows, pairs, width)

    cl_np, sl_np = np_turns(np.arange(seqs), row_ids, rows)
    merged = major(block_table(cl_np, sl_np, 1.0, True, rows_reim_inner=True), moved)
    merged = merged.reshape(seqs, chans, width) * (1.0 / full)
    arrived = lax.all_to_all(merged.astype(bf16), "seq", 0, 0, tiled=True)
    conv = arrived.astype(f32).transpose(1, 0, 2).reshape(chans, length)
    gated_out = (query_gate.astype(f32) * conv).astype(bf16)

    tp_index = lax.axis_index("tp")
    tps = lax.axis_size("tp")
    other_chip = tp_index ^ 2
    other_core = tp_index ^ 1
    cross = [(i, i ^ 2) for i in range(tps)]
    gated_far = lax.ppermute(gated_out, "tp", cross)

    def weights(rows_of, cols_of):
        return lax.dynamic_slice(out_weight, (rows_of * chans, cols_of * chans), (chans, chans))

    def partial(rows_of):
        near = jnp.dot(weights(rows_of, tp_index), gated_out, preferred_element_type=f32)
        far = jnp.dot(weights(rows_of, other_chip), gated_far, preferred_element_type=f32)
        return near + far

    pair = [(i, i ^ 1) for i in range(tps)]
    send_part = partial(other_core)
    keep_part = partial(tp_index)
    total = keep_part + lax.ppermute(send_part.astype(bf16), "tp", pair).astype(f32)
    return total.astype(bf16)


def solution(mesh):
    return jax.shard_map(
        body,
        mesh=mesh,
        in_specs=(P("tp", "seq"), P("tp", "seq"), P("tp", "seq"), P("tp", "seq"), P()),
        out_specs=P("tp", "seq"),
        check_vma=False,
    )
```

```python
import math

import jax
import numpy as np
import jax.numpy as jnp
from jax import lax
from jax.experimental import pallas as pl
from jax.sharding import PartitionSpec as P

HIGH = lax.Precision.HIGH


def turn_table(row_ids, col_ids, modulus):
    turns = (np.asarray(row_ids, np.int64)[:, None] * np.asarray(col_ids, np.int64)[None, :]) % modulus
    angles = turns.astype(np.float64) * (2.0 * math.pi / modulus)
    return (jnp.asarray(np.cos(angles), jnp.float32), jnp.asarray(np.sin(angles), jnp.float32))


def block_table(cos, sin, sign, cols_reim_inner, rows_reim_inner=False):
    n_out, n_in = cos.shape
    tab = np.zeros((2, n_out, 2, n_in))
    tab[0, :, 0], tab[0, :, 1] = cos, -sign * sin
    tab[1, :, 0], tab[1, :, 1] = sign * sin, cos
    if cols_reim_inner:
        tab = tab.transpose(0, 1, 3, 2)
    if rows_reim_inner:
        tab = tab.transpose(1, 0, 2, 3)
    return jnp.asarray(tab.reshape(2 * n_out, 2 * n_in), jnp.float32)


def np_turns(row_ids, col_ids, modulus):
    turns = (np.asarray(row_ids, np.int64)[:, None] * np.asarray(col_ids, np.int64)[None, :]) % modulus
    angles = turns.astype(np.float64) * (2.0 * math.pi / modulus)
    return np.cos(angles), np.sin(angles)


def row_list(seqs):
    return np.array([d if s == 0 else (seqs if d == 0 else 2 * seqs - d) for d in range(seqs) for s in range(2)])


def slot_rows(device, slot, seqs):
    return jnp.where(slot == 0, device, jnp.where(device == 0, seqs, 2 * seqs - device))


def major(table, data):
    return jnp.einsum("qk,k...->q...", table, data, precision=HIGH)


def minor(data, table):
    return jnp.einsum("...b,bm->...m", data, table, precision=HIGH)


def send_blocks(key_gate, value_input, long_filter, seqs, interpret=False):
    chans, length = key_gate.shape
    width = length // seqs
    pairs = chans // 2

    def kernel(key_ref, value_ref, taps_ref, out_ref):
        for d in range(seqs):
            cols = slice(d * width, (d + 1) * width)
            gated = key_ref[:, cols].astype(jnp.float32) * value_ref[:, cols].astype(jnp.float32)
            gated = gated.astype(jnp.bfloat16)
            taps = taps_ref[:, cols].astype(jnp.bfloat16)
            out_ref[d, 0:pairs] = gated[:pairs]
            out_ref[d, pairs:chans] = taps[:pairs]
            out_ref[d, chans:chans + pairs] = gated[pairs:]
            out_ref[d, chans + pairs:2 * chans] = taps[pairs:]

    return pl.pallas_call(
        kernel,
        out_shape=jax.ShapeDtypeStruct((seqs, 2 * chans, width), jnp.bfloat16),
        interpret=interpret,
    )(key_gate, value_input, long_filter)


def body(query_gate, key_gate, value_input, long_filter, out_weight):
    chans, length = key_gate.shape
    seqs = lax.axis_size("seq")
    seq_index = lax.axis_index("seq")
    width = length // seqs
    rows = 2 * seqs
    full = rows * length
    pairs = chans // 2
    f32, bf16 = jnp.float32, jnp.bfloat16

    send = send_blocks(key_gate, value_input, long_filter, seqs)
    got = lax.all_to_all(send, "seq", 0, 0, tiled=True).astype(f32)
    got = got.reshape((2 * seqs, chans, width))

    row_ids = row_list(seqs)
    ca_np, sa_np = np_turns(row_ids, np.arange(seqs), rows)
    first_tab = block_table(ca_np, sa_np, -1.0, True).reshape(2, seqs, 2, 2 * seqs)
    first_tab = first_tab.transpose(1, 0, 2, 3).reshape(2 * rows, 2 * seqs)
    freq = major(first_tab, got).reshape(seqs, 2, 2, chans, width)
    freq_real, freq_imag = freq[:, 0], freq[:, 1]
    cos_dev, sin_dev = turn_table(np.arange(seqs) * width, row_ids, full)
    cos_dev = lax.dynamic_index_in_dim(cos_dev, seq_index, 0, keepdims=False).reshape(seqs, 2, 1, 1)
    sin_dev = lax.dynamic_index_in_dim(sin_dev, seq_index, 0, keepdims=False).reshape(seqs, 2, 1, 1)
    cos_col, sin_col = turn_table(row_ids, np.arange(width), full)
    cos_col, sin_col = cos_col.reshape(seqs, 2, 1, width), sin_col.reshape(seqs, 2, 1, width)
    cos_t = cos_dev * cos_col - sin_dev * sin_col
    sin_t = sin_dev * cos_col + cos_dev * sin_col
    spread_real = freq_real * cos_t + freq_imag * sin_t
    spread_imag = freq_imag * cos_t - freq_real * sin_t
    spread = jnp.stack([spread_real, spread_imag], axis=1).astype(bf16)
    recv = lax.all_to_all(spread, "seq", 0, 0, tiled=True).astype(f32)

    cos_o, sin_o = turn_table(np.arange(seqs), np.arange(seqs), seqs)
    cos_w, sin_w = turn_table(np.arange(seqs), np.arange(width), length)
    cos_w, sin_w = cos_w[:, None, None, :], sin_w[:, None, None, :]
    cos_i, sin_i = turn_table(np.arange(width), np.arange(width), width)
    co_np, so_np = np_turns(np.arange(seqs), np.arange(seqs), seqs)
    first = major(block_table(co_np, so_np, -1.0, True), recv.reshape((2 * seqs,) + recv.shape[2:]))
    first_real, first_imag = first[:seqs], first[seqs:]
    twist_real = first_real * cos_w + first_imag * sin_w
    twist_imag = first_imag * cos_w - first_real * sin_w
    fwd_block = jnp.concatenate(
        [jnp.concatenate([cos_i, -sin_i], axis=1), jnp.concatenate([sin_i, cos_i], axis=1)], axis=0
    )
    inv_block = jnp.concatenate(
        [jnp.concatenate([cos_i, sin_i], axis=1), jnp.concatenate([-sin_i, cos_i], axis=1)], axis=0
    )
    spec = minor(jnp.concatenate([twist_real, twist_imag], axis=-1), fwd_block)
    spec_real, spec_imag = spec[..., :width], spec[..., width:]

    lane_in = lax.broadcasted_iota(jnp.int32, (width, width), 0)
    lane_out = lax.broadcasted_iota(jnp.int32, (width, width), 1)
    lane_flip = (lane_in == width - 1 - lane_out).astype(f32)
    lane_neg = (lane_in == (width - lane_out) % width).astype(f32)
    place = lax.broadcasted_iota(jnp.int32, (rows, rows), 0)
    source = lax.broadcasted_iota(jnp.int32, (rows, rows), 1)
    place_q, place_s = place // 2, place % 2
    cross_src = 2 * (seqs - 1 - place_q) + 1 - place_s
    self_src = jnp.where(place_s == 1, 2 * (seqs - 1 - place_q) + 1, 2 * ((seqs - place_q) % seqs))
    first_dev = seq_index == 0
    regroup = (source == jnp.where(first_dev, self_src, cross_src)).astype(f32)

    def negated(spec):
        flipped = jnp.einsum("...b,bm->...m", spec, lane_flip, precision=HIGH)
        moved = jnp.einsum(
            "uv,vcb->ucb", regroup, flipped.reshape(rows, chans, width), precision=HIGH
        ).reshape(spec.shape)
        corner = jnp.einsum("cb,bm->cm", spec[0, 0], lane_neg, precision=HIGH)
        return moved.at[0, 0].set(jnp.where(first_dev, corner, moved[0, 0]))

    neg_real = negated(spec_real)
    neg_imag = negated(spec_imag)

    a_real = 0.5 * (spec_real + neg_real)
    a_imag = 0.5 * (spec_imag - neg_imag)
    b_real = 0.5 * (spec_imag + neg_imag)
    b_imag = 0.5 * (neg_real - spec_real)
    sig1_r, sig1_i, filt1_r, filt1_i = (
        a_real[:, :, :pairs], a_imag[:, :, :pairs], a_real[:, :, pairs:], a_imag[:, :, pairs:]
    )
    sig2_r, sig2_i, filt2_r, filt2_i = (
        b_real[:, :, :pairs], b_imag[:, :, :pairs], b_real[:, :, pairs:], b_imag[:, :, pairs:]
    )
    prod1_r = sig1_r * filt1_r - sig1_i * filt1_i
    prod1_i = sig1_r * filt1_i + sig1_i * filt1_r
    prod2_r = sig2_r * filt2_r - sig2_i * filt2_i
    prod2_i = sig2_r * filt2_i + sig2_i * filt2_r
    prod_real = prod1_r - prod2_i
    prod_imag = prod1_i + prod2_r

    inv = minor(jnp.concatenate([prod_real, prod_imag], axis=-1), inv_block)
    inv_real, inv_imag = inv[..., :width], inv[..., width:]
    untwist_real = inv_real * cos_w - inv_imag * sin_w
    untwist_imag = inv_imag * cos_w + inv_real * sin_w
    untwist = jnp.stack([untwist_real, untwist_imag], axis=0)
    back = major(block_table(co_np, so_np, 1.0, False), untwist.reshape((2 * seqs,) + untwist.shape[2:]))
    back_real, back_imag = back[:seqs], back[seqs:]

    own_rows = slot_rows(seq_index, jnp.arange(2), seqs)
    cos_blk, sin_blk = turn_table(np.arange(rows), np.arange(seqs) * width, full)
    cos_off, sin_off = turn_table(np.arange(rows), np.arange(width), full)
    cos_blk, sin_blk = jnp.take(cos_blk, own_rows, axis=0).T, jnp.take(sin_blk, own_rows, axis=0).T
    cos_off, sin_off = jnp.take(cos_off, own_rows, axis=0), jnp.take(sin_off, own_rows, axis=0)
    cos_b = (cos_blk[:, :, None] * cos_off[None] - sin_blk[:, :, None] * sin_off[None])[:, :, None, :]
    sin_b = (sin_blk[:, :, None] * cos_off[None] + cos_blk[:, :, None] * sin_off[None])[:, :, None, :]
    reverted_real = back_real * cos_b - back_imag * sin_b
    reverted_imag = back_imag * cos_b + back_real * sin_b
    reverted = jnp.stack([reverted_real, reverted_imag], axis=2).astype(bf16)
    moved = lax.all_to_all(reverted, "seq", 0, 0, tiled=True).astype(f32)
    moved = moved.reshape(2 * rows, pairs, width)

    cl_np, sl_np = np_turns(np.arange(seqs), row_ids, rows)
    merged = major(block_table(cl_np, sl_np, 1.0, True, rows_reim_inner=True), moved)
    merged = merged.reshape(seqs, chans, width) * (1.0 / full)
    arrived = lax.all_to_all(merged.astype(bf16), "seq", 0, 0, tiled=True)
    conv = arrived.astype(f32).transpose(1, 0, 2).reshape(chans, length)
    gated_out = (query_gate.astype(f32) * conv).astype(bf16)

    tp_index = lax.axis_index("tp")
    tps = lax.axis_size("tp")
    other_chip = tp_index ^ 2
    other_core = tp_index ^ 1
    cross = [(i, i ^ 2) for i in range(tps)]
    gated_far = lax.ppermute(gated_out, "tp", cross)

    def weights(rows_of, cols_of):
        return lax.dynamic_slice(out_weight, (rows_of * chans, cols_of * chans), (chans, chans))

    def partial(rows_of):
        near = jnp.dot(weights(rows_of, tp_index), gated_out, preferred_element_type=f32)
        far = jnp.dot(weights(rows_of, other_chip), gated_far, preferred_element_type=f32)
        return near + far

    pair = [(i, i ^ 1) for i in range(tps)]
    send_part = partial(other_core)
    keep_part = partial(tp_index)
    total = keep_part + lax.ppermute(send_part.astype(bf16), "tp", pair).astype(f32)
    return total.astype(bf16)


def solution(mesh):
    return jax.shard_map(
        body,
        mesh=mesh,
        in_specs=(P("tp", "seq"), P("tp", "seq"), P("tp", "seq"), P("tp", "seq"), P()),
        out_specs=P("tp", "seq"),
        check_vma=False,
    )
```

```python
import math

import jax
import numpy as np
import jax.numpy as jnp
from jax import lax
from jax.experimental import pallas as pl
from jax.sharding import PartitionSpec as P

HIGH = lax.Precision.HIGH


def turn_table(row_ids, col_ids, modulus):
    turns = (np.asarray(row_ids, np.int64)[:, None] * np.asarray(col_ids, np.int64)[None, :]) % modulus
    angles = turns.astype(np.float64) * (2.0 * math.pi / modulus)
    return (jnp.asarray(np.cos(angles), jnp.float32), jnp.asarray(np.sin(angles), jnp.float32))


def block_table(cos, sin, sign, cols_reim_inner, rows_reim_inner=False):
    n_out, n_in = cos.shape
    tab = np.zeros((2, n_out, 2, n_in))
    tab[0, :, 0], tab[0, :, 1] = cos, -sign * sin
    tab[1, :, 0], tab[1, :, 1] = sign * sin, cos
    if cols_reim_inner:
        tab = tab.transpose(0, 1, 3, 2)
    if rows_reim_inner:
        tab = tab.transpose(1, 0, 2, 3)
    return jnp.asarray(tab.reshape(2 * n_out, 2 * n_in), jnp.float32)


def np_turns(row_ids, col_ids, modulus):
    turns = (np.asarray(row_ids, np.int64)[:, None] * np.asarray(col_ids, np.int64)[None, :]) % modulus
    angles = turns.astype(np.float64) * (2.0 * math.pi / modulus)
    return np.cos(angles), np.sin(angles)


def row_list(seqs):
    return np.array([d if s == 0 else (seqs if d == 0 else 2 * seqs - d) for d in range(seqs) for s in range(2)])


def slot_rows(device, slot, seqs):
    return jnp.where(slot == 0, device, jnp.where(device == 0, seqs, 2 * seqs - device))


def major(table, data):
    return jnp.einsum("qk,k...->q...", table, data, precision=HIGH)


def major_exact(table, data):
    head = table.astype(jnp.bfloat16)
    tail = (table - head.astype(jnp.float32)).astype(jnp.bfloat16)
    spec = "qk,k...->q..."
    return (jnp.einsum(spec, head, data, preferred_element_type=jnp.float32)
            + jnp.einsum(spec, tail, data, preferred_element_type=jnp.float32))


def minor(data, table):
    return jnp.einsum("...b,bm->...m", data, table, precision=HIGH)


def send_blocks(key_gate, value_input, long_filter, seqs, interpret=False):
    chans, length = key_gate.shape
    width = length // seqs
    pairs = chans // 2

    def kernel(key_ref, value_ref, taps_ref, out_ref):
        for d in range(seqs):
            cols = slice(d * width, (d + 1) * width)
            gated = key_ref[:, cols].astype(jnp.float32) * value_ref[:, cols].astype(jnp.float32)
            gated = gated.astype(jnp.bfloat16)
            taps = taps_ref[:, cols].astype(jnp.bfloat16)
            out_ref[d, 0:pairs] = gated[:pairs]
            out_ref[d, pairs:chans] = taps[:pairs]
            out_ref[d, chans:chans + pairs] = gated[pairs:]
            out_ref[d, chans + pairs:2 * chans] = taps[pairs:]

    return pl.pallas_call(
        kernel,
        out_shape=jax.ShapeDtypeStruct((seqs, 2 * chans, width), jnp.bfloat16),
        interpret=interpret,
    )(key_gate, value_input, long_filter)


def body(query_gate, key_gate, value_input, long_filter, out_weight):
    chans, length = key_gate.shape
    seqs = lax.axis_size("seq")
    seq_index = lax.axis_index("seq")
    width = length // seqs
    rows = 2 * seqs
    full = rows * length
    pairs = chans // 2
    f32, bf16 = jnp.float32, jnp.bfloat16

    send = send_blocks(key_gate, value_input, long_filter, seqs)
    got = lax.all_to_all(send, "seq", 0, 0, tiled=True)
    packed_real, packed_imag = got[:, :chans], got[:, chans:]

    row_ids = row_list(seqs)
    cos_a, sin_a = turn_table(row_ids, np.arange(seqs), rows)
    freq_real = major_exact(cos_a, packed_real) + major_exact(sin_a, packed_imag)
    freq_imag = major_exact(cos_a, packed_imag) - major_exact(sin_a, packed_real)
    cos_dev, sin_dev = turn_table(np.arange(seqs) * width, row_ids, full)
    cos_dev = lax.dynamic_index_in_dim(cos_dev, seq_index, 0, keepdims=False)[:, None, None]
    sin_dev = lax.dynamic_index_in_dim(sin_dev, seq_index, 0, keepdims=False)[:, None, None]
    cos_col, sin_col = turn_table(row_ids, np.arange(width), full)
    cos_col, sin_col = cos_col[:, None, :], sin_col[:, None, :]
    cos_t = cos_dev * cos_col - sin_dev * sin_col
    sin_t = sin_dev * cos_col + cos_dev * sin_col
    spread_real = freq_real * cos_t + freq_imag * sin_t
    spread_imag = freq_imag * cos_t - freq_real * sin_t
    spread = jnp.stack([spread_real, spread_imag], axis=1).astype(bf16)
    spread = spread.reshape(seqs, 2, 2, chans, width).transpose(0, 2, 1, 3, 4)
    recv = lax.all_to_all(spread, "seq", 0, 0, tiled=True)

    cos_o, sin_o = turn_table(np.arange(seqs), np.arange(seqs), seqs)
    cos_w, sin_w = turn_table(np.arange(seqs), np.arange(width), length)
    cos_w, sin_w = cos_w[:, None, None, :], sin_w[:, None, None, :]
    cos_i, sin_i = turn_table(np.arange(width), np.arange(width), width)
    co_np, so_np = np_turns(np.arange(seqs), np.arange(seqs), seqs)
    first = major_exact(block_table(co_np, so_np, -1.0, True), recv.reshape((2 * seqs,) + recv.shape[2:]))
    first_real, first_imag = first[:seqs], first[seqs:]
    twist_real = first_real * cos_w + first_imag * sin_w
    twist_imag = first_imag * cos_w - first_real * sin_w
    fwd_block = jnp.concatenate(
        [jnp.concatenate([cos_i, -sin_i], axis=1), jnp.concatenate([sin_i, cos_i], axis=1)], axis=0
    )
    inv_block = jnp.concatenate(
        [jnp.concatenate([cos_i, sin_i], axis=1), jnp.concatenate([-sin_i, cos_i], axis=1)], axis=0
    )
    spec = minor(jnp.concatenate([twist_real, twist_imag], axis=-1), fwd_block)
    spec_real, spec_imag = spec[..., :width], spec[..., width:]

    lane_in = lax.broadcasted_iota(jnp.int32, (width, width), 0)
    lane_out = lax.broadcasted_iota(jnp.int32, (width, width), 1)
    lane_flip = (lane_in == width - 1 - lane_out).astype(f32)
    lane_neg = (lane_in == (width - lane_out) % width).astype(f32)
    place = lax.broadcasted_iota(jnp.int32, (rows, rows), 0)
    source = lax.broadcasted_iota(jnp.int32, (rows, rows), 1)
    place_q, place_s = place // 2, place % 2
    cross_src = 2 * (seqs - 1 - place_q) + 1 - place_s
    self_src = jnp.where(place_s == 1, 2 * (seqs - 1 - place_q) + 1, 2 * ((seqs - place_q) % seqs))
    first_dev = seq_index == 0
    regroup = (source == jnp.where(first_dev, self_src, cross_src)).astype(f32)

    def negated(spec):
        flipped = jnp.einsum("...b,bm->...m", spec, lane_flip, precision=HIGH)
        moved = jnp.einsum(
            "uv,vcb->ucb", regroup, flipped.reshape(rows, chans, width), precision=HIGH
        ).reshape(spec.shape)
        corner = jnp.einsum("cb,bm->cm", spec[0, 0], lane_neg, precision=HIGH)
        return moved.at[0, 0].set(jnp.where(first_dev, corner, moved[0, 0]))

    neg_real = negated(spec_real)
    neg_imag = negated(spec_imag)

    a_real = 0.5 * (spec_real + neg_real)
    a_imag = 0.5 * (spec_imag - neg_imag)
    b_real = 0.5 * (spec_imag + neg_imag)
    b_imag = 0.5 * (neg_real - spec_real)
    sig1_r, sig1_i, filt1_r, filt1_i = (
        a_real[:, :, :pairs], a_imag[:, :, :pairs], a_real[:, :, pairs:], a_imag[:, :, pairs:]
    )
    sig2_r, sig2_i, filt2_r, filt2_i = (
        b_real[:, :, :pairs], b_imag[:, :, :pairs], b_real[:, :, pairs:], b_imag[:, :, pairs:]
    )
    prod1_r = sig1_r * filt1_r - sig1_i * filt1_i
    prod1_i = sig1_r * filt1_i + sig1_i * filt1_r
    prod2_r = sig2_r * filt2_r - sig2_i * filt2_i
    prod2_i = sig2_r * filt2_i + sig2_i * filt2_r
    prod_real = prod1_r - prod2_i
    prod_imag = prod1_i + prod2_r

    inv = minor(jnp.concatenate([prod_real, prod_imag], axis=-1), inv_block)
    inv_real, inv_imag = inv[..., :width], inv[..., width:]
    untwist_real = inv_real * cos_w - inv_imag * sin_w
    untwist_imag = inv_imag * cos_w + inv_real * sin_w
    untwist = jnp.stack([untwist_real, untwist_imag], axis=0)
    back = major(block_table(co_np, so_np, 1.0, False), untwist.reshape((2 * seqs,) + untwist.shape[2:]))
    back_real, back_imag = back[:seqs], back[seqs:]

    own_rows = slot_rows(seq_index, jnp.arange(2), seqs)
    cos_blk, sin_blk = turn_table(np.arange(rows), np.arange(seqs) * width, full)
    cos_off, sin_off = turn_table(np.arange(rows), np.arange(width), full)
    cos_blk, sin_blk = jnp.take(cos_blk, own_rows, axis=0).T, jnp.take(sin_blk, own_rows, axis=0).T
    cos_off, sin_off = jnp.take(cos_off, own_rows, axis=0), jnp.take(sin_off, own_rows, axis=0)
    cos_b = (cos_blk[:, :, None] * cos_off[None] - sin_blk[:, :, None] * sin_off[None])[:, :, None, :]
    sin_b = (sin_blk[:, :, None] * cos_off[None] + cos_blk[:, :, None] * sin_off[None])[:, :, None, :]
    reverted_real = back_real * cos_b - back_imag * sin_b
    reverted_imag = back_imag * cos_b + back_real * sin_b
    reverted = jnp.stack([reverted_real, reverted_imag], axis=2).astype(bf16)
    moved = lax.all_to_all(reverted, "seq", 0, 0, tiled=True)
    moved = moved.reshape(2 * rows, pairs, width)

    cl_np, sl_np = np_turns(np.arange(seqs), row_ids, rows)
    merged = major_exact(block_table(cl_np, sl_np, 1.0, True, rows_reim_inner=True), moved)
    merged = merged.reshape(seqs, chans, width) * (1.0 / full)
    arrived = lax.all_to_all(merged.astype(bf16), "seq", 0, 0, tiled=True)
    conv = arrived.astype(f32).transpose(1, 0, 2).reshape(chans, length)
    gated_out = (query_gate.astype(f32) * conv).astype(bf16)

    tp_index = lax.axis_index("tp")
    tps = lax.axis_size("tp")
    other_chip = tp_index ^ 2
    other_core = tp_index ^ 1
    cross = [(i, i ^ 2) for i in range(tps)]
    gated_far = lax.ppermute(gated_out, "tp", cross)

    def weights(rows_of, cols_of):
        return lax.dynamic_slice(out_weight, (rows_of * chans, cols_of * chans), (chans, chans))

    def partial(rows_of):
        near = jnp.dot(weights(rows_of, tp_index), gated_out, preferred_element_type=f32)
        far = jnp.dot(weights(rows_of, other_chip), gated_far, preferred_element_type=f32)
        return near + far

    pair = [(i, i ^ 1) for i in range(tps)]
    send_part = partial(other_core)
    keep_part = partial(tp_index)
    total = keep_part + lax.ppermute(send_part.astype(bf16), "tp", pair).astype(f32)
    return total.astype(bf16)


def solution(mesh):
    return jax.shard_map(
        body,
        mesh=mesh,
        in_specs=(P("tp", "seq"), P("tp", "seq"), P("tp", "seq"), P("tp", "seq"), P()),
        out_specs=P("tp", "seq"),
        check_vma=False,
    )
```

```python
import math

import jax
import numpy as np
import jax.numpy as jnp
from jax import lax
from jax.experimental import pallas as pl
from jax.sharding import PartitionSpec as P

HIGH = lax.Precision.HIGH


def turn_table(row_ids, col_ids, modulus):
    turns = (np.asarray(row_ids, np.int64)[:, None] * np.asarray(col_ids, np.int64)[None, :]) % modulus
    angles = turns.astype(np.float64) * (2.0 * math.pi / modulus)
    return (jnp.asarray(np.cos(angles), jnp.float32), jnp.asarray(np.sin(angles), jnp.float32))


def block_table(cos, sin, sign, cols_reim_inner, rows_reim_inner=False):
    n_out, n_in = cos.shape
    tab = np.zeros((2, n_out, 2, n_in))
    tab[0, :, 0], tab[0, :, 1] = cos, -sign * sin
    tab[1, :, 0], tab[1, :, 1] = sign * sin, cos
    if cols_reim_inner:
        tab = tab.transpose(0, 1, 3, 2)
    if rows_reim_inner:
        tab = tab.transpose(1, 0, 2, 3)
    return jnp.asarray(tab.reshape(2 * n_out, 2 * n_in), jnp.float32)


def np_turns(row_ids, col_ids, modulus):
    turns = (np.asarray(row_ids, np.int64)[:, None] * np.asarray(col_ids, np.int64)[None, :]) % modulus
    angles = turns.astype(np.float64) * (2.0 * math.pi / modulus)
    return np.cos(angles), np.sin(angles)


def row_list(seqs):
    return np.array([d if s == 0 else (seqs if d == 0 else 2 * seqs - d) for d in range(seqs) for s in range(2)])


def slot_rows(device, slot, seqs):
    return jnp.where(slot == 0, device, jnp.where(device == 0, seqs, 2 * seqs - device))


def major(table, data):
    return jnp.einsum("qk,k...->q...", table, data, precision=HIGH)


def minor(data, table):
    return jnp.einsum("...b,bm->...m", data, table, precision=HIGH)


def send_blocks(key_gate, value_input, long_filter, seqs, interpret=False):
    chans, length = key_gate.shape
    width = length // seqs
    pairs = chans // 2

    def kernel(key_ref, value_ref, taps_ref, out_ref):
        for d in range(seqs):
            cols = slice(d * width, (d + 1) * width)
            gated = key_ref[:, cols].astype(jnp.float32) * value_ref[:, cols].astype(jnp.float32)
            gated = gated.astype(jnp.bfloat16)
            taps = taps_ref[:, cols].astype(jnp.bfloat16)
            out_ref[d, 0:pairs] = gated[:pairs]
            out_ref[d, pairs:chans] = taps[:pairs]
            out_ref[d, chans:chans + pairs] = gated[pairs:]
            out_ref[d, chans + pairs:2 * chans] = taps[pairs:]

    return pl.pallas_call(
        kernel,
        out_shape=jax.ShapeDtypeStruct((seqs, 2 * chans, width), jnp.bfloat16),
        interpret=interpret,
    )(key_gate, value_input, long_filter)


def body(query_gate, key_gate, value_input, long_filter, out_weight):
    chans, length = key_gate.shape
    seqs = lax.axis_size("seq")
    seq_index = lax.axis_index("seq")
    width = length // seqs
    rows = 2 * seqs
    full = rows * length
    pairs = chans // 2
    f32, bf16 = jnp.float32, jnp.bfloat16

    send = send_blocks(key_gate, value_input, long_filter, seqs)
    got = lax.all_to_all(send, "seq", 0, 0, tiled=True).astype(f32)
    packed_real, packed_imag = got[:, :chans], got[:, chans:]

    row_ids = row_list(seqs)
    cos_a, sin_a = turn_table(row_ids, np.arange(seqs), rows)
    freq_real = major(cos_a, packed_real) + major(sin_a, packed_imag)
    freq_imag = major(cos_a, packed_imag) - major(sin_a, packed_real)
    cos_dev, sin_dev = turn_table(np.arange(seqs) * width, row_ids, full)
    cos_dev = lax.dynamic_index_in_dim(cos_dev, seq_index, 0, keepdims=False)[:, None, None]
    sin_dev = lax.dynamic_index_in_dim(sin_dev, seq_index, 0, keepdims=False)[:, None, None]
    cos_col, sin_col = turn_table(row_ids, np.arange(width), full)
    cos_col, sin_col = cos_col[:, None, :], sin_col[:, None, :]
    cos_t = cos_dev * cos_col - sin_dev * sin_col
    sin_t = sin_dev * cos_col + cos_dev * sin_col
    spread_real = freq_real * cos_t + freq_imag * sin_t
    spread_imag = freq_imag * cos_t - freq_real * sin_t
    spread = jnp.stack([spread_real, spread_imag], axis=1).astype(bf16)
    spread = spread.reshape(seqs, 2, 2, chans, width).transpose(0, 2, 1, 3, 4)
    recv = lax.all_to_all(spread, "seq", 0, 0, tiled=True).astype(f32)

    cos_o, sin_o = turn_table(np.arange(seqs), np.arange(seqs), seqs)
    cos_w, sin_w = turn_table(np.arange(seqs), np.arange(width), length)
    cos_w, sin_w = cos_w[:, None, None, :], sin_w[:, None, None, :]
    cos_i, sin_i = turn_table(np.arange(width), np.arange(width), width)
    co_np, so_np = np_turns(np.arange(seqs), np.arange(seqs), seqs)
    first = major(block_table(co_np, so_np, -1.0, True), recv.reshape((2 * seqs,) + recv.shape[2:]))
    first_real, first_imag = first[:seqs], first[seqs:]
    twist_real = first_real * cos_w + first_imag * sin_w
    twist_imag = first_imag * cos_w - first_real * sin_w
    fwd_block = jnp.concatenate(
        [jnp.concatenate([cos_i, -sin_i], axis=1), jnp.concatenate([sin_i, cos_i], axis=1)], axis=0
    )
    inv_block = jnp.concatenate(
        [jnp.concatenate([cos_i, sin_i], axis=1), jnp.concatenate([-sin_i, cos_i], axis=1)], axis=0
    )
    spec = minor(jnp.concatenate([twist_real, twist_imag], axis=-1), fwd_block)
    spec_real, spec_imag = spec[..., :width], spec[..., width:]

    lane_in = lax.broadcasted_iota(jnp.int32, (width, width), 0)
    lane_out = lax.broadcasted_iota(jnp.int32, (width, width), 1)
    lane_flip = (lane_in == width - 1 - lane_out).astype(f32)
    lane_neg = (lane_in == (width - lane_out) % width).astype(f32)
    place = lax.broadcasted_iota(jnp.int32, (rows, rows), 0)
    source = lax.broadcasted_iota(jnp.int32, (rows, rows), 1)
    place_q, place_s = place // 2, place % 2
    cross_src = 2 * (seqs - 1 - place_q) + 1 - place_s
    self_src = jnp.where(place_s == 1, 2 * (seqs - 1 - place_q) + 1, 2 * ((seqs - place_q) % seqs))
    first_dev = seq_index == 0
    regroup = (source == jnp.where(first_dev, self_src, cross_src)).astype(f32)

    def negated(spec):
        flipped = jnp.einsum("...b,bm->...m", spec, lane_flip, precision=HIGH)
        moved = jnp.einsum(
            "uv,vcb->ucb", regroup, flipped.reshape(rows, chans, 2 * width), precision=HIGH
        ).reshape(spec.shape)
        corner = jnp.einsum("cb,bm->cm", spec[0, 0], lane_neg, precision=HIGH)
        return moved.at[0, 0].set(jnp.where(first_dev, corner, moved[0, 0]))

    zeros = jnp.zeros_like(lane_flip)
    lane_flip = jnp.concatenate(
        [jnp.concatenate([lane_flip, zeros], axis=1), jnp.concatenate([zeros, lane_flip], axis=1)], axis=0
    )
    lane_neg = jnp.concatenate(
        [jnp.concatenate([lane_neg, zeros], axis=1), jnp.concatenate([zeros, lane_neg], axis=1)], axis=0
    )
    neg = negated(spec)
    neg_real, neg_imag = neg[..., :width], neg[..., width:]

    a_real = 0.5 * (spec_real + neg_real)
    a_imag = 0.5 * (spec_imag - neg_imag)
    b_real = 0.5 * (spec_imag + neg_imag)
    b_imag = 0.5 * (neg_real - spec_real)
    sig1_r, sig1_i, filt1_r, filt1_i = (
        a_real[:, :, :pairs], a_imag[:, :, :pairs], a_real[:, :, pairs:], a_imag[:, :, pairs:]
    )
    sig2_r, sig2_i, filt2_r, filt2_i = (
        b_real[:, :, :pairs], b_imag[:, :, :pairs], b_real[:, :, pairs:], b_imag[:, :, pairs:]
    )
    prod1_r = sig1_r * filt1_r - sig1_i * filt1_i
    prod1_i = sig1_r * filt1_i + sig1_i * filt1_r
    prod2_r = sig2_r * filt2_r - sig2_i * filt2_i
    prod2_i = sig2_r * filt2_i + sig2_i * filt2_r
    prod_real = prod1_r - prod2_i
    prod_imag = prod1_i + prod2_r

    inv = minor(jnp.concatenate([prod_real, prod_imag], axis=-1), inv_block)
    inv_real, inv_imag = inv[..., :width], inv[..., width:]
    untwist_real = inv_real * cos_w - inv_imag * sin_w
    untwist_imag = inv_imag * cos_w + inv_real * sin_w
    untwist = jnp.stack([untwist_real, untwist_imag], axis=0)
    back = major(block_table(co_np, so_np, 1.0, False), untwist.reshape((2 * seqs,) + untwist.shape[2:]))
    back_real, back_imag = back[:seqs], back[seqs:]

    own_rows = slot_rows(seq_index, jnp.arange(2), seqs)
    cos_blk, sin_blk = turn_table(np.arange(rows), np.arange(seqs) * width, full)
    cos_off, sin_off = turn_table(np.arange(rows), np.arange(width), full)
    cos_blk, sin_blk = jnp.take(cos_blk, own_rows, axis=0).T, jnp.take(sin_blk, own_rows, axis=0).T
    cos_off, sin_off = jnp.take(cos_off, own_rows, axis=0), jnp.take(sin_off, own_rows, axis=0)
    cos_b = (cos_blk[:, :, None] * cos_off[None] - sin_blk[:, :, None] * sin_off[None])[:, :, None, :]
    sin_b = (sin_blk[:, :, None] * cos_off[None] + cos_blk[:, :, None] * sin_off[None])[:, :, None, :]
    reverted_real = back_real * cos_b - back_imag * sin_b
    reverted_imag = back_imag * cos_b + back_real * sin_b
    reverted = jnp.stack([reverted_real, reverted_imag], axis=2).astype(bf16)
    moved = lax.all_to_all(reverted, "seq", 0, 0, tiled=True).astype(f32)
    moved = moved.reshape(2 * rows, pairs, width)

    cl_np, sl_np = np_turns(np.arange(seqs), row_ids, rows)
    merged = major(block_table(cl_np, sl_np, 1.0, True, rows_reim_inner=True), moved)
    merged = merged.reshape(seqs, chans, width) * (1.0 / full)
    arrived = lax.all_to_all(merged.astype(bf16), "seq", 0, 0, tiled=True)
    conv = arrived.astype(f32).transpose(1, 0, 2).reshape(chans, length)
    gated_out = (query_gate.astype(f32) * conv).astype(bf16)

    tp_index = lax.axis_index("tp")
    tps = lax.axis_size("tp")
    other_chip = tp_index ^ 2
    other_core = tp_index ^ 1
    cross = [(i, i ^ 2) for i in range(tps)]
    gated_far = lax.ppermute(gated_out, "tp", cross)

    def weights(rows_of, cols_of):
        return lax.dynamic_slice(out_weight, (rows_of * chans, cols_of * chans), (chans, chans))

    def partial(rows_of):
        near = jnp.dot(weights(rows_of, tp_index), gated_out, preferred_element_type=f32)
        far = jnp.dot(weights(rows_of, other_chip), gated_far, preferred_element_type=f32)
        return near + far

    pair = [(i, i ^ 1) for i in range(tps)]
    send_part = partial(other_core)
    keep_part = partial(tp_index)
    total = keep_part + lax.ppermute(send_part.astype(bf16), "tp", pair).astype(f32)
    return total.astype(bf16)


def solution(mesh):
    return jax.shard_map(
        body,
        mesh=mesh,
        in_specs=(P("tp", "seq"), P("tp", "seq"), P("tp", "seq"), P("tp", "seq"), P()),
        out_specs=P("tp", "seq"),
        check_vma=False,
    )
```

```python
import math

import jax
import numpy as np
import jax.numpy as jnp
from jax import lax
from jax.experimental import pallas as pl
from jax.sharding import PartitionSpec as P

HIGH = lax.Precision.HIGH


def turn_table(row_ids, col_ids, modulus):
    turns = (np.asarray(row_ids, np.int64)[:, None] * np.asarray(col_ids, np.int64)[None, :]) % modulus
    angles = turns.astype(np.float64) * (2.0 * math.pi / modulus)
    return (jnp.asarray(np.cos(angles), jnp.float32), jnp.asarray(np.sin(angles), jnp.float32))


def block_table(cos, sin, sign, cols_reim_inner, rows_reim_inner=False):
    n_out, n_in = cos.shape
    tab = np.zeros((2, n_out, 2, n_in))
    tab[0, :, 0], tab[0, :, 1] = cos, -sign * sin
    tab[1, :, 0], tab[1, :, 1] = sign * sin, cos
    if cols_reim_inner:
        tab = tab.transpose(0, 1, 3, 2)
    if rows_reim_inner:
        tab = tab.transpose(1, 0, 2, 3)
    return jnp.asarray(tab.reshape(2 * n_out, 2 * n_in), jnp.float32)


def np_turns(row_ids, col_ids, modulus):
    turns = (np.asarray(row_ids, np.int64)[:, None] * np.asarray(col_ids, np.int64)[None, :]) % modulus
    angles = turns.astype(np.float64) * (2.0 * math.pi / modulus)
    return np.cos(angles), np.sin(angles)


def row_list(seqs):
    return np.array([d if s == 0 else (seqs if d == 0 else 2 * seqs - d) for d in range(seqs) for s in range(2)])


def slot_rows(device, slot, seqs):
    return jnp.where(slot == 0, device, jnp.where(device == 0, seqs, 2 * seqs - device))


def major(table, data):
    return jnp.einsum("qk,k...->q...", table, data, precision=HIGH)


def minor(data, table):
    return jnp.einsum("...b,bm->...m", data, table, precision=HIGH)


def permuted(spec, data, table):
    head = data.astype(jnp.bfloat16)
    tail = (data - head.astype(jnp.float32)).astype(jnp.bfloat16)
    perm = table.astype(jnp.bfloat16)
    return (jnp.einsum(spec, head, perm, preferred_element_type=jnp.float32)
            + jnp.einsum(spec, tail, perm, preferred_element_type=jnp.float32))


def send_blocks(key_gate, value_input, long_filter, seqs, interpret=False):
    chans, length = key_gate.shape
    width = length // seqs
    pairs = chans // 2

    def kernel(key_ref, value_ref, taps_ref, out_ref):
        for d in range(seqs):
            cols = slice(d * width, (d + 1) * width)
            gated = key_ref[:, cols].astype(jnp.float32) * value_ref[:, cols].astype(jnp.float32)
            gated = gated.astype(jnp.bfloat16)
            taps = taps_ref[:, cols].astype(jnp.bfloat16)
            out_ref[d, 0:pairs] = gated[:pairs]
            out_ref[d, pairs:chans] = taps[:pairs]
            out_ref[d, chans:chans + pairs] = gated[pairs:]
            out_ref[d, chans + pairs:2 * chans] = taps[pairs:]

    return pl.pallas_call(
        kernel,
        out_shape=jax.ShapeDtypeStruct((seqs, 2 * chans, width), jnp.bfloat16),
        interpret=interpret,
    )(key_gate, value_input, long_filter)


def body(query_gate, key_gate, value_input, long_filter, out_weight):
    chans, length = key_gate.shape
    seqs = lax.axis_size("seq")
    seq_index = lax.axis_index("seq")
    width = length // seqs
    rows = 2 * seqs
    full = rows * length
    pairs = chans // 2
    f32, bf16 = jnp.float32, jnp.bfloat16

    send = send_blocks(key_gate, value_input, long_filter, seqs)
    got = lax.all_to_all(send, "seq", 0, 0, tiled=True).astype(f32)
    packed_real, packed_imag = got[:, :chans], got[:, chans:]

    row_ids = row_list(seqs)
    cos_a, sin_a = turn_table(row_ids, np.arange(seqs), rows)
    freq_real = major(cos_a, packed_real) + major(sin_a, packed_imag)
    freq_imag = major(cos_a, packed_imag) - major(sin_a, packed_real)
    cos_dev, sin_dev = turn_table(np.arange(seqs) * width, row_ids, full)
    cos_dev = lax.dynamic_index_in_dim(cos_dev, seq_index, 0, keepdims=False)[:, None, None]
    sin_dev = lax.dynamic_index_in_dim(sin_dev, seq_index, 0, keepdims=False)[:, None, None]
    cos_col, sin_col = turn_table(row_ids, np.arange(width), full)
    cos_col, sin_col = cos_col[:, None, :], sin_col[:, None, :]
    cos_t = cos_dev * cos_col - sin_dev * sin_col
    sin_t = sin_dev * cos_col + cos_dev * sin_col
    spread_real = freq_real * cos_t + freq_imag * sin_t
    spread_imag = freq_imag * cos_t - freq_real * sin_t
    spread = jnp.stack([spread_real, spread_imag], axis=1).astype(bf16)
    spread = spread.reshape(seqs, 2, 2, chans, width).transpose(0, 2, 1, 3, 4)
    recv = lax.all_to_all(spread, "seq", 0, 0, tiled=True).astype(f32)

    cos_o, sin_o = turn_table(np.arange(seqs), np.arange(seqs), seqs)
    cos_w, sin_w = turn_table(np.arange(seqs), np.arange(width), length)
    cos_w, sin_w = cos_w[:, None, None, :], sin_w[:, None, None, :]
    cos_i, sin_i = turn_table(np.arange(width), np.arange(width), width)
    co_np, so_np = np_turns(np.arange(seqs), np.arange(seqs), seqs)
    first = major(block_table(co_np, so_np, -1.0, True), recv.reshape((2 * seqs,) + recv.shape[2:]))
    first_real, first_imag = first[:seqs], first[seqs:]
    twist_real = first_real * cos_w + first_imag * sin_w
    twist_imag = first_imag * cos_w - first_real * sin_w
    fwd_block = jnp.concatenate(
        [jnp.concatenate([cos_i, -sin_i], axis=1), jnp.concatenate([sin_i, cos_i], axis=1)], axis=0
    )
    inv_block = jnp.concatenate(
        [jnp.concatenate([cos_i, sin_i], axis=1), jnp.concatenate([-sin_i, cos_i], axis=1)], axis=0
    )
    spec = minor(jnp.concatenate([twist_real, twist_imag], axis=-1), fwd_block)
    spec_real, spec_imag = spec[..., :width], spec[..., width:]

    lane_in = lax.broadcasted_iota(jnp.int32, (width, width), 0)
    lane_out = lax.broadcasted_iota(jnp.int32, (width, width), 1)
    lane_flip = (lane_in == width - 1 - lane_out).astype(f32)
    lane_neg = (lane_in == (width - lane_out) % width).astype(f32)
    place = lax.broadcasted_iota(jnp.int32, (rows, rows), 0)
    source = lax.broadcasted_iota(jnp.int32, (rows, rows), 1)
    place_q, place_s = place // 2, place % 2
    cross_src = 2 * (seqs - 1 - place_q) + 1 - place_s
    self_src = jnp.where(place_s == 1, 2 * (seqs - 1 - place_q) + 1, 2 * ((seqs - place_q) % seqs))
    first_dev = seq_index == 0
    regroup = (source == jnp.where(first_dev, self_src, cross_src)).astype(f32)

    def negated(spec):
        flipped = permuted("...b,bm->...m", spec, lane_flip)
        moved = permuted("vcb,uv->ucb", flipped.reshape(rows, chans, 2 * width), regroup).reshape(spec.shape)
        corner = permuted("cb,bm->cm", spec[0, 0], lane_neg)
        return moved.at[0, 0].set(jnp.where(first_dev, corner, moved[0, 0]))

    zeros = jnp.zeros_like(lane_flip)
    lane_flip = jnp.concatenate(
        [jnp.concatenate([lane_flip, zeros], axis=1), jnp.concatenate([zeros, lane_flip], axis=1)], axis=0
    )
    lane_neg = jnp.concatenate(
        [jnp.concatenate([lane_neg, zeros], axis=1), jnp.concatenate([zeros, lane_neg], axis=1)], axis=0
    )
    neg = negated(spec)
    neg_real, neg_imag = neg[..., :width], neg[..., width:]

    a_real = 0.5 * (spec_real + neg_real)
    a_imag = 0.5 * (spec_imag - neg_imag)
    b_real = 0.5 * (spec_imag + neg_imag)
    b_imag = 0.5 * (neg_real - spec_real)
    sig1_r, sig1_i, filt1_r, filt1_i = (
        a_real[:, :, :pairs], a_imag[:, :, :pairs], a_real[:, :, pairs:], a_imag[:, :, pairs:]
    )
    sig2_r, sig2_i, filt2_r, filt2_i = (
        b_real[:, :, :pairs], b_imag[:, :, :pairs], b_real[:, :, pairs:], b_imag[:, :, pairs:]
    )
    prod1_r = sig1_r * filt1_r - sig1_i * filt1_i
    prod1_i = sig1_r * filt1_i + sig1_i * filt1_r
    prod2_r = sig2_r * filt2_r - sig2_i * filt2_i
    prod2_i = sig2_r * filt2_i + sig2_i * filt2_r
    prod_real = prod1_r - prod2_i
    prod_imag = prod1_i + prod2_r

    inv = minor(jnp.concatenate([prod_real, prod_imag], axis=-1), inv_block)
    inv_real, inv_imag = inv[..., :width], inv[..., width:]
    untwist_real = inv_real * cos_w - inv_imag * sin_w
    untwist_imag = inv_imag * cos_w + inv_real * sin_w
    untwist = jnp.stack([untwist_real, untwist_imag], axis=0)
    back = major(block_table(co_np, so_np, 1.0, False), untwist.reshape((2 * seqs,) + untwist.shape[2:]))
    back_real, back_imag = back[:seqs], back[seqs:]

    own_rows = slot_rows(seq_index, jnp.arange(2), seqs)
    cos_blk, sin_blk = turn_table(np.arange(rows), np.arange(seqs) * width, full)
    cos_off, sin_off = turn_table(np.arange(rows), np.arange(width), full)
    cos_blk, sin_blk = jnp.take(cos_blk, own_rows, axis=0).T, jnp.take(sin_blk, own_rows, axis=0).T
    cos_off, sin_off = jnp.take(cos_off, own_rows, axis=0), jnp.take(sin_off, own_rows, axis=0)
    cos_b = (cos_blk[:, :, None] * cos_off[None] - sin_blk[:, :, None] * sin_off[None])[:, :, None, :]
    sin_b = (sin_blk[:, :, None] * cos_off[None] + cos_blk[:, :, None] * sin_off[None])[:, :, None, :]
    reverted_real = back_real * cos_b - back_imag * sin_b
    reverted_imag = back_imag * cos_b + back_real * sin_b
    reverted = jnp.stack([reverted_real, reverted_imag], axis=2).astype(bf16)
    moved = lax.all_to_all(reverted, "seq", 0, 0, tiled=True).astype(f32)
    moved = moved.reshape(2 * rows, pairs, width)

    cl_np, sl_np = np_turns(np.arange(seqs), row_ids, rows)
    merged = major(block_table(cl_np, sl_np, 1.0, True, rows_reim_inner=True), moved)
    merged = merged.reshape(seqs, chans, width) * (1.0 / full)
    arrived = lax.all_to_all(merged.astype(bf16), "seq", 0, 0, tiled=True)
    conv = arrived.astype(f32).transpose(1, 0, 2).reshape(chans, length)
    gated_out = (query_gate.astype(f32) * conv).astype(bf16)

    tp_index = lax.axis_index("tp")
    tps = lax.axis_size("tp")
    other_chip = tp_index ^ 2
    other_core = tp_index ^ 1
    cross = [(i, i ^ 2) for i in range(tps)]
    gated_far = lax.ppermute(gated_out, "tp", cross)

    def weights(rows_of, cols_of):
        return lax.dynamic_slice(out_weight, (rows_of * chans, cols_of * chans), (chans, chans))

    def partial(rows_of):
        near = jnp.dot(weights(rows_of, tp_index), gated_out, preferred_element_type=f32)
        far = jnp.dot(weights(rows_of, other_chip), gated_far, preferred_element_type=f32)
        return near + far

    pair = [(i, i ^ 1) for i in range(tps)]
    send_part = partial(other_core)
    keep_part = partial(tp_index)
    total = keep_part + lax.ppermute(send_part.astype(bf16), "tp", pair).astype(f32)
    return total.astype(bf16)


def solution(mesh):
    return jax.shard_map(
        body,
        mesh=mesh,
        in_specs=(P("tp", "seq"), P("tp", "seq"), P("tp", "seq"), P("tp", "seq"), P()),
        out_specs=P("tp", "seq"),
        check_vma=False,
    )
```

```python
import math

import jax
import numpy as np
import jax.numpy as jnp
from jax import lax
from jax.experimental import pallas as pl
from jax.sharding import PartitionSpec as P

HIGH = lax.Precision.HIGH


def turn_table(row_ids, col_ids, modulus):
    turns = (np.asarray(row_ids, np.int64)[:, None] * np.asarray(col_ids, np.int64)[None, :]) % modulus
    angles = turns.astype(np.float64) * (2.0 * math.pi / modulus)
    return (jnp.asarray(np.cos(angles), jnp.float32), jnp.asarray(np.sin(angles), jnp.float32))


def block_table(cos, sin, sign, cols_reim_inner, rows_reim_inner=False):
    n_out, n_in = cos.shape
    tab = np.zeros((2, n_out, 2, n_in))
    tab[0, :, 0], tab[0, :, 1] = cos, -sign * sin
    tab[1, :, 0], tab[1, :, 1] = sign * sin, cos
    if cols_reim_inner:
        tab = tab.transpose(0, 1, 3, 2)
    if rows_reim_inner:
        tab = tab.transpose(1, 0, 2, 3)
    return jnp.asarray(tab.reshape(2 * n_out, 2 * n_in), jnp.float32)


def np_turns(row_ids, col_ids, modulus):
    turns = (np.asarray(row_ids, np.int64)[:, None] * np.asarray(col_ids, np.int64)[None, :]) % modulus
    angles = turns.astype(np.float64) * (2.0 * math.pi / modulus)
    return np.cos(angles), np.sin(angles)


def row_list(seqs):
    return np.array([d if s == 0 else (seqs if d == 0 else 2 * seqs - d) for d in range(seqs) for s in range(2)])


def slot_rows(device, slot, seqs):
    return jnp.where(slot == 0, device, jnp.where(device == 0, seqs, 2 * seqs - device))


def major(table, data):
    return jnp.einsum("qk,k...->q...", table, data, precision=HIGH)


def minor(data, table):
    return jnp.einsum("...b,bm->...m", data, table, precision=HIGH)


def send_blocks(key_gate, value_input, long_filter, seqs, interpret=False):
    chans, length = key_gate.shape
    width = length // seqs
    pairs = chans // 2

    def kernel(key_ref, value_ref, taps_ref, out_ref):
        for d in range(seqs):
            cols = slice(d * width, (d + 1) * width)
            gated = key_ref[:, cols].astype(jnp.float32) * value_ref[:, cols].astype(jnp.float32)
            gated = gated.astype(jnp.bfloat16)
            taps = taps_ref[:, cols].astype(jnp.bfloat16)
            out_ref[d, 0:pairs] = gated[:pairs]
            out_ref[d, pairs:chans] = taps[:pairs]
            out_ref[d, chans:chans + pairs] = gated[pairs:]
            out_ref[d, chans + pairs:2 * chans] = taps[pairs:]

    return pl.pallas_call(
        kernel,
        out_shape=jax.ShapeDtypeStruct((seqs, 2 * chans, width), jnp.bfloat16),
        interpret=interpret,
    )(key_gate, value_input, long_filter)


def body(query_gate, key_gate, value_input, long_filter, out_weight):
    chans, length = key_gate.shape
    seqs = lax.axis_size("seq")
    seq_index = lax.axis_index("seq")
    width = length // seqs
    rows = 2 * seqs
    full = rows * length
    pairs = chans // 2
    f32, bf16 = jnp.float32, jnp.bfloat16

    send = send_blocks(key_gate, value_input, long_filter, seqs)
    got = lax.all_to_all(send, "seq", 0, 0, tiled=True).astype(f32)
    packed_real, packed_imag = got[:, :chans], got[:, chans:]

    row_ids = row_list(seqs)
    cos_a, sin_a = turn_table(row_ids, np.arange(seqs), rows)
    freq_real = major(cos_a, packed_real) + major(sin_a, packed_imag)
    freq_imag = major(cos_a, packed_imag) - major(sin_a, packed_real)
    cos_dev, sin_dev = turn_table(np.arange(seqs) * width, row_ids, full)
    cos_dev = lax.dynamic_index_in_dim(cos_dev, seq_index, 0, keepdims=False)[:, None, None]
    sin_dev = lax.dynamic_index_in_dim(sin_dev, seq_index, 0, keepdims=False)[:, None, None]
    cos_col, sin_col = turn_table(row_ids, np.arange(width), full)
    cos_col, sin_col = cos_col[:, None, :], sin_col[:, None, :]
    cos_t = cos_dev * cos_col - sin_dev * sin_col
    sin_t = sin_dev * cos_col + cos_dev * sin_col
    spread_real = freq_real * cos_t + freq_imag * sin_t
    spread_imag = freq_imag * cos_t - freq_real * sin_t
    spread = jnp.stack([spread_real, spread_imag], axis=1).astype(bf16)
    spread = spread.reshape(seqs, 2, 2, chans, width).transpose(0, 2, 1, 3, 4)
    recv = lax.all_to_all(spread, "seq", 0, 0, tiled=True).astype(f32)

    cos_o, sin_o = turn_table(np.arange(seqs), np.arange(seqs), seqs)
    cos_w, sin_w = turn_table(np.arange(seqs), np.arange(width), length)
    cos_w, sin_w = cos_w[:, None, None, :], sin_w[:, None, None, :]
    cos_i, sin_i = turn_table(np.arange(width), np.arange(width), width)
    co_np, so_np = np_turns(np.arange(seqs), np.arange(seqs), seqs)
    first = major(block_table(co_np, so_np, -1.0, True), recv.reshape((2 * seqs,) + recv.shape[2:]))
    first_real, first_imag = first[:seqs], first[seqs:]
    twist_real = first_real * cos_w + first_imag * sin_w
    twist_imag = first_imag * cos_w - first_real * sin_w
    fwd_block = jnp.concatenate(
        [jnp.concatenate([cos_i, -sin_i], axis=1), jnp.concatenate([sin_i, cos_i], axis=1)], axis=0
    )
    inv_block = jnp.concatenate(
        [jnp.concatenate([cos_i, sin_i], axis=1), jnp.concatenate([-sin_i, cos_i], axis=1)], axis=0
    )
    spec = minor(jnp.concatenate([twist_real, twist_imag], axis=-1), fwd_block)
    spec_real, spec_imag = spec[..., :width], spec[..., width:]

    lane_in = lax.broadcasted_iota(jnp.int32, (width, width), 0)
    lane_out = lax.broadcasted_iota(jnp.int32, (width, width), 1)
    lane_flip = (lane_in == width - 1 - lane_out).astype(f32)
    lane_neg = (lane_in == (width - lane_out) % width).astype(f32)
    place = lax.broadcasted_iota(jnp.int32, (rows, rows), 0)
    source = lax.broadcasted_iota(jnp.int32, (rows, rows), 1)
    place_q, place_s = place // 2, place % 2
    cross_src = 2 * (seqs - 1 - place_q) + 1 - place_s
    self_src = jnp.where(place_s == 1, 2 * (seqs - 1 - place_q) + 1, 2 * ((seqs - place_q) % seqs))
    first_dev = seq_index == 0
    regroup = (source == jnp.where(first_dev, self_src, cross_src)).astype(f32)

    def negated(spec):
        regrouped = jnp.einsum(
            "uv,vcb->ucb", regroup, spec.reshape(rows, chans, 2 * width), precision=HIGH
        ).reshape(spec.shape)
        moved = jnp.einsum("...b,bm->...m", regrouped, lane_flip, precision=HIGH)
        corner = jnp.einsum("cb,bm->cm", spec[0, 0], lane_neg, precision=HIGH)
        return moved.at[0, 0].set(jnp.where(first_dev, corner, moved[0, 0]))

    zeros = jnp.zeros_like(lane_flip)
    lane_flip = jnp.concatenate(
        [jnp.concatenate([lane_flip, zeros], axis=1), jnp.concatenate([zeros, lane_flip], axis=1)], axis=0
    )
    lane_neg = jnp.concatenate(
        [jnp.concatenate([lane_neg, zeros], axis=1), jnp.concatenate([zeros, lane_neg], axis=1)], axis=0
    )
    neg = negated(spec)
    neg_real, neg_imag = neg[..., :width], neg[..., width:]

    a_real = 0.5 * (spec_real + neg_real)
    a_imag = 0.5 * (spec_imag - neg_imag)
    b_real = 0.5 * (spec_imag + neg_imag)
    b_imag = 0.5 * (neg_real - spec_real)
    sig1_r, sig1_i, filt1_r, filt1_i = (
        a_real[:, :, :pairs], a_imag[:, :, :pairs], a_real[:, :, pairs:], a_imag[:, :, pairs:]
    )
    sig2_r, sig2_i, filt2_r, filt2_i = (
        b_real[:, :, :pairs], b_imag[:, :, :pairs], b_real[:, :, pairs:], b_imag[:, :, pairs:]
    )
    prod1_r = sig1_r * filt1_r - sig1_i * filt1_i
    prod1_i = sig1_r * filt1_i + sig1_i * filt1_r
    prod2_r = sig2_r * filt2_r - sig2_i * filt2_i
    prod2_i = sig2_r * filt2_i + sig2_i * filt2_r
    prod_real = prod1_r - prod2_i
    prod_imag = prod1_i + prod2_r

    inv = minor(jnp.concatenate([prod_real, prod_imag], axis=-1), inv_block)
    inv_real, inv_imag = inv[..., :width], inv[..., width:]
    untwist_real = inv_real * cos_w - inv_imag * sin_w
    untwist_imag = inv_imag * cos_w + inv_real * sin_w
    untwist = jnp.stack([untwist_real, untwist_imag], axis=0)
    back = major(block_table(co_np, so_np, 1.0, False), untwist.reshape((2 * seqs,) + untwist.shape[2:]))
    back_real, back_imag = back[:seqs], back[seqs:]

    own_rows = slot_rows(seq_index, jnp.arange(2), seqs)
    cos_blk, sin_blk = turn_table(np.arange(rows), np.arange(seqs) * width, full)
    cos_off, sin_off = turn_table(np.arange(rows), np.arange(width), full)
    cos_blk, sin_blk = jnp.take(cos_blk, own_rows, axis=0).T, jnp.take(sin_blk, own_rows, axis=0).T
    cos_off, sin_off = jnp.take(cos_off, own_rows, axis=0), jnp.take(sin_off, own_rows, axis=0)
    cos_b = (cos_blk[:, :, None] * cos_off[None] - sin_blk[:, :, None] * sin_off[None])[:, :, None, :]
    sin_b = (sin_blk[:, :, None] * cos_off[None] + cos_blk[:, :, None] * sin_off[None])[:, :, None, :]
    reverted_real = back_real * cos_b - back_imag * sin_b
    reverted_imag = back_imag * cos_b + back_real * sin_b
    reverted = jnp.stack([reverted_real, reverted_imag], axis=2).astype(bf16)
    moved = lax.all_to_all(reverted, "seq", 0, 0, tiled=True).astype(f32)
    moved = moved.reshape(2 * rows, pairs, width)

    cl_np, sl_np = np_turns(np.arange(seqs), row_ids, rows)
    merged = major(block_table(cl_np, sl_np, 1.0, True, rows_reim_inner=True), moved)
    merged = merged.reshape(seqs, chans, width) * (1.0 / full)
    arrived = lax.all_to_all(merged.astype(bf16), "seq", 0, 0, tiled=True)
    conv = arrived.astype(f32).transpose(1, 0, 2).reshape(chans, length)
    gated_out = (query_gate.astype(f32) * conv).astype(bf16)

    tp_index = lax.axis_index("tp")
    tps = lax.axis_size("tp")
    other_chip = tp_index ^ 2
    other_core = tp_index ^ 1
    cross = [(i, i ^ 2) for i in range(tps)]
    gated_far = lax.ppermute(gated_out, "tp", cross)

    def weights(rows_of, cols_of):
        return lax.dynamic_slice(out_weight, (rows_of * chans, cols_of * chans), (chans, chans))

    def partial(rows_of):
        near = jnp.dot(weights(rows_of, tp_index), gated_out, preferred_element_type=f32)
        far = jnp.dot(weights(rows_of, other_chip), gated_far, preferred_element_type=f32)
        return near + far

    pair = [(i, i ^ 1) for i in range(tps)]
    send_part = partial(other_core)
    keep_part = partial(tp_index)
    total = keep_part + lax.ppermute(send_part.astype(bf16), "tp", pair).astype(f32)
    return total.astype(bf16)


def solution(mesh):
    return jax.shard_map(
        body,
        mesh=mesh,
        in_specs=(P("tp", "seq"), P("tp", "seq"), P("tp", "seq"), P("tp", "seq"), P()),
        out_specs=P("tp", "seq"),
        check_vma=False,
    )
```

```python
import math

import jax
import numpy as np
import jax.numpy as jnp
from jax import lax
from jax.experimental import pallas as pl
from jax.sharding import PartitionSpec as P

HIGH = lax.Precision.HIGH


def turn_table(row_ids, col_ids, modulus):
    turns = (np.asarray(row_ids, np.int64)[:, None] * np.asarray(col_ids, np.int64)[None, :]) % modulus
    angles = turns.astype(np.float64) * (2.0 * math.pi / modulus)
    return (jnp.asarray(np.cos(angles), jnp.float32), jnp.asarray(np.sin(angles), jnp.float32))


def block_table(cos, sin, sign, cols_reim_inner, rows_reim_inner=False):
    n_out, n_in = cos.shape
    tab = np.zeros((2, n_out, 2, n_in))
    tab[0, :, 0], tab[0, :, 1] = cos, -sign * sin
    tab[1, :, 0], tab[1, :, 1] = sign * sin, cos
    if cols_reim_inner:
        tab = tab.transpose(0, 1, 3, 2)
    if rows_reim_inner:
        tab = tab.transpose(1, 0, 2, 3)
    return jnp.asarray(tab.reshape(2 * n_out, 2 * n_in), jnp.float32)


def np_turns(row_ids, col_ids, modulus):
    turns = (np.asarray(row_ids, np.int64)[:, None] * np.asarray(col_ids, np.int64)[None, :]) % modulus
    angles = turns.astype(np.float64) * (2.0 * math.pi / modulus)
    return np.cos(angles), np.sin(angles)


def row_list(seqs):
    return np.array([d if s == 0 else (seqs if d == 0 else 2 * seqs - d) for d in range(seqs) for s in range(2)])


def slot_rows(device, slot, seqs):
    return jnp.where(slot == 0, device, jnp.where(device == 0, seqs, 2 * seqs - device))


def major(table, data):
    return jnp.einsum("qk,k...->q...", table, data, precision=HIGH)


def minor(data, table):
    return jnp.einsum("...b,bm->...m", data, table, precision=HIGH)


def send_blocks(key_gate, value_input, long_filter, seqs, interpret=False):
    chans, length = key_gate.shape
    width = length // seqs
    pairs = chans // 2

    def kernel(key_ref, value_ref, taps_ref, out_ref):
        for d in range(seqs):
            cols = slice(d * width, (d + 1) * width)
            gated = key_ref[:, cols].astype(jnp.float32) * value_ref[:, cols].astype(jnp.float32)
            gated = gated.astype(jnp.bfloat16)
            taps = taps_ref[:, cols].astype(jnp.bfloat16)
            out_ref[d, 0:pairs] = gated[:pairs]
            out_ref[d, pairs:chans] = taps[:pairs]
            out_ref[d, chans:chans + pairs] = gated[pairs:]
            out_ref[d, chans + pairs:2 * chans] = taps[pairs:]

    return pl.pallas_call(
        kernel,
        out_shape=jax.ShapeDtypeStruct((seqs, 2 * chans, width), jnp.bfloat16),
        interpret=interpret,
    )(key_gate, value_input, long_filter)


def body(query_gate, key_gate, value_input, long_filter, out_weight):
    chans, length = key_gate.shape
    seqs = lax.axis_size("seq")
    seq_index = lax.axis_index("seq")
    width = length // seqs
    rows = 2 * seqs
    full = rows * length
    pairs = chans // 2
    f32, bf16 = jnp.float32, jnp.bfloat16

    send = send_blocks(key_gate, value_input, long_filter, seqs)
    got = lax.all_to_all(send, "seq", 0, 0, tiled=True).astype(f32)
    packed_real, packed_imag = got[:, :chans], got[:, chans:]

    row_ids = row_list(seqs)
    cos_a, sin_a = turn_table(row_ids, np.arange(seqs), rows)
    freq_real = major(cos_a, packed_real) + major(sin_a, packed_imag)
    freq_imag = major(cos_a, packed_imag) - major(sin_a, packed_real)
    cos_dev, sin_dev = turn_table(np.arange(seqs) * width, row_ids, full)
    cos_dev = lax.dynamic_index_in_dim(cos_dev, seq_index, 0, keepdims=False)[:, None, None]
    sin_dev = lax.dynamic_index_in_dim(sin_dev, seq_index, 0, keepdims=False)[:, None, None]
    cos_col, sin_col = turn_table(row_ids, np.arange(width), full)
    cos_col, sin_col = cos_col[:, None, :], sin_col[:, None, :]
    cos_t = cos_dev * cos_col - sin_dev * sin_col
    sin_t = sin_dev * cos_col + cos_dev * sin_col
    spread_real = freq_real * cos_t + freq_imag * sin_t
    spread_imag = freq_imag * cos_t - freq_real * sin_t
    spread = jnp.stack([spread_real, spread_imag], axis=1).astype(bf16)
    spread = spread.reshape(seqs, 2, 2, chans, width).transpose(0, 2, 1, 3, 4)
    recv = lax.all_to_all(spread, "seq", 0, 0, tiled=True).astype(f32)

    cos_o, sin_o = turn_table(np.arange(seqs), np.arange(seqs), seqs)
    cos_w, sin_w = turn_table(np.arange(seqs), np.arange(width), length)
    cos_w, sin_w = cos_w[:, None, None, :], sin_w[:, None, None, :]
    cos_i, sin_i = turn_table(np.arange(width), np.arange(width), width)
    co_np, so_np = np_turns(np.arange(seqs), np.arange(seqs), seqs)
    first = major(block_table(co_np, so_np, -1.0, True), recv.reshape((2 * seqs,) + recv.shape[2:]))
    first_real, first_imag = first[:seqs], first[seqs:]
    twist_real = first_real * cos_w + first_imag * sin_w
    twist_imag = first_imag * cos_w - first_real * sin_w
    fwd_block = jnp.concatenate(
        [jnp.concatenate([cos_i, -sin_i], axis=1), jnp.concatenate([sin_i, cos_i], axis=1)], axis=0
    )
    inv_block = jnp.concatenate(
        [jnp.concatenate([cos_i, sin_i], axis=1), jnp.concatenate([-sin_i, cos_i], axis=1)], axis=0
    )
    spec = minor(jnp.concatenate([twist_real, twist_imag], axis=-1), fwd_block)
    spec_real, spec_imag = spec[..., :width], spec[..., width:]

    lane_in = lax.broadcasted_iota(jnp.int32, (width, width), 0)
    lane_out = lax.broadcasted_iota(jnp.int32, (width, width), 1)
    lane_flip = (lane_in == width - 1 - lane_out).astype(f32)
    lane_neg = (lane_in == (width - lane_out) % width).astype(f32)
    place = lax.broadcasted_iota(jnp.int32, (rows, rows), 0)
    source = lax.broadcasted_iota(jnp.int32, (rows, rows), 1)
    place_q, place_s = place // 2, place % 2
    cross_src = 2 * (seqs - 1 - place_q) + 1 - place_s
    self_src = jnp.where(place_s == 1, 2 * (seqs - 1 - place_q) + 1, 2 * ((seqs - place_q) % seqs))
    first_dev = seq_index == 0
    regroup = (source == jnp.where(first_dev, self_src, cross_src)).astype(f32)

    def negated(spec):
        regrouped = jnp.einsum(
            "uv,vcb->ucb", regroup, spec.reshape(rows, chans, 2 * width), precision=HIGH
        ).reshape(spec.shape)
        moved = jnp.einsum("...b,bm->...m", regrouped, lane_flip, precision=HIGH)
        corner = jnp.einsum("cb,bm->cm", spec[0, 0], lane_neg, precision=HIGH)
        return moved.at[0, 0].set(jnp.where(first_dev, corner, moved[0, 0]))

    zeros = jnp.zeros_like(lane_flip)
    lane_flip = jnp.concatenate(
        [jnp.concatenate([lane_flip, zeros], axis=1), jnp.concatenate([zeros, lane_flip], axis=1)], axis=0
    )
    lane_neg = jnp.concatenate(
        [jnp.concatenate([lane_neg, zeros], axis=1), jnp.concatenate([zeros, lane_neg], axis=1)], axis=0
    )
    neg = negated(spec)
    neg_real, neg_imag = neg[..., :width], neg[..., width:]

    a_real = 0.5 * (spec_real + neg_real)
    a_imag = 0.5 * (spec_imag - neg_imag)
    b_real = 0.5 * (spec_imag + neg_imag)
    b_imag = 0.5 * (neg_real - spec_real)
    sig1_r, sig1_i, filt1_r, filt1_i = (
        a_real[:, :, :pairs], a_imag[:, :, :pairs], a_real[:, :, pairs:], a_imag[:, :, pairs:]
    )
    sig2_r, sig2_i, filt2_r, filt2_i = (
        b_real[:, :, :pairs], b_imag[:, :, :pairs], b_real[:, :, pairs:], b_imag[:, :, pairs:]
    )
    prod1_r = sig1_r * filt1_r - sig1_i * filt1_i
    prod1_i = sig1_r * filt1_i + sig1_i * filt1_r
    prod2_r = sig2_r * filt2_r - sig2_i * filt2_i
    prod2_i = sig2_r * filt2_i + sig2_i * filt2_r
    prod_real = prod1_r - prod2_i
    prod_imag = prod1_i + prod2_r

    inv = minor(jnp.concatenate([prod_real, prod_imag], axis=-1), inv_block)
    inv_real, inv_imag = inv[..., :width], inv[..., width:]
    untwist_real = inv_real * cos_w - inv_imag * sin_w
    untwist_imag = inv_imag * cos_w + inv_real * sin_w
    untwist = jnp.stack([untwist_real, untwist_imag], axis=0)
    back = major(block_table(co_np, so_np, 1.0, False), untwist.reshape((2 * seqs,) + untwist.shape[2:]))
    back_real, back_imag = back[:seqs], back[seqs:]

    own_rows = slot_rows(seq_index, jnp.arange(2), seqs)
    cos_blk, sin_blk = turn_table(np.arange(rows), np.arange(seqs) * width, full)
    cos_off, sin_off = turn_table(np.arange(rows), np.arange(width), full)
    cos_blk, sin_blk = jnp.take(cos_blk, own_rows, axis=0).T, jnp.take(sin_blk, own_rows, axis=0).T
    cos_off, sin_off = jnp.take(cos_off, own_rows, axis=0), jnp.take(sin_off, own_rows, axis=0)
    cos_b = (cos_blk[:, :, None] * cos_off[None] - sin_blk[:, :, None] * sin_off[None])[:, :, None, :]
    sin_b = (sin_blk[:, :, None] * cos_off[None] + cos_blk[:, :, None] * sin_off[None])[:, :, None, :]
    reverted_real = back_real * cos_b - back_imag * sin_b
    reverted_imag = back_imag * cos_b + back_real * sin_b
    reverted = jnp.stack([reverted_real, reverted_imag], axis=1).astype(bf16)
    moved = lax.all_to_all(reverted, "seq", 0, 0, tiled=True).astype(f32)
    moved = moved.reshape(2 * rows, pairs, width)

    cl_np, sl_np = np_turns(np.arange(seqs), row_ids, rows)
    last_tab = block_table(cl_np, sl_np, 1.0, True, rows_reim_inner=True).reshape(2 * seqs, seqs, 2, 2)
    last_tab = last_tab.transpose(0, 1, 3, 2).reshape(2 * seqs, 2 * rows)
    merged = major(last_tab, moved)
    merged = merged.reshape(seqs, chans, width) * (1.0 / full)
    arrived = lax.all_to_all(merged.astype(bf16), "seq", 0, 0, tiled=True)
    conv = arrived.astype(f32).transpose(1, 0, 2).reshape(chans, length)
    gated_out = (query_gate.astype(f32) * conv).astype(bf16)

    tp_index = lax.axis_index("tp")
    tps = lax.axis_size("tp")
    other_chip = tp_index ^ 2
    other_core = tp_index ^ 1
    cross = [(i, i ^ 2) for i in range(tps)]
    gated_far = lax.ppermute(gated_out, "tp", cross)

    def weights(rows_of, cols_of):
        return lax.dynamic_slice(out_weight, (rows_of * chans, cols_of * chans), (chans, chans))

    def partial(rows_of):
        near = jnp.dot(weights(rows_of, tp_index), gated_out, preferred_element_type=f32)
        far = jnp.dot(weights(rows_of, other_chip), gated_far, preferred_element_type=f32)
        return near + far

    pair = [(i, i ^ 1) for i in range(tps)]
    send_part = partial(other_core)
    keep_part = partial(tp_index)
    total = keep_part + lax.ppermute(send_part.astype(bf16), "tp", pair).astype(f32)
    return total.astype(bf16)


def solution(mesh):
    return jax.shard_map(
        body,
        mesh=mesh,
        in_specs=(P("tp", "seq"), P("tp", "seq"), P("tp", "seq"), P("tp", "seq"), P()),
        out_specs=P("tp", "seq"),
        check_vma=False,
    )
```
